32 devices in a mesh: groups: 2 (over y), tm: 4 (over z), height: 2 (over x), chan: 2 (over core).
Axes of the slice: x: 2, y: 2, z: 4, core: 2. Of those that a mesh axis runs over, the one named last changes fastest.
Arguments:
- video: bfloat16 [16, 72, 320, 128], P(('groups', 'tm'), 'height', 'chan'), parts along dimension 0, may hold values from -52 to 52
- norm1_gain: float32 [320], P('chan'), may hold values from 0.25 to 1.75
- norm1_bias: float32 [320], P('chan'), may hold values from -3 to 3
- spatial_weight: bfloat16 [3, 3, 320, 320], P(None, None, 'tm', 'chan'), may hold values from -0.3125 to 0.3125
- spatial_bias: float32 [320], P('chan'), may hold values from -3 to 3
- norm2_gain: float32 [320], P('chan'), may hold values from 0.25 to 1.75
- norm2_bias: float32 [320], P('chan'), may hold values from -3 to 3
- temporal_weight: bfloat16 [3, 320, 320], P(None, 'tm', 'chan'), may hold values from -0.3125 to 0.3125
- temporal_bias: float32 [320], P('chan'), may hold values from -3 to 3
Outputs:
- clip_out: bfloat16 [16, 72, 320, 128], P(('groups', 'tm'), 'height', 'chan'), parts along dimension 0
The draws below stay inside these ranges and needn't reach their ends.
There are 2 independent parts, one for each index of `groups`. The reference program is written for one: setup_inputs(seed, part) draws one part's arguments, and reference() takes and returns one part's arrays. A program takes and returns all parts, laid end to end along the dimension named above; an argument that names none is the same for every part. Nothing has to cross between parts.
All inputs are finite; a program needn't handle non-finite values.
Results may differ from the reference program's by a relative error of at most 0.0052.
Values may be sent and summed in bfloat16 or wider, within the bound.
No kernel may reach another device: no remote copies, remote signals or barrier semaphores. Data moves between devices by JAX's collectives and lax.ppermute only.
A program may use at most 128 MiB of HBM per device.

```python
import jax
import jax.numpy as jnp
from jax import lax

C = 320
GROUPS = 32
WID = 128
FRAMES = 8
H = 72


def draw_video(key, part):
    subkeys = jax.random.split(key, 11)
    full_shape = (FRAMES, H, C, WID)
    noise_base = jnp.clip(jax.random.normal(subkeys[0], full_shape, jnp.float32), -3.0, 3.0)
    frame_index = jnp.arange(FRAMES, dtype=jnp.int32)
    row_index = jnp.arange(H, dtype=jnp.int32)
    frame_pos = jnp.arange(FRAMES, dtype=jnp.float32) / max(FRAMES - 1, 1)
    row_pos = jnp.arange(H, dtype=jnp.float32) / max(H - 1, 1)
    frame_scale = jnp.exp(jnp.log(3.0) * frame_pos) * jnp.exp(jax.random.uniform(subkeys[1], (FRAMES,), jnp.float32, -0.3, 0.3))
    row_scale = jnp.exp(jnp.log(1.5) * row_pos)
    cut_low = max(FRAMES // 4, 1)
    cut_high = max(FRAMES - FRAMES // 4, cut_low + 1)
    cut_frame = jax.random.randint(subkeys[2], (), cut_low, cut_high)
    later = (frame_index >= cut_frame)[:, None]
    scale_first = jnp.exp(jax.random.uniform(subkeys[3], (C,), jnp.float32, -0.6, 0.6))
    scale_second = jnp.exp(jax.random.uniform(subkeys[4], (C,), jnp.float32, -0.6, 0.6))
    chan_scale = jnp.where(later, scale_second[None, :], scale_first[None, :])
    offset_first = 2.0 * jnp.clip(jax.random.normal(subkeys[5], (C,), jnp.float32), -3.0, 3.0)
    offset_second = 2.0 * jnp.clip(jax.random.normal(subkeys[6], (C,), jnp.float32), -3.0, 3.0)
    drift_pattern = jnp.clip(jax.random.normal(subkeys[7], (C,), jnp.float32), -2.0, 2.0)
    offset = jnp.where(later, offset_second[None, :], offset_first[None, :]) + (frame_pos - 0.5)[:, None] * drift_pattern[None, :]
    amplitude = jax.random.uniform(subkeys[8], (FRAMES,), jnp.float32, -6.0, 6.0)
    quarter = max(H // 4, 1)
    band_start = jax.random.randint(subkeys[9], (), 0, H - quarter + 1)
    in_band = ((row_index >= band_start) & (row_index < band_start + quarter)).astype(jnp.float32)
    band_level = jax.random.uniform(subkeys[10], (FRAMES,), jnp.float32, -3.0, 3.0)
    row_shift = amplitude[:, None] * (row_pos - 0.5)[None, :] + band_level[:, None] * in_band[None, :]
    scales = frame_scale[:, None, None, None] * row_scale[None, :, None, None] * chan_scale[:, None, :, None]
    frame_shift = 1.5 * (frame_pos - 0.5)
    drawn = noise_base * scales + offset[:, None, :, None] + row_shift[:, :, None, None] + frame_shift[:, None, None, None]
    return drawn.astype(jnp.bfloat16)


def level_of(stream_key, extent, shards, least, largest):
    gain, own = 1.0, jax.random.fold_in(stream_key, 6)
    for axis_at, blocks in shards:
        heights = jnp.exp(jax.random.uniform(jax.random.fold_in(own, axis_at), (blocks,), jnp.float32, least / len(shards), largest / len(shards)))
        gain = gain * jnp.repeat(heights, extent[axis_at] // blocks).reshape([-1 if axis == axis_at else 1 for axis in range(len(extent))])
    return gain


def gaussian(rng, shape, scale, bound, pieces=(), kind=jnp.bfloat16):
    values = scale * jax.random.normal(rng, shape, jnp.float32)
    if pieces:
        values = values * level_of(rng, shape, pieces, -0.22, 0.18)
    return jnp.clip(values, -bound, bound).astype(kind)


def setup_inputs(seed: int = 0, part: int = 0) -> dict:
    streams_of = jax.random.split(jax.random.key(seed), 10)
    own_keys = jax.random.split(jax.random.fold_in(streams_of[9], part), 10)
    return {
        "video": draw_video(jax.random.fold_in(jax.random.fold_in(streams_of[9], part), 71), part),
        "norm1_gain": jnp.clip(1.0 + 0.15 * jax.random.normal(streams_of[1], (C,), jnp.float32), 0.25, 1.75),
        "norm1_bias": gaussian(streams_of[2], (C,), 0.5, 3.0, ((0, 2),), jnp.float32),
        "spatial_weight": gaussian(streams_of[3], (3, 3, C, C), C ** -0.5, 0.3125, ((2, 4), (3, 2))),
        "spatial_bias": gaussian(streams_of[4], (C,), 0.5, 3.0, ((0, 2),), jnp.float32),
        "norm2_gain": jnp.clip(1.0 + 0.15 * jax.random.normal(streams_of[5], (C,), jnp.float32), 0.25, 1.75),
        "norm2_bias": gaussian(streams_of[6], (C,), 0.5, 3.0, ((0, 2),), jnp.float32),
        "temporal_weight": gaussian(streams_of[7], (3, C, C), C ** -0.5, 0.3125, ((1, 4), (2, 2))),
        "temporal_bias": gaussian(streams_of[8], (C,), 0.5, 3.0, ((0, 2),), jnp.float32),
    }


EPSILON = 1e-06

def reference(video, norm1_gain, norm1_bias, spatial_weight, spatial_bias, norm2_gain, norm2_bias, temporal_weight, temporal_bias):
    group_size = C // GROUPS
    gain_one = norm1_gain[:, None]
    shift_one = norm1_bias[:, None]
    gain_two = norm2_gain[:, None]
    shift_two = norm2_bias[:, None]

    def spatial_frame(one_frame):
        values = one_frame.astype(jnp.float32)
        grouped = values.reshape(H, GROUPS, group_size, WID)
        average = lax.optimization_barrier(jnp.mean(grouped, axis=(0, 2, 3), keepdims=True))
        centred = grouped - average
        variance = lax.optimization_barrier(jnp.mean(centred * centred, axis=(0, 2, 3), keepdims=True))
        scaled = (centred * lax.rsqrt(variance + EPSILON)).reshape(H, C, WID)
        act_one = jax.nn.silu(scaled * gain_one + shift_one).astype(jnp.bfloat16)
        padded = jnp.pad(act_one, ((1, 1), (0, 0), (1, 1)))
        summed = jnp.zeros((H, C, WID), jnp.float32)
        for row_tap in range(3):
            for col_tap in range(3):
                window = padded[row_tap:row_tap + H, :, col_tap:col_tap + WID].astype(jnp.float32)
                summed = summed + jnp.einsum('hcw,co->how', window, spatial_weight[row_tap, col_tap].astype(jnp.float32))
        return (values + summed + spatial_bias[:, None]).astype(jnp.bfloat16)
    hidden = lax.map(spatial_frame, video)
    entries = FRAMES * H * WID * group_size

    def frame_sums(one_frame):
        return lax.optimization_barrier(jnp.sum(one_frame.astype(jnp.float32).reshape(H, GROUPS, group_size, WID), axis=(0, 2, 3)))
    average_two = lax.optimization_barrier(jnp.sum(lax.map(frame_sums, hidden), axis=0)) / entries

    def frame_squares(one_frame):
        centred = one_frame.astype(jnp.float32).reshape(H, GROUPS, group_size, WID) - average_two[:, None, None]
        return lax.optimization_barrier(jnp.sum(centred * centred, axis=(0, 2, 3)))
    variance_two = lax.optimization_barrier(jnp.sum(lax.map(frame_squares, hidden), axis=0)) / entries

    def frame_act(one_frame):
        centred = one_frame.astype(jnp.float32).reshape(H, GROUPS, group_size, WID) - average_two[:, None, None]
        scaled = (centred * lax.rsqrt(variance_two[:, None, None] + EPSILON)).reshape(H, C, WID)
        return jax.nn.silu(scaled * gain_two + shift_two).astype(jnp.bfloat16)
    act_two = lax.map(frame_act, hidden)
    padded_two = jnp.pad(act_two, ((1, 1), (0, 0), (0, 0), (0, 0)))

    def temporal_frame(index):
        summed = jnp.zeros((H, C, WID), jnp.float32)
        for frame_tap in range(3):
            window = lax.dynamic_index_in_dim(padded_two, index + frame_tap, 0, keepdims=False).astype(jnp.float32)
            summed = summed + jnp.einsum('hcw,co->how', window, temporal_weight[frame_tap].astype(jnp.float32))
        residual = lax.dynamic_index_in_dim(hidden, index, 0, keepdims=False).astype(jnp.float32)
        return (residual + summed + temporal_bias[:, None]).astype(jnp.bfloat16)
    return lax.map(temporal_frame, jnp.arange(FRAMES, dtype=jnp.int32))
```

```python
import jax
import jax.numpy as jnp
from jax import lax
from jax.sharding import PartitionSpec as P

C = 320
GROUPS = 32


EPSILON = 1e-06


def swap_chan(block):
    return lax.ppermute(block, "chan", [(0, 1), (1, 0)])


def row_halo(block):
    count = lax.axis_size("height")
    forward = [(i, i + 1) for i in range(count - 1)]
    backward = [(target, source) for source, target in forward]
    low = lax.ppermute(block[:, -1:], "height", forward)
    high = lax.ppermute(block[:, :1], "height", backward)
    return jnp.concatenate([low, block, high], axis=1)


def spatial_conv(inputs, weight):
    return lax.conv_general_dilated(
        inputs,
        weight,
        window_strides=(1, 1),
        padding=((0, 0), (1, 1)),
        dimension_numbers=("NHCW", "HWIO", "NHCW"),
        preferred_element_type=jnp.float32,
    )


def temporal_conv(inputs, weight):
    return lax.conv_general_dilated(
        inputs,
        weight[:, None],
        window_strides=(1, 1),
        padding=((0, 0), (0, 0)),
        dimension_numbers=("HNCW", "HWIO", "HNCW"),
        preferred_element_type=jnp.float32,
    )


def group_act(values, average, variance, gain, bias):
    frames, rows, local_chan, width = values.shape
    local_groups = average.shape[-1]
    grouped = values.reshape(frames, rows, local_groups, local_chan // local_groups, width)
    centred = grouped - average.reshape(-1, 1, local_groups, 1, 1)
    scaled = (centred * lax.rsqrt(variance.reshape(-1, 1, local_groups, 1, 1) + EPSILON)).reshape(
        frames, rows, local_chan, width
    )
    return jax.nn.silu(scaled * gain[:, None] + bias[:, None]).astype(jnp.bfloat16)


def body(
    video,
    norm1_gain,
    norm1_bias,
    spatial_weight,
    spatial_bias,
    norm2_gain,
    norm2_bias,
    temporal_weight,
    temporal_bias,
):
    frames, rows, local_chan, width = video.shape
    group_size = C // GROUPS
    local_groups = local_chan // group_size
    chan_index = lax.axis_index("chan")
    tm_index = lax.axis_index("tm")
    tm_count = lax.axis_size("tm")

    piece = spatial_weight.shape[2]
    merged = jnp.concatenate(
        [spatial_weight.reshape(9, piece, local_chan), temporal_weight], axis=0
    )
    full_weight = lax.all_gather(merged, "tm", axis=1, tiled=True)
    own_start = chan_index * local_chan
    other_start = (1 - chan_index) * local_chan
    own_weight = lax.dynamic_slice_in_dim(full_weight, own_start, local_chan, axis=1)
    other_weight = lax.dynamic_slice_in_dim(full_weight, other_start, local_chan, axis=1)
    spatial_own = own_weight[:9].reshape(3, 3, local_chan, local_chan)
    spatial_other = other_weight[:9].reshape(3, 3, local_chan, local_chan)
    temporal_own = own_weight[9:]
    temporal_other = other_weight[9:]

    values = video.astype(jnp.float32)
    grouped = values.reshape(frames, rows, local_groups, group_size, width)
    entries = rows * lax.axis_size("height") * width * group_size
    totals = lax.psum(jnp.sum(grouped, axis=(1, 3, 4)), "height")
    average = totals / entries
    centred = grouped - average.reshape(frames, 1, local_groups, 1, 1)
    squares = lax.psum(jnp.sum(centred * centred, axis=(1, 3, 4)), "height")
    variance = squares / entries
    act_one = group_act(values, average, variance, norm1_gain, norm1_bias)

    with_rows = row_halo(act_one)
    other_rows = swap_chan(with_rows)
    spatial_sum = spatial_conv(with_rows, spatial_own) + spatial_conv(other_rows, spatial_other)
    hidden = (values + spatial_sum + spatial_bias[:, None]).astype(jnp.bfloat16)

    forward = [(i, i + 1) for i in range(tm_count - 1)]
    backward = [(target, source) for source, target in forward]
    before = lax.ppermute(hidden[-1:], "tm", forward)
    after = lax.ppermute(hidden[:1], "tm", backward)

    hidden_values = hidden.astype(jnp.float32)
    grouped_two = hidden_values.reshape(frames, rows, local_groups, group_size, width)
    entries_two = frames * tm_count * entries
    totals_two = lax.psum(lax.psum(jnp.sum(grouped_two, axis=(0, 1, 3, 4)), "height"), "tm")
    average_two = totals_two / entries_two
    centred_two = grouped_two - average_two.reshape(1, 1, local_groups, 1, 1)
    squares_two = lax.psum(
        lax.psum(jnp.sum(centred_two * centred_two, axis=(0, 1, 3, 4)), "height"), "tm"
    )
    variance_two = squares_two / entries_two

    extended = jnp.concatenate([before, hidden, after], axis=0).astype(jnp.float32)
    act_two = group_act(extended, average_two, variance_two, norm2_gain, norm2_bias)
    frame_ids = jnp.arange(frames + 2)
    inside = (frame_ids > 0) | (tm_index > 0)
    inside = inside & ((frame_ids < frames + 1) | (tm_index < tm_count - 1))
    act_two = jnp.where(inside[:, None, None, None], act_two, jnp.zeros_like(act_two))

    other_two = swap_chan(act_two)
    temporal_sum = temporal_conv(act_two, temporal_own) + temporal_conv(other_two, temporal_other)
    return (hidden_values + temporal_sum + temporal_bias[:, None]).astype(jnp.bfloat16)


def solution(mesh):
    return jax.shard_map(
        body,
        mesh=mesh,
        in_specs=(
            P(("groups", "tm"), "height", "chan", None),
            P("chan"),
            P("chan"),
            P(None, None, "tm", "chan"),
            P("chan"),
            P("chan"),
            P("chan"),
            P(None, "tm", "chan"),
            P("chan"),
        ),
        out_specs=P(("groups", "tm"), "height", "chan", None),
        check_vma=False,
    )
```

```python
import jax
import jax.numpy as jnp
from jax import lax
from jax.sharding import PartitionSpec as P

C = 320
GROUPS = 32


EPSILON = 1e-06


def swap_chan(block):
    return lax.ppermute(block, "chan", [(0, 1), (1, 0)])


def row_halo(block):
    count = lax.axis_size("height")
    forward = [(i, i + 1) for i in range(count - 1)]
    backward = [(target, source) for source, target in forward]
    low = lax.ppermute(block[:, -1:], "height", forward)
    high = lax.ppermute(block[:, :1], "height", backward)
    return jnp.concatenate([low, block, high], axis=1)


def gather_tm(piece):
    count = lax.axis_size("tm")
    index = lax.axis_index("tm")
    pieces = [piece]
    for shift in range(1, count):
        pairs = [(i, (i - shift) % count) for i in range(count)]
        pieces.append(lax.ppermute(piece, "tm", pairs))
    stacked = jnp.roll(jnp.stack(pieces), index, axis=0)
    return stacked


def group_stats(grouped, axes, slot_axes):
    count = 1
    for axis in axes:
        count *= grouped.shape[axis]
    local_mean = jnp.sum(grouped, axis=axes) / count
    centred = grouped - jnp.expand_dims(local_mean, axes)
    local_m2 = jnp.sum(centred * centred, axis=axes)
    slots = 1
    for name in slot_axes:
        slots *= lax.axis_size(name)
    slot = 0
    for name in slot_axes:
        slot = slot * lax.axis_size(name) + lax.axis_index(name)
    mine = jnp.stack([local_mean, local_m2])
    table = jnp.zeros((slots,) + mine.shape, jnp.float32)
    table = lax.dynamic_update_index_in_dim(table, mine, slot, 0)
    for name in reversed(slot_axes):
        table = lax.psum(table, name)
    means = table[:, 0]
    average = jnp.sum(means, axis=0) / slots
    spread = means - average
    m2 = jnp.sum(table[:, 1], axis=0) + count * jnp.sum(spread * spread, axis=0)
    variance = m2 / (count * slots)
    return average, variance


def group_act(values, average, variance, gain, bias):
    frames, rows, local_chan, width = values.shape
    local_groups = average.shape[-1]
    grouped = values.reshape(frames, rows, local_groups, local_chan // local_groups, width)
    centred = grouped - average.reshape(-1, 1, local_groups, 1, 1)
    scaled = (centred * lax.rsqrt(variance.reshape(-1, 1, local_groups, 1, 1) + EPSILON)).reshape(
        frames, rows, local_chan, width
    )
    return jax.nn.silu(scaled * gain[:, None] + bias[:, None]).astype(jnp.bfloat16)


def both_halves(own, other, chan_index):
    first = jnp.where(chan_index == 0, own, other)
    second = jnp.where(chan_index == 0, other, own)
    return jnp.concatenate([first, second], axis=2)


def spatial_taps(running, channel_slab, weight, rows, width):
    for row_tap in range(3):
        for col_tap in range(3):
            window = channel_slab[:, row_tap : row_tap + rows, :, col_tap : col_tap + width]
            running = running + jnp.einsum(
                "frcw,co->frow", window, weight[row_tap, col_tap], preferred_element_type=jnp.float32
            )
    return running


def temporal_taps(running, channel_slab, weight, frames):
    for frame_tap in range(3):
        window = channel_slab[frame_tap : frame_tap + frames]
        running = running + jnp.einsum(
            "frcw,co->frow", window, weight[frame_tap], preferred_element_type=jnp.float32
        )
    return running


def body(
    video,
    norm1_gain,
    norm1_bias,
    spatial_weight,
    spatial_bias,
    norm2_gain,
    norm2_bias,
    temporal_weight,
    temporal_bias,
):
    frames, rows, local_chan, width = video.shape
    group_size = C // GROUPS
    local_groups = local_chan // group_size
    chan_index = lax.axis_index("chan")
    tm_index = lax.axis_index("tm")
    tm_count = lax.axis_size("tm")

    piece = spatial_weight.shape[2]
    merged = jnp.concatenate([spatial_weight.reshape(9, piece, local_chan), temporal_weight], axis=0)
    gathered = gather_tm(merged)
    full_weight = jnp.moveaxis(gathered, 0, 1).reshape(12, tm_count * piece, local_chan)
    spatial_full = full_weight[:9].reshape(3, 3, C, local_chan)
    temporal_full = full_weight[9:]

    values = video.astype(jnp.float32)
    grouped = values.reshape(frames, rows, local_groups, group_size, width)
    average, variance = group_stats(grouped, (1, 3, 4), ("height",))
    act_one = group_act(values, average, variance, norm1_gain, norm1_bias)

    with_rows = row_halo(act_one)
    all_rows = both_halves(with_rows, swap_chan(with_rows), chan_index)
    padded = jnp.pad(all_rows, ((0, 0), (0, 0), (0, 0), (1, 1)))
    empty = jnp.zeros((frames, rows, local_chan, width), jnp.float32)
    spatial_sum = spatial_taps(empty, padded, spatial_full, rows, width)
    hidden = (values + spatial_sum + spatial_bias[:, None]).astype(jnp.bfloat16)

    forward = [(i, i + 1) for i in range(tm_count - 1)]
    backward = [(target, source) for source, target in forward]
    before = lax.ppermute(hidden[-1:], "tm", forward)
    after = lax.ppermute(hidden[:1], "tm", backward)

    hidden_values = hidden.astype(jnp.float32)
    grouped_two = hidden_values.reshape(frames, rows, local_groups, group_size, width)
    average_two, variance_two = group_stats(grouped_two, (0, 1, 3, 4), ("tm", "height"))

    extended = jnp.concatenate([before, hidden, after], axis=0).astype(jnp.float32)
    act_two = group_act(extended, average_two, variance_two, norm2_gain, norm2_bias)
    frame_ids = jnp.arange(frames + 2)
    inside = (frame_ids > 0) | (tm_index > 0)
    inside = inside & ((frame_ids < frames + 1) | (tm_index < tm_count - 1))
    act_two = jnp.where(inside[:, None, None, None], act_two, jnp.zeros_like(act_two))

    all_two = both_halves(act_two, swap_chan(act_two), chan_index)
    temporal_sum = temporal_taps(empty, all_two, temporal_full, frames)
    return (hidden_values + temporal_sum + temporal_bias[:, None]).astype(jnp.bfloat16)


def solution(mesh):
    return jax.shard_map(
        body,
        mesh=mesh,
        in_specs=(
            P(("groups", "tm"), "height", "chan", None),
            P("chan"),
            P("chan"),
            P(None, None, "tm", "chan"),
            P("chan"),
            P("chan"),
            P("chan"),
            P(None, "tm", "chan"),
            P("chan"),
        ),
        out_specs=P(("groups", "tm"), "height", "chan", None),
        check_vma=False,
    )
```

```python
import jax
import jax.numpy as jnp
from jax import lax
from jax.sharding import PartitionSpec as P

C = 320
GROUPS = 32


EPSILON = 1e-06


def swap_chan(block):
    return lax.ppermute(block, "chan", [(0, 1), (1, 0)])


def row_halo(block):
    count = lax.axis_size("height")
    forward = [(i, i + 1) for i in range(count - 1)]
    backward = [(target, source) for source, target in forward]
    low = lax.ppermute(block[:, -1:], "height", forward)
    high = lax.ppermute(block[:, :1], "height", backward)
    return jnp.concatenate([low, block, high], axis=1)


def gather_tm(piece):
    count = lax.axis_size("tm")
    index = lax.axis_index("tm")
    pieces = [piece]
    for shift in range(1, count):
        pairs = [(i, (i - shift) % count) for i in range(count)]
        pieces.append(lax.ppermute(piece, "tm", pairs))
    stacked = jnp.roll(jnp.stack(pieces), index, axis=0)
    return stacked


def group_stats(grouped, axes, slot_axes):
    count = 1
    for axis in axes:
        count *= grouped.shape[axis]
    local_mean = jnp.sum(grouped, axis=axes) / count
    centred = grouped - jnp.expand_dims(local_mean, axes)
    local_m2 = jnp.sum(centred * centred, axis=axes)
    slots = 1
    for name in slot_axes:
        slots *= lax.axis_size(name)
    slot = 0
    for name in slot_axes:
        slot = slot * lax.axis_size(name) + lax.axis_index(name)
    mine = jnp.stack([local_mean, local_m2])
    table = jnp.zeros((slots,) + mine.shape, jnp.float32)
    table = lax.dynamic_update_index_in_dim(table, mine, slot, 0)
    for name in reversed(slot_axes):
        table = lax.psum(table, name)
    means = table[:, 0]
    average = jnp.sum(means, axis=0) / slots
    spread = means - average
    m2 = jnp.sum(table[:, 1], axis=0) + count * jnp.sum(spread * spread, axis=0)
    variance = m2 / (count * slots)
    return average, variance


def group_act(values, average, variance, gain, bias):
    frames, rows, local_chan, width = values.shape
    local_groups = average.shape[-1]
    grouped = values.reshape(frames, rows, local_groups, local_chan // local_groups, width)
    centred = grouped - average.reshape(-1, 1, local_groups, 1, 1)
    scaled = (centred * lax.rsqrt(variance.reshape(-1, 1, local_groups, 1, 1) + EPSILON)).reshape(
        frames, rows, local_chan, width
    )
    return jax.nn.silu(scaled * gain[:, None] + bias[:, None]).astype(jnp.bfloat16)


def own_first(weight, own_start, other_start, size):
    own = lax.dynamic_slice_in_dim(weight, own_start, size, axis=1)
    other = lax.dynamic_slice_in_dim(weight, other_start, size, axis=1)
    return jnp.concatenate([own, other], axis=1)


def spatial_taps(running, channel_slab, weight, rows, width):
    for row_tap in range(3):
        for col_tap in range(3):
            window = channel_slab[:, row_tap : row_tap + rows, :, col_tap : col_tap + width]
            running = running + jnp.einsum(
                "frcw,co->frow", window, weight[row_tap, col_tap], preferred_element_type=jnp.float32
            )
    return running


def temporal_taps(running, channel_slab, weight, frames):
    for frame_tap in range(3):
        window = channel_slab[frame_tap : frame_tap + frames]
        running = running + jnp.einsum(
            "frcw,co->frow", window, weight[frame_tap], preferred_element_type=jnp.float32
        )
    return running


def body(
    video,
    norm1_gain,
    norm1_bias,
    spatial_weight,
    spatial_bias,
    norm2_gain,
    norm2_bias,
    temporal_weight,
    temporal_bias,
):
    frames, rows, local_chan, width = video.shape
    group_size = C // GROUPS
    local_groups = local_chan // group_size
    chan_index = lax.axis_index("chan")
    tm_index = lax.axis_index("tm")
    tm_count = lax.axis_size("tm")

    spatial_full = lax.all_gather(spatial_weight, "tm", axis=2, tiled=True).reshape(9, C, local_chan)
    temporal_pieces = gather_tm(temporal_weight)
    temporal_full = jnp.moveaxis(temporal_pieces, 0, 1).reshape(3, C, local_chan)
    own_start = chan_index * local_chan
    other_start = (1 - chan_index) * local_chan
    spatial_full = own_first(spatial_full, own_start, other_start, local_chan).reshape(
        3, 3, C, local_chan
    )
    temporal_full = own_first(temporal_full, own_start, other_start, local_chan)

    values = video.astype(jnp.float32)
    grouped = values.reshape(frames, rows, local_groups, group_size, width)
    average, variance = group_stats(grouped, (1, 3, 4), ("height",))
    act_one = group_act(values, average, variance, norm1_gain, norm1_bias)

    with_rows = row_halo(act_one)
    all_rows = jnp.concatenate([with_rows, swap_chan(with_rows)], axis=2)
    padded = jnp.pad(all_rows, ((0, 0), (0, 0), (0, 0), (1, 1)))
    empty = jnp.zeros((frames, rows, local_chan, width), jnp.float32)
    spatial_sum = spatial_taps(empty, padded, spatial_full, rows, width)
    hidden = (values + spatial_sum + spatial_bias[:, None]).astype(jnp.bfloat16)

    forward = [(i, i + 1) for i in range(tm_count - 1)]
    backward = [(target, source) for source, target in forward]
    before = lax.ppermute(hidden[-1:], "tm", forward)
    after = lax.ppermute(hidden[:1], "tm", backward)

    hidden_values = hidden.astype(jnp.float32)
    grouped_two = hidden_values.reshape(frames, rows, local_groups, group_size, width)
    average_two, variance_two = group_stats(grouped_two, (0, 1, 3, 4), ("tm", "height"))

    extended = jnp.concatenate([before, hidden, after], axis=0).astype(jnp.float32)
    act_two = group_act(extended, average_two, variance_two, norm2_gain, norm2_bias)
    frame_ids = jnp.arange(frames + 2)
    inside = (frame_ids > 0) | (tm_index > 0)
    inside = inside & ((frame_ids < frames + 1) | (tm_index < tm_count - 1))
    act_two = jnp.where(inside[:, None, None, None], act_two, jnp.zeros_like(act_two))

    all_two = jnp.concatenate([act_two, swap_chan(act_two)], axis=2)
    temporal_sum = temporal_taps(empty, all_two, temporal_full, frames)
    return (hidden_values + temporal_sum + temporal_bias[:, None]).astype(jnp.bfloat16)


def solution(mesh):
    return jax.shard_map(
        body,
        mesh=mesh,
        in_specs=(
            P(("groups", "tm"), "height", "chan", None),
            P("chan"),
            P("chan"),
            P(None, None, "tm", "chan"),
            P("chan"),
            P("chan"),
            P("chan"),
            P(None, "tm", "chan"),
            P("chan"),
        ),
        out_specs=P(("groups", "tm"), "height", "chan", None),
        check_vma=False,
    )
```

```python
import jax
import jax.numpy as jnp
from jax import lax
from jax.experimental import pallas as pl
from jax.experimental.pallas import tpu as pltpu
from jax.sharding import PartitionSpec as P

C = 320
GROUPS = 32


EPSILON = 1e-06


def swap_chan(block):
    return lax.ppermute(block, "chan", [(0, 1), (1, 0)])


def row_halo(block):
    count = lax.axis_size("height")
    forward = [(i, i + 1) for i in range(count - 1)]
    backward = [(target, source) for source, target in forward]
    low = lax.ppermute(block[:, -1:], "height", forward)
    high = lax.ppermute(block[:, :1], "height", backward)
    return jnp.concatenate([low, block, high], axis=1)


def gather_tm(piece):
    count = lax.axis_size("tm")
    index = lax.axis_index("tm")
    pieces = [piece]
    for shift in range(1, count):
        pairs = [(i, (i - shift) % count) for i in range(count)]
        pieces.append(lax.ppermute(piece, "tm", pairs))
    stacked = jnp.roll(jnp.stack(pieces), index, axis=0)
    return stacked


def group_stats(grouped, axes, slot_axes):
    count = 1
    for axis in axes:
        count *= grouped.shape[axis]
    local_mean = jnp.sum(grouped, axis=axes) / count
    centred = grouped - jnp.expand_dims(local_mean, axes)
    local_m2 = jnp.sum(centred * centred, axis=axes)
    slots = 1
    for name in slot_axes:
        slots *= lax.axis_size(name)
    slot = 0
    for name in slot_axes:
        slot = slot * lax.axis_size(name) + lax.axis_index(name)
    mine = jnp.stack([local_mean, local_m2])
    table = jnp.zeros((slots,) + mine.shape, jnp.float32)
    table = lax.dynamic_update_index_in_dim(table, mine, slot, 0)
    for name in reversed(slot_axes):
        table = lax.psum(table, name)
    means = table[:, 0]
    average = jnp.sum(means, axis=0) / slots
    spread = means - average
    m2 = jnp.sum(table[:, 1], axis=0) + count * jnp.sum(spread * spread, axis=0)
    variance = m2 / (count * slots)
    return average, variance


def group_act(values, average, variance, gain, bias):
    frames, rows, local_chan, width = values.shape
    local_groups = average.shape[-1]
    grouped = values.reshape(frames, rows, local_groups, local_chan // local_groups, width)
    centred = grouped - average.reshape(-1, 1, local_groups, 1, 1)
    scaled = (centred * lax.rsqrt(variance.reshape(-1, 1, local_groups, 1, 1) + EPSILON)).reshape(
        frames, rows, local_chan, width
    )
    return jax.nn.silu(scaled * gain[:, None] + bias[:, None]).astype(jnp.bfloat16)


def in_order(own, other, chan_index):
    size = own.shape[2]
    joined = jnp.zeros(own.shape[:2] + (2 * size,) + own.shape[3:], own.dtype)
    joined = lax.dynamic_update_slice_in_dim(joined, own, chan_index * size, axis=2)
    return lax.dynamic_update_slice_in_dim(joined, other, (1 - chan_index) * size, axis=2)


def spatial_kernel(x_ref, w_ref, res_ref, b_ref, o_ref):
    rows, local_chan, width = o_ref.shape[1], o_ref.shape[2], o_ref.shape[3]
    lane = lax.broadcasted_iota(jnp.int32, (local_chan, width), 1)
    bias = b_ref[...]

    def one_row(r, carry):
        y = jnp.dot(w_ref[0], x_ref[0, r], preferred_element_type=jnp.float32)
        y = y + jnp.dot(w_ref[1], x_ref[0, r + 1], preferred_element_type=jnp.float32)
        y = y + jnp.dot(w_ref[2], x_ref[0, r + 2], preferred_element_type=jnp.float32)
        left = pltpu.roll(y[:local_chan], 1, 1)
        left = jnp.where(lane == 0, 0.0, left)
        right = pltpu.roll(y[2 * local_chan :], width - 1, 1)
        right = jnp.where(lane == width - 1, 0.0, right)
        total = left + y[local_chan : 2 * local_chan] + right
        o_ref[0, r] = (res_ref[0, r].astype(jnp.float32) + total + bias).astype(o_ref.dtype)
        return carry

    lax.fori_loop(0, rows, one_row, 0)


def spatial_call(inputs, weight, residual, bias):
    frames, rows, local_chan, width = residual.shape
    chans = inputs.shape[2]
    return pl.pallas_call(
        spatial_kernel,
        out_shape=jax.ShapeDtypeStruct(residual.shape, jnp.bfloat16),
        grid=(frames,),
        in_specs=[
            pl.BlockSpec((1, rows + 2, chans, width), lambda f: (f, 0, 0, 0)),
            pl.BlockSpec((3, 3 * local_chan, chans), lambda f: (0, 0, 0)),
            pl.BlockSpec((1, rows, local_chan, width), lambda f: (f, 0, 0, 0)),
            pl.BlockSpec((local_chan, 1), lambda f: (0, 0)),
        ],
        out_specs=pl.BlockSpec((1, rows, local_chan, width), lambda f: (f, 0, 0, 0)),
        compiler_params=pltpu.CompilerParams(vmem_limit_bytes=48 * 1024 * 1024),
        cost_estimate=pl.CostEstimate(
            flops=2 * frames * rows * width * 9 * chans * local_chan,
            transcendentals=0,
            bytes_accessed=inputs.size * 2 + weight.size * 2 + 4 * residual.size,
        ),
    )(inputs, weight, residual, bias)


def temporal_kernel(a_ref, b_ref, c_ref, w_ref, res_ref, bias_ref, o_ref):
    rows = o_ref.shape[1]
    bias = bias_ref[...]

    def one_row(r, carry):
        y = jnp.dot(w_ref[0], a_ref[0, r], preferred_element_type=jnp.float32)
        y = y + jnp.dot(w_ref[1], b_ref[0, r], preferred_element_type=jnp.float32)
        y = y + jnp.dot(w_ref[2], c_ref[0, r], preferred_element_type=jnp.float32)
        o_ref[0, r] = (res_ref[0, r].astype(jnp.float32) + y + bias).astype(o_ref.dtype)
        return carry

    lax.fori_loop(0, rows, one_row, 0)


def frame_spec(tap, rows, chans, width):
    return pl.BlockSpec((1, rows, chans, width), lambda f: (f + tap, 0, 0, 0))


def temporal_call(inputs, weight, residual, bias):
    frames, rows, local_chan, width = residual.shape
    chans = inputs.shape[2]
    return pl.pallas_call(
        temporal_kernel,
        out_shape=jax.ShapeDtypeStruct(residual.shape, jnp.bfloat16),
        grid=(frames,),
        in_specs=[
            frame_spec(0, rows, chans, width),
            frame_spec(1, rows, chans, width),
            frame_spec(2, rows, chans, width),
            pl.BlockSpec((3, local_chan, chans), lambda f: (0, 0, 0)),
            pl.BlockSpec((1, rows, local_chan, width), lambda f: (f, 0, 0, 0)),
            pl.BlockSpec((local_chan, 1), lambda f: (0, 0)),
        ],
        out_specs=pl.BlockSpec((1, rows, local_chan, width), lambda f: (f, 0, 0, 0)),
        compiler_params=pltpu.CompilerParams(vmem_limit_bytes=48 * 1024 * 1024),
        cost_estimate=pl.CostEstimate(
            flops=2 * frames * rows * width * 3 * chans * local_chan,
            transcendentals=0,
            bytes_accessed=3 * residual.size * 4 + weight.size * 2 + 4 * residual.size,
        ),
    )(inputs, inputs, inputs, weight, residual, bias)


def spatial_taps(running, channel_slab, weight, rows, width):
    for row_tap in range(3):
        for col_tap in range(3):
            window = channel_slab[:, row_tap : row_tap + rows, :, col_tap : col_tap + width]
            running = running + jnp.einsum(
                "frcw,co->frow", window, weight[row_tap, col_tap], preferred_element_type=jnp.float32
            )
    return running


def temporal_taps(running, channel_slab, weight, frames):
    for frame_tap in range(3):
        window = channel_slab[frame_tap : frame_tap + frames]
        running = running + jnp.einsum(
            "frcw,co->frow", window, weight[frame_tap], preferred_element_type=jnp.float32
        )
    return running


def body(
    video,
    norm1_gain,
    norm1_bias,
    spatial_weight,
    spatial_bias,
    norm2_gain,
    norm2_bias,
    temporal_weight,
    temporal_bias,
):
    frames, rows, local_chan, width = video.shape
    group_size = C // GROUPS
    local_groups = local_chan // group_size
    chan_index = lax.axis_index("chan")
    tm_index = lax.axis_index("tm")
    tm_count = lax.axis_size("tm")

    spatial_full = lax.all_gather(spatial_weight, "tm", axis=2, tiled=True).reshape(9, C, local_chan)
    temporal_pieces = gather_tm(temporal_weight)
    temporal_full = jnp.moveaxis(temporal_pieces, 0, 1).reshape(3, C, local_chan)
    spatial_full = spatial_full.reshape(3, 3, C, local_chan)

    values = video.astype(jnp.float32)
    grouped = values.reshape(frames, rows, local_groups, group_size, width)
    average, variance = group_stats(grouped, (1, 3, 4), ("height",))
    act_one = group_act(values, average, variance, norm1_gain, norm1_bias)

    with_rows = row_halo(act_one)
    all_rows = in_order(with_rows, swap_chan(with_rows), chan_index)
    spatial_rows = jnp.transpose(spatial_full, (0, 1, 3, 2)).reshape(3, 3 * local_chan, C)
    hidden = spatial_call(all_rows, spatial_rows, video, spatial_bias[:, None])

    forward = [(i, i + 1) for i in range(tm_count - 1)]
    backward = [(target, source) for source, target in forward]
    before = lax.ppermute(hidden[-1:], "tm", forward)
    after = lax.ppermute(hidden[:1], "tm", backward)

    hidden_values = hidden.astype(jnp.float32)
    grouped_two = hidden_values.reshape(frames, rows, local_groups, group_size, width)
    average_two, variance_two = group_stats(grouped_two, (0, 1, 3, 4), ("tm", "height"))

    extended = jnp.concatenate([before, hidden, after], axis=0).astype(jnp.float32)
    act_two = group_act(extended, average_two, variance_two, norm2_gain, norm2_bias)
    frame_ids = jnp.arange(frames + 2)
    inside = (frame_ids > 0) | (tm_index > 0)
    inside = inside & ((frame_ids < frames + 1) | (tm_index < tm_count - 1))
    act_two = jnp.where(inside[:, None, None, None], act_two, jnp.zeros_like(act_two))

    all_two = in_order(act_two, swap_chan(act_two), chan_index)
    temporal_rows = jnp.transpose(temporal_full, (0, 2, 1))
    return temporal_call(all_two, temporal_rows, hidden, temporal_bias[:, None])


def solution(mesh):
    return jax.shard_map(
        body,
        mesh=mesh,
        in_specs=(
            P(("groups", "tm"), "height", "chan", None),
            P("chan"),
            P("chan"),
            P(None, None, "tm", "chan"),
            P("chan"),
            P("chan"),
            P("chan"),
            P(None, "tm", "chan"),
            P("chan"),
        ),
        out_specs=P(("groups", "tm"), "height", "chan", None),
        check_vma=False,
    )
```

```python
import jax
import jax.numpy as jnp
from jax import lax
from jax.experimental import pallas as pl
from jax.experimental.pallas import tpu as pltpu
from jax.sharding import PartitionSpec as P

C = 320
GROUPS = 32


EPSILON = 1e-06


def swap_chan(block):
    return lax.ppermute(block, "chan", [(0, 1), (1, 0)])


def row_halo(block):
    count = lax.axis_size("height")
    forward = [(i, i + 1) for i in range(count - 1)]
    backward = [(target, source) for source, target in forward]
    low = lax.ppermute(block[:, -1:], "height", forward)
    high = lax.ppermute(block[:, :1], "height", backward)
    return jnp.concatenate([low, block, high], axis=1)


def gather_tm(piece):
    count = lax.axis_size("tm")
    index = lax.axis_index("tm")
    pieces = [piece]
    for shift in range(1, count):
        pairs = [(i, (i - shift) % count) for i in range(count)]
        pieces.append(lax.ppermute(piece, "tm", pairs))
    stacked = jnp.roll(jnp.stack(pieces), index, axis=0)
    return stacked


def group_stats(grouped, axes, slot_axes):
    count = 1
    for axis in axes:
        count *= grouped.shape[axis]
    local_mean = jnp.sum(grouped, axis=axes) / count
    centred = grouped - jnp.expand_dims(local_mean, axes)
    local_m2 = jnp.sum(centred * centred, axis=axes)
    slots = 1
    for name in slot_axes:
        slots *= lax.axis_size(name)
    slot = 0
    for name in slot_axes:
        slot = slot * lax.axis_size(name) + lax.axis_index(name)
    mine = jnp.stack([local_mean, local_m2])
    table = jnp.zeros((slots,) + mine.shape, jnp.float32)
    table = lax.dynamic_update_index_in_dim(table, mine, slot, 0)
    for name in reversed(slot_axes):
        table = lax.psum(table, name)
    means = table[:, 0]
    average = jnp.sum(means, axis=0) / slots
    spread = means - average
    m2 = jnp.sum(table[:, 1], axis=0) + count * jnp.sum(spread * spread, axis=0)
    variance = m2 / (count * slots)
    return average, variance


def group_act(values, average, variance, gain, bias):
    frames, rows, local_chan, width = values.shape
    local_groups = average.shape[-1]
    grouped = values.reshape(frames, rows, local_groups, local_chan // local_groups, width)
    centred = grouped - average.reshape(-1, 1, local_groups, 1, 1)
    scaled = (centred * lax.rsqrt(variance.reshape(-1, 1, local_groups, 1, 1) + EPSILON)).reshape(
        frames, rows, local_chan, width
    )
    return jax.nn.silu(scaled * gain[:, None] + bias[:, None]).astype(jnp.bfloat16)


def in_order(own, other, chan_index):
    size = own.shape[2]
    joined = jnp.zeros(own.shape[:2] + (2 * size,) + own.shape[3:], own.dtype)
    joined = lax.dynamic_update_slice_in_dim(joined, own, chan_index * size, axis=2)
    return lax.dynamic_update_slice_in_dim(joined, other, (1 - chan_index) * size, axis=2)


def pair(ref, first):
    return jnp.concatenate([ref[0, first], ref[0, first + 1]], axis=1)


def spatial_kernel(xo_ref, xt_ref, wo_ref, wt_ref, res_ref, b_ref, o_ref):
    rows, local_chan, width = o_ref.shape[1], o_ref.shape[2], o_ref.shape[3]
    lane = lax.broadcasted_iota(jnp.int32, (local_chan, width), 1)
    bias = b_ref[...]

    def two_rows(i, carry):
        r = 2 * i
        y = jnp.dot(wo_ref[0], pair(xo_ref, r), preferred_element_type=jnp.float32)
        y = y + jnp.dot(wt_ref[0], pair(xt_ref, r), preferred_element_type=jnp.float32)
        for tap in (1, 2):
            y = y + jnp.dot(wo_ref[tap], pair(xo_ref, r + tap), preferred_element_type=jnp.float32)
            y = y + jnp.dot(wt_ref[tap], pair(xt_ref, r + tap), preferred_element_type=jnp.float32)
        for half in range(2):
            part = y[:, half * width : (half + 1) * width]
            left = pltpu.roll(part[:local_chan], 1, 1)
            left = jnp.where(lane == 0, 0.0, left)
            right = pltpu.roll(part[2 * local_chan :], width - 1, 1)
            right = jnp.where(lane == width - 1, 0.0, right)
            total = left + part[local_chan : 2 * local_chan] + right
            o_ref[0, r + half] = (res_ref[0, r + half].astype(jnp.float32) + total + bias).astype(
                o_ref.dtype
            )
        return carry

    lax.fori_loop(0, rows // 2, two_rows, 0)


def spatial_call(own, other, weight_own, weight_other, residual, bias):
    frames, rows, local_chan, width = residual.shape
    act_spec = pl.BlockSpec((1, rows + 2, local_chan, width), lambda f: (f, 0, 0, 0))
    weight_spec = pl.BlockSpec((3, 3 * local_chan, local_chan), lambda f: (0, 0, 0))
    return pl.pallas_call(
        spatial_kernel,
        out_shape=jax.ShapeDtypeStruct(residual.shape, jnp.bfloat16),
        grid=(frames,),
        in_specs=[
            act_spec,
            act_spec,
            weight_spec,
            weight_spec,
            pl.BlockSpec((1, rows, local_chan, width), lambda f: (f, 0, 0, 0)),
            pl.BlockSpec((local_chan, 1), lambda f: (0, 0)),
        ],
        out_specs=pl.BlockSpec((1, rows, local_chan, width), lambda f: (f, 0, 0, 0)),
        compiler_params=pltpu.CompilerParams(vmem_limit_bytes=48 * 1024 * 1024),
        cost_estimate=pl.CostEstimate(
            flops=2 * frames * rows * width * 18 * local_chan * local_chan,
            transcendentals=0,
            bytes_accessed=4 * own.size + 4 * weight_own.size + 4 * residual.size,
        ),
    )(own, other, weight_own, weight_other, residual, bias)


def temporal_kernel(*refs):
    own_refs, other_refs = refs[0:3], refs[3:6]
    wo_ref, wt_ref, res_ref, bias_ref, o_ref = refs[6:]
    rows, width = o_ref.shape[1], o_ref.shape[3]
    bias = bias_ref[...]

    def two_rows(i, carry):
        r = 2 * i
        y = jnp.dot(wo_ref[0], pair(own_refs[0], r), preferred_element_type=jnp.float32)
        y = y + jnp.dot(wt_ref[0], pair(other_refs[0], r), preferred_element_type=jnp.float32)
        for tap in (1, 2):
            y = y + jnp.dot(wo_ref[tap], pair(own_refs[tap], r), preferred_element_type=jnp.float32)
            y = y + jnp.dot(wt_ref[tap], pair(other_refs[tap], r), preferred_element_type=jnp.float32)
        for half in range(2):
            part = y[:, half * width : (half + 1) * width]
            o_ref[0, r + half] = (res_ref[0, r + half].astype(jnp.float32) + part + bias).astype(
                o_ref.dtype
            )
        return carry

    lax.fori_loop(0, rows // 2, two_rows, 0)


def frame_spec(tap, rows, chans, width):
    return pl.BlockSpec((1, rows, chans, width), lambda f: (f + tap, 0, 0, 0))


def temporal_call(own, other, weight_own, weight_other, residual, bias):
    frames, rows, local_chan, width = residual.shape
    taps = [frame_spec(tap, rows, local_chan, width) for tap in range(3)]
    weight_spec = pl.BlockSpec((3, local_chan, local_chan), lambda f: (0, 0, 0))
    return pl.pallas_call(
        temporal_kernel,
        out_shape=jax.ShapeDtypeStruct(residual.shape, jnp.bfloat16),
        grid=(frames,),
        in_specs=taps
        + taps
        + [
            weight_spec,
            weight_spec,
            pl.BlockSpec((1, rows, local_chan, width), lambda f: (f, 0, 0, 0)),
            pl.BlockSpec((local_chan, 1), lambda f: (0, 0)),
        ],
        out_specs=pl.BlockSpec((1, rows, local_chan, width), lambda f: (f, 0, 0, 0)),
        compiler_params=pltpu.CompilerParams(vmem_limit_bytes=48 * 1024 * 1024),
        cost_estimate=pl.CostEstimate(
            flops=2 * frames * rows * width * 6 * local_chan * local_chan,
            transcendentals=0,
            bytes_accessed=12 * residual.size + 4 * weight_own.size + 4 * residual.size,
        ),
    )(own, own, own, other, other, other, weight_own, weight_other, residual, bias)


def spatial_taps(running, channel_slab, weight, rows, width):
    for row_tap in range(3):
        for col_tap in range(3):
            window = channel_slab[:, row_tap : row_tap + rows, :, col_tap : col_tap + width]
            running = running + jnp.einsum(
                "frcw,co->frow", window, weight[row_tap, col_tap], preferred_element_type=jnp.float32
            )
    return running


def temporal_taps(running, channel_slab, weight, frames):
    for frame_tap in range(3):
        window = channel_slab[frame_tap : frame_tap + frames]
        running = running + jnp.einsum(
            "frcw,co->frow", window, weight[frame_tap], preferred_element_type=jnp.float32
        )
    return running


def body(
    video,
    norm1_gain,
    norm1_bias,
    spatial_weight,
    spatial_bias,
    norm2_gain,
    norm2_bias,
    temporal_weight,
    temporal_bias,
):
    frames, rows, local_chan, width = video.shape
    group_size = C // GROUPS
    local_groups = local_chan // group_size
    chan_index = lax.axis_index("chan")
    tm_index = lax.axis_index("tm")
    tm_count = lax.axis_size("tm")

    spatial_full = lax.all_gather(spatial_weight, "tm", axis=2, tiled=True).reshape(9, C, local_chan)
    temporal_pieces = gather_tm(temporal_weight)
    temporal_full = jnp.moveaxis(temporal_pieces, 0, 1).reshape(3, C, local_chan)
    spatial_full = spatial_full.reshape(3, 3, C, local_chan)

    values = video.astype(jnp.float32)
    grouped = values.reshape(frames, rows, local_groups, group_size, width)
    average, variance = group_stats(grouped, (1, 3, 4), ("height",))
    act_one = group_act(values, average, variance, norm1_gain, norm1_bias)

    with_rows = row_halo(act_one)
    own_start = chan_index * local_chan
    other_start = (1 - chan_index) * local_chan
    spatial_rows = jnp.transpose(spatial_full, (0, 1, 3, 2)).reshape(3, 3 * local_chan, C)
    hidden = spatial_call(
        with_rows,
        swap_chan(with_rows),
        lax.dynamic_slice_in_dim(spatial_rows, own_start, local_chan, axis=2),
        lax.dynamic_slice_in_dim(spatial_rows, other_start, local_chan, axis=2),
        video,
        spatial_bias[:, None],
    )

    forward = [(i, i + 1) for i in range(tm_count - 1)]
    backward = [(target, source) for source, target in forward]
    before = lax.ppermute(hidden[-1:], "tm", forward)
    after = lax.ppermute(hidden[:1], "tm", backward)

    hidden_values = hidden.astype(jnp.float32)
    grouped_two = hidden_values.reshape(frames, rows, local_groups, group_size, width)
    average_two, variance_two = group_stats(grouped_two, (0, 1, 3, 4), ("tm", "height"))

    extended = jnp.concatenate([before, hidden, after], axis=0).astype(jnp.float32)
    act_two = group_act(extended, average_two, variance_two, norm2_gain, norm2_bias)
    frame_ids = jnp.arange(frames + 2)
    inside = (frame_ids > 0) | (tm_index > 0)
    inside = inside & ((frame_ids < frames + 1) | (tm_index < tm_count - 1))
    act_two = jnp.where(inside[:, None, None, None], act_two, jnp.zeros_like(act_two))

    temporal_rows = jnp.transpose(temporal_full, (0, 2, 1))
    return temporal_call(
        act_two,
        swap_chan(act_two),
        lax.dynamic_slice_in_dim(temporal_rows, own_start, local_chan, axis=2),
        lax.dynamic_slice_in_dim(temporal_rows, other_start, local_chan, axis=2),
        hidden,
        temporal_bias[:, None],
    )


def solution(mesh):
    return jax.shard_map(
        body,
        mesh=mesh,
        in_specs=(
            P(("groups", "tm"), "height", "chan", None),
            P("chan"),
            P("chan"),
            P(None, None, "tm", "chan"),
            P("chan"),
            P("chan"),
            P("chan"),
            P(None, "tm", "chan"),
            P("chan"),
        ),
        out_specs=P(("groups", "tm"), "height", "chan", None),
        check_vma=False,
    )
```

```python
import jax
import jax.numpy as jnp
from jax import lax
from jax.experimental import pallas as pl
from jax.experimental.pallas import tpu as pltpu
from jax.sharding import PartitionSpec as P

C = 320
GROUPS = 32


EPSILON = 1e-06


def swap_chan(block):
    return lax.ppermute(block, "chan", [(0, 1), (1, 0)])


def row_halo(block):
    count = lax.axis_size("height")
    forward = [(i, i + 1) for i in range(count - 1)]
    backward = [(target, source) for source, target in forward]
    low = lax.ppermute(block[:, -1:], "height", forward)
    high = lax.ppermute(block[:, :1], "height", backward)
    return jnp.concatenate([low, block, high], axis=1)


def gather_tm(piece):
    count = lax.axis_size("tm")
    index = lax.axis_index("tm")
    pieces = [piece]
    for shift in range(1, count):
        pairs = [(i, (i - shift) % count) for i in range(count)]
        pieces.append(lax.ppermute(piece, "tm", pairs))
    stacked = jnp.roll(jnp.stack(pieces), index, axis=0)
    return stacked


def group_stats(grouped, axes, slot_axes):
    count = 1
    for axis in axes:
        count *= grouped.shape[axis]
    local_mean = jnp.sum(grouped, axis=axes) / count
    centred = grouped - jnp.expand_dims(local_mean, axes)
    local_m2 = jnp.sum(centred * centred, axis=axes)
    slots = 1
    for name in slot_axes:
        slots *= lax.axis_size(name)
    slot = 0
    for name in slot_axes:
        slot = slot * lax.axis_size(name) + lax.axis_index(name)
    mine = jnp.stack([local_mean, local_m2])
    table = jnp.zeros((slots,) + mine.shape, jnp.float32)
    table = lax.dynamic_update_index_in_dim(table, mine, slot, 0)
    for name in reversed(slot_axes):
        table = lax.psum(table, name)
    means = table[:, 0]
    average = jnp.sum(means, axis=0) / slots
    spread = means - average
    m2 = jnp.sum(table[:, 1], axis=0) + count * jnp.sum(spread * spread, axis=0)
    variance = m2 / (count * slots)
    return average, variance


def group_act(values, average, variance, gain, bias):
    frames, rows, local_chan, width = values.shape
    local_groups = average.shape[-1]
    grouped = values.reshape(frames, rows, local_groups, local_chan // local_groups, width)
    centred = grouped - average.reshape(-1, 1, local_groups, 1, 1)
    scaled = (centred * lax.rsqrt(variance.reshape(-1, 1, local_groups, 1, 1) + EPSILON)).reshape(
        frames, rows, local_chan, width
    )
    return jax.nn.silu(scaled * gain[:, None] + bias[:, None]).astype(jnp.bfloat16)


def in_order(own, other, chan_index):
    size = own.shape[2]
    joined = jnp.zeros(own.shape[:2] + (2 * size,) + own.shape[3:], own.dtype)
    joined = lax.dynamic_update_slice_in_dim(joined, own, chan_index * size, axis=2)
    return lax.dynamic_update_slice_in_dim(joined, other, (1 - chan_index) * size, axis=2)


def pair(ref, first):
    return jnp.concatenate([ref[0, first], ref[0, first + 1]], axis=1)


def spatial_kernel(xo_ref, xt_ref, wo_ref, wt_ref, res_ref, b_ref, o_ref):
    rows, local_chan, width = o_ref.shape[1], o_ref.shape[2], o_ref.shape[3]
    lane = lax.broadcasted_iota(jnp.int32, (local_chan, width), 1)
    bias = b_ref[...]

    def two_rows(i, carry):
        r = 2 * i
        y = jnp.dot(wo_ref[0], pair(xo_ref, r), preferred_element_type=jnp.float32)
        y = y + jnp.dot(wt_ref[0], pair(xt_ref, r), preferred_element_type=jnp.float32)
        for tap in (1, 2):
            y = y + jnp.dot(wo_ref[tap], pair(xo_ref, r + tap), preferred_element_type=jnp.float32)
            y = y + jnp.dot(wt_ref[tap], pair(xt_ref, r + tap), preferred_element_type=jnp.float32)
        for half in range(2):
            part = y[:, half * width : (half + 1) * width]
            left = pltpu.roll(part[:local_chan], 1, 1)
            left = jnp.where(lane == 0, 0.0, left)
            right = pltpu.roll(part[2 * local_chan :], width - 1, 1)
            right = jnp.where(lane == width - 1, 0.0, right)
            total = left + part[local_chan : 2 * local_chan] + right
            o_ref[0, r + half] = (res_ref[0, r + half].astype(jnp.float32) + total + bias).astype(
                o_ref.dtype
            )
        return carry

    lax.fori_loop(0, rows // 2, two_rows, 0)


def spatial_call(own, other, weight_own, weight_other, residual, bias):
    frames, rows, local_chan, width = residual.shape
    act_spec = pl.BlockSpec((1, rows + 2, local_chan, width), lambda f: (f, 0, 0, 0))
    weight_spec = pl.BlockSpec((3, 3 * local_chan, local_chan), lambda f: (0, 0, 0))
    return pl.pallas_call(
        spatial_kernel,
        out_shape=jax.ShapeDtypeStruct(residual.shape, jnp.bfloat16),
        grid=(frames,),
        in_specs=[
            act_spec,
            act_spec,
            weight_spec,
            weight_spec,
            pl.BlockSpec((1, rows, local_chan, width), lambda f: (f, 0, 0, 0)),
            pl.BlockSpec((local_chan, 1), lambda f: (0, 0)),
        ],
        out_specs=pl.BlockSpec((1, rows, local_chan, width), lambda f: (f, 0, 0, 0)),
        compiler_params=pltpu.CompilerParams(vmem_limit_bytes=48 * 1024 * 1024),
        cost_estimate=pl.CostEstimate(
            flops=2 * frames * rows * width * 18 * local_chan * local_chan,
            transcendentals=0,
            bytes_accessed=4 * own.size + 4 * weight_own.size + 4 * residual.size,
        ),
    )(own, other, weight_own, weight_other, residual, bias)


def temporal_kernel(*refs):
    own_refs, other_refs = refs[0:3], refs[3:6]
    wo_ref, wt_ref, res_ref, bias_ref, o_ref = refs[6:]
    rows, width = o_ref.shape[1], o_ref.shape[3]
    bias = bias_ref[...]

    def two_rows(i, carry):
        r = 2 * i
        y = jnp.dot(wo_ref[0], pair(own_refs[0], r), preferred_element_type=jnp.float32)
        y = y + jnp.dot(wt_ref[0], pair(other_refs[0], r), preferred_element_type=jnp.float32)
        for tap in (1, 2):
            y = y + jnp.dot(wo_ref[tap], pair(own_refs[tap], r), preferred_element_type=jnp.float32)
            y = y + jnp.dot(wt_ref[tap], pair(other_refs[tap], r), preferred_element_type=jnp.float32)
        for half in range(2):
            part = y[:, half * width : (half + 1) * width]
            o_ref[0, r + half] = (res_ref[0, r + half].astype(jnp.float32) + part + bias).astype(
                o_ref.dtype
            )
        return carry

    lax.fori_loop(0, rows // 2, two_rows, 0)


def frame_spec(tap, rows, chans, width):
    return pl.BlockSpec((1, rows, chans, width), lambda f: (f + tap, 0, 0, 0))


def temporal_call(own, other, weight_own, weight_other, residual, bias):
    frames, rows, local_chan, width = residual.shape
    taps = [frame_spec(tap, rows, local_chan, width) for tap in range(3)]
    weight_spec = pl.BlockSpec((3, local_chan, local_chan), lambda f: (0, 0, 0))
    return pl.pallas_call(
        temporal_kernel,
        out_shape=jax.ShapeDtypeStruct(residual.shape, jnp.bfloat16),
        grid=(frames,),
        in_specs=taps
        + taps
        + [
            weight_spec,
            weight_spec,
            pl.BlockSpec((1, rows, local_chan, width), lambda f: (f, 0, 0, 0)),
            pl.BlockSpec((local_chan, 1), lambda f: (0, 0)),
        ],
        out_specs=pl.BlockSpec((1, rows, local_chan, width), lambda f: (f, 0, 0, 0)),
        compiler_params=pltpu.CompilerParams(vmem_limit_bytes=48 * 1024 * 1024),
        cost_estimate=pl.CostEstimate(
            flops=2 * frames * rows * width * 6 * local_chan * local_chan,
            transcendentals=0,
            bytes_accessed=12 * residual.size + 4 * weight_own.size + 4 * residual.size,
        ),
    )(own, own, own, other, other, other, weight_own, weight_other, residual, bias)


def spatial_taps(running, channel_slab, weight, rows, width):
    for row_tap in range(3):
        for col_tap in range(3):
            window = channel_slab[:, row_tap : row_tap + rows, :, col_tap : col_tap + width]
            running = running + jnp.einsum(
                "frcw,co->frow", window, weight[row_tap, col_tap], preferred_element_type=jnp.float32
            )
    return running


def temporal_taps(running, channel_slab, weight, frames):
    for frame_tap in range(3):
        window = channel_slab[frame_tap : frame_tap + frames]
        running = running + jnp.einsum(
            "frcw,co->frow", window, weight[frame_tap], preferred_element_type=jnp.float32
        )
    return running


def body(
    video,
    norm1_gain,
    norm1_bias,
    spatial_weight,
    spatial_bias,
    norm2_gain,
    norm2_bias,
    temporal_weight,
    temporal_bias,
):
    frames, rows, local_chan, width = video.shape
    group_size = C // GROUPS
    local_groups = local_chan // group_size
    chan_index = lax.axis_index("chan")
    tm_index = lax.axis_index("tm")
    tm_count = lax.axis_size("tm")

    piece = spatial_weight.shape[2]
    merged = jnp.concatenate([spatial_weight.reshape(9, piece, local_chan), temporal_weight], axis=0)
    full_weight = lax.all_gather(merged, "tm", axis=1, tiled=True)
    spatial_full = full_weight[:9]
    temporal_full = full_weight[9:]
    spatial_full = spatial_full.reshape(3, 3, C, local_chan)

    values = video.astype(jnp.float32)
    grouped = values.reshape(frames, rows, local_groups, group_size, width)
    average, variance = group_stats(grouped, (1, 3, 4), ("height",))
    act_one = group_act(values, average, variance, norm1_gain, norm1_bias)

    with_rows = row_halo(act_one)
    own_start = chan_index * local_chan
    other_start = (1 - chan_index) * local_chan
    spatial_rows = jnp.transpose(spatial_full, (0, 1, 3, 2)).reshape(3, 3 * local_chan, C)
    hidden = spatial_call(
        with_rows,
        swap_chan(with_rows),
        lax.dynamic_slice_in_dim(spatial_rows, own_start, local_chan, axis=2),
        lax.dynamic_slice_in_dim(spatial_rows, other_start, local_chan, axis=2),
        video,
        spatial_bias[:, None],
    )

    forward = [(i, i + 1) for i in range(tm_count - 1)]
    backward = [(target, source) for source, target in forward]
    before = lax.ppermute(hidden[-1:], "tm", forward)
    after = lax.ppermute(hidden[:1], "tm", backward)

    hidden_values = hidden.astype(jnp.float32)
    grouped_two = hidden_values.reshape(frames, rows, local_groups, group_size, width)
    average_two, variance_two = group_stats(grouped_two, (0, 1, 3, 4), ("tm", "height"))

    extended = jnp.concatenate([before, hidden, after], axis=0).astype(jnp.float32)
    act_two = group_act(extended, average_two, variance_two, norm2_gain, norm2_bias)
    frame_ids = jnp.arange(frames + 2)
    inside = (frame_ids > 0) | (tm_index > 0)
    inside = inside & ((frame_ids < frames + 1) | (tm_index < tm_count - 1))
    act_two = jnp.where(inside[:, None, None, None], act_two, jnp.zeros_like(act_two))

    temporal_rows = jnp.transpose(temporal_full, (0, 2, 1))
    return temporal_call(
        act_two,
        swap_chan(act_two),
        lax.dynamic_slice_in_dim(temporal_rows, own_start, local_chan, axis=2),
        lax.dynamic_slice_in_dim(temporal_rows, other_start, local_chan, axis=2),
        hidden,
        temporal_bias[:, None],
    )


def solution(mesh):
    return jax.shard_map(
        body,
        mesh=mesh,
        in_specs=(
            P(("groups", "tm"), "height", "chan", None),
            P("chan"),
            P("chan"),
            P(None, None, "tm", "chan"),
            P("chan"),
            P("chan"),
            P("chan"),
            P(None, "tm", "chan"),
            P("chan"),
        ),
        out_specs=P(("groups", "tm"), "height", "chan", None),
        check_vma=False,
    )
```

```python
import jax
import jax.numpy as jnp
from jax import lax
from jax.experimental import pallas as pl
from jax.experimental.pallas import tpu as pltpu
from jax.sharding import PartitionSpec as P

C = 320
GROUPS = 32


EPSILON = 1e-06


def swap_chan(block):
    return lax.ppermute(block, "chan", [(0, 1), (1, 0)])


def row_halo(block):
    count = lax.axis_size("height")
    forward = [(i, i + 1) for i in range(count - 1)]
    backward = [(target, source) for source, target in forward]
    low = lax.ppermute(block[:, -1:], "height", forward)
    high = lax.ppermute(block[:, :1], "height", backward)
    return jnp.concatenate([low, block, high], axis=1)


def gather_tm(piece):
    count = lax.axis_size("tm")
    index = lax.axis_index("tm")
    pieces = [piece]
    for shift in range(1, count):
        pairs = [(i, (i - shift) % count) for i in range(count)]
        pieces.append(lax.ppermute(piece, "tm", pairs))
    stacked = jnp.roll(jnp.stack(pieces), index, axis=0)
    return stacked


def group_stats(grouped, axes, slot_axes):
    count = 1
    for axis in axes:
        count *= grouped.shape[axis]
    local_mean = jnp.sum(grouped, axis=axes) / count
    centred = grouped - jnp.expand_dims(local_mean, axes)
    local_m2 = jnp.sum(centred * centred, axis=axes)
    slots = 1
    for name in slot_axes:
        slots *= lax.axis_size(name)
    slot = 0
    for name in slot_axes:
        slot = slot * lax.axis_size(name) + lax.axis_index(name)
    mine = jnp.stack([local_mean, local_m2])
    table = jnp.zeros((slots,) + mine.shape, jnp.float32)
    table = lax.dynamic_update_index_in_dim(table, mine, slot, 0)
    for name in reversed(slot_axes):
        table = lax.psum(table, name)
    means = table[:, 0]
    average = jnp.sum(means, axis=0) / slots
    spread = means - average
    m2 = jnp.sum(table[:, 1], axis=0) + count * jnp.sum(spread * spread, axis=0)
    variance = m2 / (count * slots)
    return average, variance


def group_act(values, average, variance, gain, bias):
    frames, rows, local_chan, width = values.shape
    local_groups = average.shape[-1]
    grouped = values.reshape(frames, rows, local_groups, local_chan // local_groups, width)
    centred = grouped - average.reshape(-1, 1, local_groups, 1, 1)
    scaled = (centred * lax.rsqrt(variance.reshape(-1, 1, local_groups, 1, 1) + EPSILON)).reshape(
        frames, rows, local_chan, width
    )
    return jax.nn.silu(scaled * gain[:, None] + bias[:, None]).astype(jnp.bfloat16)


def in_order(own, other, chan_index):
    size = own.shape[2]
    joined = jnp.zeros(own.shape[:2] + (2 * size,) + own.shape[3:], own.dtype)
    joined = lax.dynamic_update_slice_in_dim(joined, own, chan_index * size, axis=2)
    return lax.dynamic_update_slice_in_dim(joined, other, (1 - chan_index) * size, axis=2)


def pair(ref, first):
    return jnp.concatenate([ref[0, first], ref[0, first + 1]], axis=1)


def spatial_kernel(xo_ref, xt_ref, wo_ref, wt_ref, res_ref, b_ref, early_ref, o_ref):
    rows, local_chan, width = o_ref.shape[1], o_ref.shape[2], o_ref.shape[3]
    lane = lax.broadcasted_iota(jnp.int32, (local_chan, width), 1)
    bias = b_ref[...]

    def two_rows(i, carry):
        r = 2 * i
        y = jnp.dot(wo_ref[0], pair(xo_ref, r), preferred_element_type=jnp.float32)
        y = y + jnp.dot(wt_ref[0], pair(xt_ref, r), preferred_element_type=jnp.float32)
        for tap in (1, 2):
            y = y + jnp.dot(wo_ref[tap], pair(xo_ref, r + tap), preferred_element_type=jnp.float32)
            y = y + jnp.dot(wt_ref[tap], pair(xt_ref, r + tap), preferred_element_type=jnp.float32)
        for half in range(2):
            part = y[:, half * width : (half + 1) * width]
            left = pltpu.roll(part[:local_chan], 1, 1)
            left = jnp.where(lane == 0, 0.0, left)
            right = pltpu.roll(part[2 * local_chan :], width - 1, 1)
            right = jnp.where(lane == width - 1, 0.0, right)
            total = left + part[local_chan : 2 * local_chan] + right
            o_ref[0, r + half] = (res_ref[0, r + half].astype(jnp.float32) + total + bias).astype(
                o_ref.dtype
            )
        return carry

    lax.fori_loop(0, rows // 2, two_rows, 0)


def spatial_call(own, other, weight_own, weight_other, residual, bias, early):
    frames, rows, local_chan, width = residual.shape
    act_spec = pl.BlockSpec((1, rows + 2, local_chan, width), lambda f: (f, 0, 0, 0))
    weight_spec = pl.BlockSpec((3, 3 * local_chan, local_chan), lambda f: (0, 0, 0))
    return pl.pallas_call(
        spatial_kernel,
        out_shape=jax.ShapeDtypeStruct(residual.shape, jnp.bfloat16),
        grid=(frames,),
        in_specs=[
            act_spec,
            act_spec,
            weight_spec,
            weight_spec,
            pl.BlockSpec((1, rows, local_chan, width), lambda f: (f, 0, 0, 0)),
            pl.BlockSpec((local_chan, 1), lambda f: (0, 0)),
            pl.BlockSpec(memory_space=pl.ANY),
        ],
        out_specs=pl.BlockSpec((1, rows, local_chan, width), lambda f: (f, 0, 0, 0)),
        compiler_params=pltpu.CompilerParams(vmem_limit_bytes=48 * 1024 * 1024),
        cost_estimate=pl.CostEstimate(
            flops=2 * frames * rows * width * 18 * local_chan * local_chan,
            transcendentals=0,
            bytes_accessed=4 * own.size + 4 * weight_own.size + 4 * residual.size,
        ),
    )(own, other, weight_own, weight_other, residual, bias, early)


def temporal_kernel(*refs):
    own_refs, other_refs = refs[0:3], refs[3:6]
    wo_ref, wt_ref, res_ref, bias_ref, o_ref = refs[6:]
    rows, width = o_ref.shape[1], o_ref.shape[3]
    bias = bias_ref[...]

    def two_rows(i, carry):
        r = 2 * i
        y = jnp.dot(wo_ref[0], pair(own_refs[0], r), preferred_element_type=jnp.float32)
        y = y + jnp.dot(wt_ref[0], pair(other_refs[0], r), preferred_element_type=jnp.float32)
        for tap in (1, 2):
            y = y + jnp.dot(wo_ref[tap], pair(own_refs[tap], r), preferred_element_type=jnp.float32)
            y = y + jnp.dot(wt_ref[tap], pair(other_refs[tap], r), preferred_element_type=jnp.float32)
        for half in range(2):
            part = y[:, half * width : (half + 1) * width]
            o_ref[0, r + half] = (res_ref[0, r + half].astype(jnp.float32) + part + bias).astype(
                o_ref.dtype
            )
        return carry

    lax.fori_loop(0, rows // 2, two_rows, 0)


def frame_spec(tap, rows, chans, width):
    return pl.BlockSpec((1, rows, chans, width), lambda f: (f + tap, 0, 0, 0))


def temporal_call(own, other, weight_own, weight_other, residual, bias):
    frames, rows, local_chan, width = residual.shape
    taps = [frame_spec(tap, rows, local_chan, width) for tap in range(3)]
    weight_spec = pl.BlockSpec((3, local_chan, local_chan), lambda f: (0, 0, 0))
    return pl.pallas_call(
        temporal_kernel,
        out_shape=jax.ShapeDtypeStruct(residual.shape, jnp.bfloat16),
        grid=(frames,),
        in_specs=taps
        + taps
        + [
            weight_spec,
            weight_spec,
            pl.BlockSpec((1, rows, local_chan, width), lambda f: (f, 0, 0, 0)),
            pl.BlockSpec((local_chan, 1), lambda f: (0, 0)),
        ],
        out_specs=pl.BlockSpec((1, rows, local_chan, width), lambda f: (f, 0, 0, 0)),
        compiler_params=pltpu.CompilerParams(vmem_limit_bytes=48 * 1024 * 1024),
        cost_estimate=pl.CostEstimate(
            flops=2 * frames * rows * width * 6 * local_chan * local_chan,
            transcendentals=0,
            bytes_accessed=12 * residual.size + 4 * weight_own.size + 4 * residual.size,
        ),
    )(own, own, own, other, other, other, weight_own, weight_other, residual, bias)


def spatial_taps(running, channel_slab, weight, rows, width):
    for row_tap in range(3):
        for col_tap in range(3):
            window = channel_slab[:, row_tap : row_tap + rows, :, col_tap : col_tap + width]
            running = running + jnp.einsum(
                "frcw,co->frow", window, weight[row_tap, col_tap], preferred_element_type=jnp.float32
            )
    return running


def temporal_taps(running, channel_slab, weight, frames):
    for frame_tap in range(3):
        window = channel_slab[frame_tap : frame_tap + frames]
        running = running + jnp.einsum(
            "frcw,co->frow", window, weight[frame_tap], preferred_element_type=jnp.float32
        )
    return running


def body(
    video,
    norm1_gain,
    norm1_bias,
    spatial_weight,
    spatial_bias,
    norm2_gain,
    norm2_bias,
    temporal_weight,
    temporal_bias,
):
    frames, rows, local_chan, width = video.shape
    group_size = C // GROUPS
    local_groups = local_chan // group_size
    chan_index = lax.axis_index("chan")
    tm_index = lax.axis_index("tm")
    tm_count = lax.axis_size("tm")

    spatial_full = lax.all_gather(spatial_weight, "tm", axis=2, tiled=True).reshape(9, C, local_chan)
    temporal_pieces = gather_tm(temporal_weight)
    temporal_full = jnp.moveaxis(temporal_pieces, 0, 1).reshape(3, C, local_chan)
    spatial_full = spatial_full.reshape(3, 3, C, local_chan)

    values = video.astype(jnp.float32)
    grouped = values.reshape(frames, rows, local_groups, group_size, width)
    average, variance = group_stats(grouped, (1, 3, 4), ("height",))
    act_one = group_act(values, average, variance, norm1_gain, norm1_bias)

    with_rows = row_halo(act_one)
    own_start = chan_index * local_chan
    other_start = (1 - chan_index) * local_chan
    spatial_rows = jnp.transpose(spatial_full, (0, 1, 3, 2)).reshape(3, 3 * local_chan, C)
    hidden = spatial_call(
        with_rows,
        swap_chan(with_rows),
        lax.dynamic_slice_in_dim(spatial_rows, own_start, local_chan, axis=2),
        lax.dynamic_slice_in_dim(spatial_rows, other_start, local_chan, axis=2),
        video,
        spatial_bias[:, None],
        temporal_pieces,
    )

    forward = [(i, i + 1) for i in range(tm_count - 1)]
    backward = [(target, source) for source, target in forward]
    before = lax.ppermute(hidden[-1:], "tm", forward)
    after = lax.ppermute(hidden[:1], "tm", backward)

    hidden_values = hidden.astype(jnp.float32)
    grouped_two = hidden_values.reshape(frames, rows, local_groups, group_size, width)
    average_two, variance_two = group_stats(grouped_two, (0, 1, 3, 4), ("tm", "height"))

    extended = jnp.concatenate([before, hidden, after], axis=0).astype(jnp.float32)
    act_two = group_act(extended, average_two, variance_two, norm2_gain, norm2_bias)
    frame_ids = jnp.arange(frames + 2)
    inside = (frame_ids > 0) | (tm_index > 0)
    inside = inside & ((frame_ids < frames + 1) | (tm_index < tm_count - 1))
    act_two = jnp.where(inside[:, None, None, None], act_two, jnp.zeros_like(act_two))

    temporal_rows = jnp.transpose(temporal_full, (0, 2, 1))
    return temporal_call(
        act_two,
        swap_chan(act_two),
        lax.dynamic_slice_in_dim(temporal_rows, own_start, local_chan, axis=2),
        lax.dynamic_slice_in_dim(temporal_rows, other_start, local_chan, axis=2),
        hidden,
        temporal_bias[:, None],
    )


def solution(mesh):
    return jax.shard_map(
        body,
        mesh=mesh,
        in_specs=(
            P(("groups", "tm"), "height", "chan", None),
            P("chan"),
            P("chan"),
            P(None, None, "tm", "chan"),
            P("chan"),
            P("chan"),
            P("chan"),
            P(None, "tm", "chan"),
            P("chan"),
        ),
        out_specs=P(("groups", "tm"), "height", "chan", None),
        check_vma=False,
    )
```

```python
import jax
import jax.numpy as jnp
from jax import lax
from jax.experimental import pallas as pl
from jax.experimental.pallas import tpu as pltpu
from jax.sharding import PartitionSpec as P

C = 320
GROUPS = 32


EPSILON = 1e-06


def swap_chan(block):
    return lax.ppermute(block, "chan", [(0, 1), (1, 0)])


def row_halo(block):
    count = lax.axis_size("height")
    forward = [(i, i + 1) for i in range(count - 1)]
    backward = [(target, source) for source, target in forward]
    low = lax.ppermute(block[:, -1:], "height", forward)
    high = lax.ppermute(block[:, :1], "height", backward)
    return jnp.concatenate([low, block, high], axis=1)


def gather_tm(piece):
    count = lax.axis_size("tm")
    index = lax.axis_index("tm")
    pieces = [piece]
    for shift in range(1, count):
        pairs = [(i, (i - shift) % count) for i in range(count)]
        pieces.append(lax.ppermute(piece, "tm", pairs))
    stacked = jnp.roll(jnp.stack(pieces), index, axis=0)
    return stacked


def group_stats(grouped, axes, slot_axes):
    count = 1
    for axis in axes:
        count *= grouped.shape[axis]
    local_mean = jnp.sum(grouped, axis=axes) / count
    centred = grouped - jnp.expand_dims(local_mean, axes)
    local_m2 = jnp.sum(centred * centred, axis=axes)
    slots = 1
    for name in slot_axes:
        slots *= lax.axis_size(name)
    slot = 0
    for name in slot_axes:
        slot = slot * lax.axis_size(name) + lax.axis_index(name)
    mine = jnp.stack([local_mean, local_m2])
    table = jnp.zeros((slots,) + mine.shape, jnp.float32)
    table = lax.dynamic_update_index_in_dim(table, mine, slot, 0)
    for name in reversed(slot_axes):
        table = lax.psum(table, name)
    means = table[:, 0]
    average = jnp.sum(means, axis=0) / slots
    spread = means - average
    m2 = jnp.sum(table[:, 1], axis=0) + count * jnp.sum(spread * spread, axis=0)
    variance = m2 / (count * slots)
    return average, variance


def group_act(values, average, variance, gain, bias):
    frames, rows, local_chan, width = values.shape
    local_groups = average.shape[-1]
    grouped = values.reshape(frames, rows, local_groups, local_chan // local_groups, width)
    centred = grouped - average.reshape(-1, 1, local_groups, 1, 1)
    scaled = (centred * lax.rsqrt(variance.reshape(-1, 1, local_groups, 1, 1) + EPSILON)).reshape(
        frames, rows, local_chan, width
    )
    return jax.nn.silu(scaled * gain[:, None] + bias[:, None]).astype(jnp.bfloat16)


def in_order(own, other, chan_index):
    size = own.shape[2]
    joined = jnp.zeros(own.shape[:2] + (2 * size,) + own.shape[3:], own.dtype)
    joined = lax.dynamic_update_slice_in_dim(joined, own, chan_index * size, axis=2)
    return lax.dynamic_update_slice_in_dim(joined, other, (1 - chan_index) * size, axis=2)


def pair(ref, first):
    return jnp.concatenate([ref[0, first], ref[0, first + 1]], axis=1)


def spatial_kernel(xo_ref, xt_ref, wo_ref, wt_ref, res_ref, b_ref, early_ref, o_ref):
    rows, local_chan, width = o_ref.shape[1], o_ref.shape[2], o_ref.shape[3]
    lane = lax.broadcasted_iota(jnp.int32, (local_chan, width), 1)
    bias = b_ref[...]

    def two_rows(i, carry):
        r = 2 * i
        y = jnp.dot(wo_ref[0], pair(xo_ref, r), preferred_element_type=jnp.float32)
        y = y + jnp.dot(wt_ref[0], pair(xt_ref, r), preferred_element_type=jnp.float32)
        for tap in (1, 2):
            y = y + jnp.dot(wo_ref[tap], pair(xo_ref, r + tap), preferred_element_type=jnp.float32)
            y = y + jnp.dot(wt_ref[tap], pair(xt_ref, r + tap), preferred_element_type=jnp.float32)
        for half in range(2):
            part = y[:, half * width : (half + 1) * width]
            left = pltpu.roll(part[:local_chan], 1, 1)
            left = jnp.where(lane == 0, 0.0, left)
            right = pltpu.roll(part[2 * local_chan :], width - 1, 1)
            right = jnp.where(lane == width - 1, 0.0, right)
            total = left + part[local_chan : 2 * local_chan] + right
            o_ref[0, r + half] = (res_ref[0, r + half].astype(jnp.float32) + total + bias).astype(
                o_ref.dtype
            )
        return carry

    lax.fori_loop(0, rows // 2, two_rows, 0)


def spatial_call(own, other, weight_own, weight_other, residual, bias, early):
    frames, rows, local_chan, width = residual.shape
    act_spec = pl.BlockSpec((1, rows + 2, local_chan, width), lambda f: (f, 0, 0, 0))
    weight_spec = pl.BlockSpec((3, 3 * local_chan, local_chan), lambda f: (0, 0, 0))
    return pl.pallas_call(
        spatial_kernel,
        out_shape=jax.ShapeDtypeStruct(residual.shape, jnp.bfloat16),
        grid=(frames,),
        in_specs=[
            act_spec,
            act_spec,
            weight_spec,
            weight_spec,
            pl.BlockSpec((1, rows, local_chan, width), lambda f: (f, 0, 0, 0)),
            pl.BlockSpec((local_chan, 1), lambda f: (0, 0)),
            pl.BlockSpec(memory_space=pl.ANY),
        ],
        out_specs=pl.BlockSpec((1, rows, local_chan, width), lambda f: (f, 0, 0, 0)),
        compiler_params=pltpu.CompilerParams(vmem_limit_bytes=48 * 1024 * 1024),
        cost_estimate=pl.CostEstimate(
            flops=2 * frames * rows * width * 18 * local_chan * local_chan,
            transcendentals=0,
            bytes_accessed=4 * own.size + 4 * weight_own.size + 4 * residual.size,
        ),
    )(own, other, weight_own, weight_other, residual, bias, early)


def temporal_kernel(*refs):
    own_refs, other_refs = refs[0:3], refs[3:6]
    wo_ref, wt_ref, res_ref, bias_ref, o_ref = refs[6:]
    rows, width = o_ref.shape[1], o_ref.shape[3]
    bias = bias_ref[...]

    def two_rows(i, carry):
        r = 2 * i
        y = jnp.dot(wo_ref[0], pair(own_refs[0], r), preferred_element_type=jnp.float32)
        y = y + jnp.dot(wt_ref[0], pair(other_refs[0], r), preferred_element_type=jnp.float32)
        for tap in (1, 2):
            y = y + jnp.dot(wo_ref[tap], pair(own_refs[tap], r), preferred_element_type=jnp.float32)
            y = y + jnp.dot(wt_ref[tap], pair(other_refs[tap], r), preferred_element_type=jnp.float32)
        for half in range(2):
            part = y[:, half * width : (half + 1) * width]
            o_ref[0, r + half] = (res_ref[0, r + half].astype(jnp.float32) + part + bias).astype(
                o_ref.dtype
            )
        return carry

    lax.fori_loop(0, rows // 2, two_rows, 0)


def frame_spec(tap, rows, chans, width):
    return pl.BlockSpec((1, rows, chans, width), lambda f: (f + tap, 0, 0, 0))


def temporal_call(own, other, weight_own, weight_other, residual, bias):
    frames, rows, local_chan, width = residual.shape
    taps = [frame_spec(tap, rows, local_chan, width) for tap in range(3)]
    weight_spec = pl.BlockSpec((3, local_chan, local_chan), lambda f: (0, 0, 0))
    return pl.pallas_call(
        temporal_kernel,
        out_shape=jax.ShapeDtypeStruct(residual.shape, jnp.bfloat16),
        grid=(frames,),
        in_specs=taps
        + taps
        + [
            weight_spec,
            weight_spec,
            pl.BlockSpec((1, rows, local_chan, width), lambda f: (f, 0, 0, 0)),
            pl.BlockSpec((local_chan, 1), lambda f: (0, 0)),
        ],
        out_specs=pl.BlockSpec((1, rows, local_chan, width), lambda f: (f, 0, 0, 0)),
        compiler_params=pltpu.CompilerParams(vmem_limit_bytes=48 * 1024 * 1024),
        cost_estimate=pl.CostEstimate(
            flops=2 * frames * rows * width * 6 * local_chan * local_chan,
            transcendentals=0,
            bytes_accessed=12 * residual.size + 4 * weight_own.size + 4 * residual.size,
        ),
    )(own, own, own, other, other, other, weight_own, weight_other, residual, bias)


def spatial_taps(running, channel_slab, weight, rows, width):
    for row_tap in range(3):
        for col_tap in range(3):
            window = channel_slab[:, row_tap : row_tap + rows, :, col_tap : col_tap + width]
            running = running + jnp.einsum(
                "frcw,co->frow", window, weight[row_tap, col_tap], preferred_element_type=jnp.float32
            )
    return running


def temporal_taps(running, channel_slab, weight, frames):
    for frame_tap in range(3):
        window = channel_slab[frame_tap : frame_tap + frames]
        running = running + jnp.einsum(
            "frcw,co->frow", window, weight[frame_tap], preferred_element_type=jnp.float32
        )
    return running


def body(
    video,
    norm1_gain,
    norm1_bias,
    spatial_weight,
    spatial_bias,
    norm2_gain,
    norm2_bias,
    temporal_weight,
    temporal_bias,
):
    frames, rows, local_chan, width = video.shape
    group_size = C // GROUPS
    local_groups = local_chan // group_size
    chan_index = lax.axis_index("chan")
    tm_index = lax.axis_index("tm")
    tm_count = lax.axis_size("tm")

    spatial_pieces = gather_tm(spatial_weight)
    temporal_pieces = gather_tm(temporal_weight)
    temporal_full = jnp.moveaxis(temporal_pieces, 0, 1).reshape(3, C, local_chan)

    values = video.astype(jnp.float32)
    grouped = values.reshape(frames, rows, local_groups, group_size, width)
    average, variance = group_stats(grouped, (1, 3, 4), ("height",))
    act_one = group_act(values, average, variance, norm1_gain, norm1_bias)
    act_one, spatial_pieces = lax.optimization_barrier((act_one, spatial_pieces))
    spatial_full = jnp.moveaxis(spatial_pieces, 0, 2).reshape(3, 3, C, local_chan)

    with_rows = row_halo(act_one)
    own_start = chan_index * local_chan
    other_start = (1 - chan_index) * local_chan
    spatial_rows = jnp.transpose(spatial_full, (0, 1, 3, 2)).reshape(3, 3 * local_chan, C)
    hidden = spatial_call(
        with_rows,
        swap_chan(with_rows),
        lax.dynamic_slice_in_dim(spatial_rows, own_start, local_chan, axis=2),
        lax.dynamic_slice_in_dim(spatial_rows, other_start, local_chan, axis=2),
        video,
        spatial_bias[:, None],
        temporal_pieces,
    )

    forward = [(i, i + 1) for i in range(tm_count - 1)]
    backward = [(target, source) for source, target in forward]
    before = lax.ppermute(hidden[-1:], "tm", forward)
    after = lax.ppermute(hidden[:1], "tm", backward)

    hidden_values = hidden.astype(jnp.float32)
    grouped_two = hidden_values.reshape(frames, rows, local_groups, group_size, width)
    average_two, variance_two = group_stats(grouped_two, (0, 1, 3, 4), ("tm", "height"))

    extended = jnp.concatenate([before, hidden, after], axis=0).astype(jnp.float32)
    act_two = group_act(extended, average_two, variance_two, norm2_gain, norm2_bias)
    frame_ids = jnp.arange(frames + 2)
    inside = (frame_ids > 0) | (tm_index > 0)
    inside = inside & ((frame_ids < frames + 1) | (tm_index < tm_count - 1))
    act_two = jnp.where(inside[:, None, None, None], act_two, jnp.zeros_like(act_two))

    temporal_rows = jnp.transpose(temporal_full, (0, 2, 1))
    return temporal_call(
        act_two,
        swap_chan(act_two),
        lax.dynamic_slice_in_dim(temporal_rows, own_start, local_chan, axis=2),
        lax.dynamic_slice_in_dim(temporal_rows, other_start, local_chan, axis=2),
        hidden,
        temporal_bias[:, None],
    )


def solution(mesh):
    return jax.shard_map(
        body,
        mesh=mesh,
        in_specs=(
            P(("groups", "tm"), "height", "chan", None),
            P("chan"),
            P("chan"),
            P(None, None, "tm", "chan"),
            P("chan"),
            P("chan"),
            P("chan"),
            P(None, "tm", "chan"),
            P("chan"),
        ),
        out_specs=P(("groups", "tm"), "height", "chan", None),
        check_vma=False,
    )
```

```python
import jax
import jax.numpy as jnp
from jax import lax
from jax.experimental import pallas as pl
from jax.experimental.pallas import tpu as pltpu
from jax.sharding import PartitionSpec as P

C = 320
GROUPS = 32


EPSILON = 1e-06


def swap_chan(block):
    return lax.ppermute(block, "chan", [(0, 1), (1, 0)])


def row_halo(block):
    count = lax.axis_size("height")
    forward = [(i, i + 1) for i in range(count - 1)]
    backward = [(target, source) for source, target in forward]
    low = lax.ppermute(block[:, -1:], "height", forward)
    high = lax.ppermute(block[:, :1], "height", backward)
    return jnp.concatenate([low, block, high], axis=1)


def gather_tm(piece):
    count = lax.axis_size("tm")
    index = lax.axis_index("tm")
    pieces = [piece]
    for shift in range(1, count):
        pairs = [(i, (i - shift) % count) for i in range(count)]
        pieces.append(lax.ppermute(piece, "tm", pairs))
    stacked = jnp.roll(jnp.stack(pieces), index, axis=0)
    return stacked


def butterfly_sum(block, name):
    count = lax.axis_size(name)
    if count & (count - 1):
        return lax.psum(block, name)
    distance = 1
    while distance < count:
        pairs = [(i, i ^ distance) for i in range(count)]
        block = block + lax.ppermute(block, name, pairs)
        distance *= 2
    return block


def group_stats(grouped, axes, slot_axes):
    count = 1
    for axis in axes:
        count *= grouped.shape[axis]
    local_mean = jnp.sum(grouped, axis=axes) / count
    centred = grouped - jnp.expand_dims(local_mean, axes)
    local_m2 = jnp.sum(centred * centred, axis=axes)
    slots = 1
    for name in slot_axes:
        slots *= lax.axis_size(name)
    slot = 0
    for name in slot_axes:
        slot = slot * lax.axis_size(name) + lax.axis_index(name)
    mine = jnp.stack([local_mean, local_m2])
    table = jnp.zeros((slots,) + mine.shape, jnp.float32)
    table = lax.dynamic_update_index_in_dim(table, mine, slot, 0)
    for name in reversed(slot_axes):
        table = butterfly_sum(table, name)
    means = table[:, 0]
    average = jnp.sum(means, axis=0) / slots
    spread = means - average
    m2 = jnp.sum(table[:, 1], axis=0) + count * jnp.sum(spread * spread, axis=0)
    variance = m2 / (count * slots)
    return average, variance


def group_act(values, average, variance, gain, bias):
    frames, rows, local_chan, width = values.shape
    local_groups = average.shape[-1]
    grouped = values.reshape(frames, rows, local_groups, local_chan // local_groups, width)
    centred = grouped - average.reshape(-1, 1, local_groups, 1, 1)
    scaled = (centred * lax.rsqrt(variance.reshape(-1, 1, local_groups, 1, 1) + EPSILON)).reshape(
        frames, rows, local_chan, width
    )
    return jax.nn.silu(scaled * gain[:, None] + bias[:, None]).astype(jnp.bfloat16)


def in_order(own, other, chan_index):
    size = own.shape[2]
    joined = jnp.zeros(own.shape[:2] + (2 * size,) + own.shape[3:], own.dtype)
    joined = lax.dynamic_update_slice_in_dim(joined, own, chan_index * size, axis=2)
    return lax.dynamic_update_slice_in_dim(joined, other, (1 - chan_index) * size, axis=2)


def pair(ref, first):
    return jnp.concatenate([ref[0, first], ref[0, first + 1]], axis=1)


def spatial_kernel(xo_ref, xt_ref, wo_ref, wt_ref, res_ref, b_ref, early_ref, o_ref):
    rows, local_chan, width = o_ref.shape[1], o_ref.shape[2], o_ref.shape[3]
    lane = lax.broadcasted_iota(jnp.int32, (local_chan, width), 1)
    bias = b_ref[...]

    def two_rows(i, carry):
        r = 2 * i
        y = jnp.dot(wo_ref[0], pair(xo_ref, r), preferred_element_type=jnp.float32)
        y = y + jnp.dot(wt_ref[0], pair(xt_ref, r), preferred_element_type=jnp.float32)
        for tap in (1, 2):
            y = y + jnp.dot(wo_ref[tap], pair(xo_ref, r + tap), preferred_element_type=jnp.float32)
            y = y + jnp.dot(wt_ref[tap], pair(xt_ref, r + tap), preferred_element_type=jnp.float32)
        for half in range(2):
            part = y[:, half * width : (half + 1) * width]
            left = pltpu.roll(part[:local_chan], 1, 1)
            left = jnp.where(lane == 0, 0.0, left)
            right = pltpu.roll(part[2 * local_chan :], width - 1, 1)
            right = jnp.where(lane == width - 1, 0.0, right)
            total = left + part[local_chan : 2 * local_chan] + right
            o_ref[0, r + half] = (res_ref[0, r + half].astype(jnp.float32) + total + bias).astype(
                o_ref.dtype
            )
        return carry

    lax.fori_loop(0, rows // 2, two_rows, 0)


def spatial_call(own, other, weight_own, weight_other, residual, bias, early):
    frames, rows, local_chan, width = residual.shape
    act_spec = pl.BlockSpec((1, rows + 2, local_chan, width), lambda f: (f, 0, 0, 0))
    weight_spec = pl.BlockSpec((3, 3 * local_chan, local_chan), lambda f: (0, 0, 0))
    return pl.pallas_call(
        spatial_kernel,
        out_shape=jax.ShapeDtypeStruct(residual.shape, jnp.bfloat16),
        grid=(frames,),
        in_specs=[
            act_spec,
            act_spec,
            weight_spec,
            weight_spec,
            pl.BlockSpec((1, rows, local_chan, width), lambda f: (f, 0, 0, 0)),
            pl.BlockSpec((local_chan, 1), lambda f: (0, 0)),
            pl.BlockSpec(memory_space=pl.ANY),
        ],
        out_specs=pl.BlockSpec((1, rows, local_chan, width), lambda f: (f, 0, 0, 0)),
        compiler_params=pltpu.CompilerParams(vmem_limit_bytes=48 * 1024 * 1024),
        cost_estimate=pl.CostEstimate(
            flops=2 * frames * rows * width * 18 * local_chan * local_chan,
            transcendentals=0,
            bytes_accessed=4 * own.size + 4 * weight_own.size + 4 * residual.size,
        ),
    )(own, other, weight_own, weight_other, residual, bias, early)


def temporal_kernel(*refs):
    own_refs, other_refs = refs[0:3], refs[3:6]
    wo_ref, wt_ref, res_ref, bias_ref, o_ref = refs[6:]
    rows, width = o_ref.shape[1], o_ref.shape[3]
    bias = bias_ref[...]

    def two_rows(i, carry):
        r = 2 * i
        y = jnp.dot(wo_ref[0], pair(own_refs[0], r), preferred_element_type=jnp.float32)
        y = y + jnp.dot(wt_ref[0], pair(other_refs[0], r), preferred_element_type=jnp.float32)
        for tap in (1, 2):
            y = y + jnp.dot(wo_ref[tap], pair(own_refs[tap], r), preferred_element_type=jnp.float32)
            y = y + jnp.dot(wt_ref[tap], pair(other_refs[tap], r), preferred_element_type=jnp.float32)
        for half in range(2):
            part = y[:, half * width : (half + 1) * width]
            o_ref[0, r + half] = (res_ref[0, r + half].astype(jnp.float32) + part + bias).astype(
                o_ref.dtype
            )
        return carry

    lax.fori_loop(0, rows // 2, two_rows, 0)


def frame_spec(tap, rows, chans, width):
    return pl.BlockSpec((1, rows, chans, width), lambda f: (f + tap, 0, 0, 0))


def temporal_call(own, other, weight_own, weight_other, residual, bias):
    frames, rows, local_chan, width = residual.shape
    taps = [frame_spec(tap, rows, local_chan, width) for tap in range(3)]
    weight_spec = pl.BlockSpec((3, local_chan, local_chan), lambda f: (0, 0, 0))
    return pl.pallas_call(
        temporal_kernel,
        out_shape=jax.ShapeDtypeStruct(residual.shape, jnp.bfloat16),
        grid=(frames,),
        in_specs=taps
        + taps
        + [
            weight_spec,
            weight_spec,
            pl.BlockSpec((1, rows, local_chan, width), lambda f: (f, 0, 0, 0)),
            pl.BlockSpec((local_chan, 1), lambda f: (0, 0)),
        ],
        out_specs=pl.BlockSpec((1, rows, local_chan, width), lambda f: (f, 0, 0, 0)),
        compiler_params=pltpu.CompilerParams(vmem_limit_bytes=48 * 1024 * 1024),
        cost_estimate=pl.CostEstimate(
            flops=2 * frames * rows * width * 6 * local_chan * local_chan,
            transcendentals=0,
            bytes_accessed=12 * residual.size + 4 * weight_own.size + 4 * residual.size,
        ),
    )(own, own, own, other, other, other, weight_own, weight_other, residual, bias)


def spatial_taps(running, channel_slab, weight, rows, width):
    for row_tap in range(3):
        for col_tap in range(3):
            window = channel_slab[:, row_tap : row_tap + rows, :, col_tap : col_tap + width]
            running = running + jnp.einsum(
                "frcw,co->frow", window, weight[row_tap, col_tap], preferred_element_type=jnp.float32
            )
    return running


def temporal_taps(running, channel_slab, weight, frames):
    for frame_tap in range(3):
        window = channel_slab[frame_tap : frame_tap + frames]
        running = running + jnp.einsum(
            "frcw,co->frow", window, weight[frame_tap], preferred_element_type=jnp.float32
        )
    return running


def body(
    video,
    norm1_gain,
    norm1_bias,
    spatial_weight,
    spatial_bias,
    norm2_gain,
    norm2_bias,
    temporal_weight,
    temporal_bias,
):
    frames, rows, local_chan, width = video.shape
    group_size = C // GROUPS
    local_groups = local_chan // group_size
    chan_index = lax.axis_index("chan")
    tm_index = lax.axis_index("tm")
    tm_count = lax.axis_size("tm")

    spatial_full = lax.all_gather(spatial_weight, "tm", axis=2, tiled=True).reshape(9, C, local_chan)
    temporal_pieces = gather_tm(temporal_weight)
    temporal_full = jnp.moveaxis(temporal_pieces, 0, 1).reshape(3, C, local_chan)
    spatial_full = spatial_full.reshape(3, 3, C, local_chan)

    values = video.astype(jnp.float32)
    grouped = values.reshape(frames, rows, local_groups, group_size, width)
    average, variance = group_stats(grouped, (1, 3, 4), ("height",))
    act_one = group_act(values, average, variance, norm1_gain, norm1_bias)

    with_rows = row_halo(act_one)
    own_start = chan_index * local_chan
    other_start = (1 - chan_index) * local_chan
    spatial_rows = jnp.transpose(spatial_full, (0, 1, 3, 2)).reshape(3, 3 * local_chan, C)
    hidden = spatial_call(
        with_rows,
        swap_chan(with_rows),
        lax.dynamic_slice_in_dim(spatial_rows, own_start, local_chan, axis=2),
        lax.dynamic_slice_in_dim(spatial_rows, other_start, local_chan, axis=2),
        video,
        spatial_bias[:, None],
        temporal_pieces,
    )

    forward = [(i, i + 1) for i in range(tm_count - 1)]
    backward = [(target, source) for source, target in forward]
    before = lax.ppermute(hidden[-1:], "tm", forward)
    after = lax.ppermute(hidden[:1], "tm", backward)

    hidden_values = hidden.astype(jnp.float32)
    grouped_two = hidden_values.reshape(frames, rows, local_groups, group_size, width)
    average_two, variance_two = group_stats(grouped_two, (0, 1, 3, 4), ("tm", "height"))

    extended = jnp.concatenate([before, hidden, after], axis=0).astype(jnp.float32)
    act_two = group_act(extended, average_two, variance_two, norm2_gain, norm2_bias)
    frame_ids = jnp.arange(frames + 2)
    inside = (frame_ids > 0) | (tm_index > 0)
    inside = inside & ((frame_ids < frames + 1) | (tm_index < tm_count - 1))
    act_two = jnp.where(inside[:, None, None, None], act_two, jnp.zeros_like(act_two))

    temporal_rows = jnp.transpose(temporal_full, (0, 2, 1))
    return temporal_call(
        act_two,
        swap_chan(act_two),
        lax.dynamic_slice_in_dim(temporal_rows, own_start, local_chan, axis=2),
        lax.dynamic_slice_in_dim(temporal_rows, other_start, local_chan, axis=2),
        hidden,
        temporal_bias[:, None],
    )


def solution(mesh):
    return jax.shard_map(
        body,
        mesh=mesh,
        in_specs=(
            P(("groups", "tm"), "height", "chan", None),
            P("chan"),
            P("chan"),
            P(None, None, "tm", "chan"),
            P("chan"),
            P("chan"),
            P("chan"),
            P(None, "tm", "chan"),
            P("chan"),
        ),
        out_specs=P(("groups", "tm"), "height", "chan", None),
        check_vma=False,
    )
```

```python
import jax
import jax.numpy as jnp
from jax import lax
from jax.experimental import pallas as pl
from jax.experimental.pallas import tpu as pltpu
from jax.sharding import PartitionSpec as P

C = 320
GROUPS = 32


EPSILON = 1e-06


def swap_chan(block):
    return lax.ppermute(block, "chan", [(0, 1), (1, 0)])


def row_halo(block):
    count = lax.axis_size("height")
    forward = [(i, i + 1) for i in range(count - 1)]
    backward = [(target, source) for source, target in forward]
    low = lax.ppermute(block[:, -1:], "height", forward)
    high = lax.ppermute(block[:, :1], "height", backward)
    return jnp.concatenate([low, block, high], axis=1)


def gather_tm(piece):
    count = lax.axis_size("tm")
    index = lax.axis_index("tm")
    pieces = [piece]
    for shift in range(1, count):
        pairs = [(i, (i - shift) % count) for i in range(count)]
        pieces.append(lax.ppermute(piece, "tm", pairs))
    stacked = jnp.roll(jnp.stack(pieces), index, axis=0)
    return stacked


def group_stats(grouped, axes, slot_axes):
    count = 1
    for axis in axes:
        count *= grouped.shape[axis]
    local_mean = jnp.sum(grouped, axis=axes) / count
    centred = grouped - jnp.expand_dims(local_mean, axes)
    local_m2 = jnp.sum(centred * centred, axis=axes)
    slots = 1
    for name in slot_axes:
        slots *= lax.axis_size(name)
    slot = 0
    for name in slot_axes:
        slot = slot * lax.axis_size(name) + lax.axis_index(name)
    mine = jnp.stack([local_mean, local_m2])
    table = jnp.zeros((slots,) + mine.shape, jnp.float32)
    table = lax.dynamic_update_index_in_dim(table, mine, slot, 0)
    for name in reversed(slot_axes):
        table = lax.psum(table, name)
    means = table[:, 0]
    average = jnp.sum(means, axis=0) / slots
    spread = means - average
    m2 = jnp.sum(table[:, 1], axis=0) + count * jnp.sum(spread * spread, axis=0)
    variance = m2 / (count * slots)
    return average, variance


def group_act(values, average, variance, gain, bias):
    frames, rows, local_chan, width = values.shape
    local_groups = average.shape[-1]
    grouped = values.reshape(frames, rows, local_groups, local_chan // local_groups, width)
    centred = grouped - average.reshape(-1, 1, local_groups, 1, 1)
    scaled = (centred * lax.rsqrt(variance.reshape(-1, 1, local_groups, 1, 1) + EPSILON)).reshape(
        frames, rows, local_chan, width
    )
    return jax.nn.silu(scaled * gain[:, None] + bias[:, None]).astype(jnp.bfloat16)


def in_order(own, other, chan_index):
    size = own.shape[2]
    joined = jnp.zeros(own.shape[:2] + (2 * size,) + own.shape[3:], own.dtype)
    joined = lax.dynamic_update_slice_in_dim(joined, own, chan_index * size, axis=2)
    return lax.dynamic_update_slice_in_dim(joined, other, (1 - chan_index) * size, axis=2)


def pair(ref, first):
    return jnp.concatenate([ref[0, first], ref[0, first + 1]], axis=1)


def spatial_kernel(xo_ref, xt_ref, wo_ref, wt_ref, res_ref, b_ref, o_ref):
    rows, local_chan, width = o_ref.shape[1], o_ref.shape[2], o_ref.shape[3]
    lane = lax.broadcasted_iota(jnp.int32, (local_chan, width), 1)
    bias = b_ref[...]

    def two_rows(i, carry):
        r = 2 * i
        y = jnp.dot(wo_ref[0], pair(xo_ref, r), preferred_element_type=jnp.float32)
        y = y + jnp.dot(wt_ref[0], pair(xt_ref, r), preferred_element_type=jnp.float32)
        for tap in (1, 2):
            y = y + jnp.dot(wo_ref[tap], pair(xo_ref, r + tap), preferred_element_type=jnp.float32)
            y = y + jnp.dot(wt_ref[tap], pair(xt_ref, r + tap), preferred_element_type=jnp.float32)
        for half in range(2):
            part = y[:, half * width : (half + 1) * width]
            left = pltpu.roll(part[:local_chan], 1, 1)
            left = jnp.where(lane == 0, 0.0, left)
            right = pltpu.roll(part[2 * local_chan :], width - 1, 1)
            right = jnp.where(lane == width - 1, 0.0, right)
            total = left + part[local_chan : 2 * local_chan] + right
            o_ref[0, r + half] = (res_ref[0, r + half].astype(jnp.float32) + total + bias).astype(
                o_ref.dtype
            )
        return carry

    lax.fori_loop(0, rows // 2, two_rows, 0)


def spatial_call(own, other, weight_own, weight_other, residual, bias):
    frames, rows, local_chan, width = residual.shape
    act_spec = pl.BlockSpec((1, rows + 2, local_chan, width), lambda f: (f, 0, 0, 0))
    weight_spec = pl.BlockSpec((3, 3 * local_chan, local_chan), lambda f: (0, 0, 0))
    return pl.pallas_call(
        spatial_kernel,
        out_shape=jax.ShapeDtypeStruct(residual.shape, jnp.bfloat16),
        grid=(frames,),
        in_specs=[
            act_spec,
            act_spec,
            weight_spec,
            weight_spec,
            pl.BlockSpec((1, rows, local_chan, width), lambda f: (f, 0, 0, 0)),
            pl.BlockSpec((local_chan, 1), lambda f: (0, 0)),
        ],
        out_specs=pl.BlockSpec((1, rows, local_chan, width), lambda f: (f, 0, 0, 0)),
        compiler_params=pltpu.CompilerParams(vmem_limit_bytes=48 * 1024 * 1024),
        cost_estimate=pl.CostEstimate(
            flops=2 * frames * rows * width * 18 * local_chan * local_chan,
            transcendentals=0,
            bytes_accessed=4 * own.size + 4 * weight_own.size + 4 * residual.size,
        ),
    )(own, other, weight_own, weight_other, residual, bias)


def temporal_kernel(*refs):
    own_refs, other_refs = refs[0:3], refs[3:6]
    wo_ref, wt_ref, res_ref, bias_ref, o_ref = refs[6:]
    rows, width = o_ref.shape[1], o_ref.shape[3]
    bias = bias_ref[...]

    def two_rows(i, carry):
        r = 2 * i
        y = jnp.dot(wo_ref[0], pair(own_refs[0], r), preferred_element_type=jnp.float32)
        y = y + jnp.dot(wt_ref[0], pair(other_refs[0], r), preferred_element_type=jnp.float32)
        for tap in (1, 2):
            y = y + jnp.dot(wo_ref[tap], pair(own_refs[tap], r), preferred_element_type=jnp.float32)
            y = y + jnp.dot(wt_ref[tap], pair(other_refs[tap], r), preferred_element_type=jnp.float32)
        for half in range(2):
            part = y[:, half * width : (half + 1) * width]
            o_ref[0, r + half] = (res_ref[0, r + half].astype(jnp.float32) + part + bias).astype(
                o_ref.dtype
            )
        return carry

    lax.fori_loop(0, rows // 2, two_rows, 0)


def frame_spec(tap, rows, chans, width):
    return pl.BlockSpec((1, rows, chans, width), lambda f: (f + tap, 0, 0, 0))


def temporal_call(own, other, weight_own, weight_other, residual, bias):
    frames, rows, local_chan, width = residual.shape
    taps = [frame_spec(tap, rows, local_chan, width) for tap in range(3)]
    weight_spec = pl.BlockSpec((3, local_chan, local_chan), lambda f: (0, 0, 0))
    return pl.pallas_call(
        temporal_kernel,
        out_shape=jax.ShapeDtypeStruct(residual.shape, jnp.bfloat16),
        grid=(frames,),
        in_specs=taps
        + taps
        + [
            weight_spec,
            weight_spec,
            pl.BlockSpec((1, rows, local_chan, width), lambda f: (f, 0, 0, 0)),
            pl.BlockSpec((local_chan, 1), lambda f: (0, 0)),
        ],
        out_specs=pl.BlockSpec((1, rows, local_chan, width), lambda f: (f, 0, 0, 0)),
        compiler_params=pltpu.CompilerParams(vmem_limit_bytes=48 * 1024 * 1024),
        cost_estimate=pl.CostEstimate(
            flops=2 * frames * rows * width * 6 * local_chan * local_chan,
            transcendentals=0,
            bytes_accessed=12 * residual.size + 4 * weight_own.size + 4 * residual.size,
        ),
    )(own, own, own, other, other, other, weight_own, weight_other, residual, bias)


def spatial_taps(running, channel_slab, weight, rows, width):
    for row_tap in range(3):
        for col_tap in range(3):
            window = channel_slab[:, row_tap : row_tap + rows, :, col_tap : col_tap + width]
            running = running + jnp.einsum(
                "frcw,co->frow", window, weight[row_tap, col_tap], preferred_element_type=jnp.float32
            )
    return running


def temporal_taps(running, channel_slab, weight, frames):
    for frame_tap in range(3):
        window = channel_slab[frame_tap : frame_tap + frames]
        running = running + jnp.einsum(
            "frcw,co->frow", window, weight[frame_tap], preferred_element_type=jnp.float32
        )
    return running


def body(
    video,
    norm1_gain,
    norm1_bias,
    spatial_weight,
    spatial_bias,
    norm2_gain,
    norm2_bias,
    temporal_weight,
    temporal_bias,
):
    frames, rows, local_chan, width = video.shape
    group_size = C // GROUPS
    local_groups = local_chan // group_size
    chan_index = lax.axis_index("chan")
    tm_index = lax.axis_index("tm")
    tm_count = lax.axis_size("tm")

    piece = spatial_weight.shape[2]
    merged = jnp.concatenate([spatial_weight.reshape(9, piece, local_chan), temporal_weight], axis=0)
    sharers = lax.axis_size("groups") * lax.axis_size("height")
    share = local_chan // sharers
    slot = lax.axis_index("groups") * lax.axis_size("height") + lax.axis_index("height")
    mine = lax.dynamic_slice_in_dim(merged, slot * share, share, axis=2)
    along_tm = gather_tm(mine)
    shared = [along_tm]
    for shift in range(1, sharers):
        pairs = [(i, (i - shift) % sharers) for i in range(sharers)]
        shared.append(lax.ppermute(along_tm, ("groups", "height"), pairs))
    shared = jnp.roll(jnp.stack(shared), slot, axis=0)

    values = video.astype(jnp.float32)
    grouped = values.reshape(frames, rows, local_groups, group_size, width)
    average, variance = group_stats(grouped, (1, 3, 4), ("height",))
    act_one = group_act(values, average, variance, norm1_gain, norm1_bias)
    act_one, shared = lax.optimization_barrier((act_one, shared))
    full_weight = jnp.transpose(shared, (2, 1, 3, 0, 4)).reshape(12, C, local_chan)
    spatial_full = full_weight[:9].reshape(3, 3, C, local_chan)
    temporal_full = full_weight[9:]

    with_rows = row_halo(act_one)
    own_start = chan_index * local_chan
    other_start = (1 - chan_index) * local_chan
    spatial_rows = jnp.transpose(spatial_full, (0, 1, 3, 2)).reshape(3, 3 * local_chan, C)
    hidden = spatial_call(
        with_rows,
        swap_chan(with_rows),
        lax.dynamic_slice_in_dim(spatial_rows, own_start, local_chan, axis=2),
        lax.dynamic_slice_in_dim(spatial_rows, other_start, local_chan, axis=2),
        video,
        spatial_bias[:, None],
    )

    forward = [(i, i + 1) for i in range(tm_count - 1)]
    backward = [(target, source) for source, target in forward]
    before = lax.ppermute(hidden[-1:], "tm", forward)
    after = lax.ppermute(hidden[:1], "tm", backward)

    hidden_values = hidden.astype(jnp.float32)
    grouped_two = hidden_values.reshape(frames, rows, local_groups, group_size, width)
    average_two, variance_two = group_stats(grouped_two, (0, 1, 3, 4), ("tm", "height"))

    extended = jnp.concatenate([before, hidden, after], axis=0).astype(jnp.float32)
    act_two = group_act(extended, average_two, variance_two, norm2_gain, norm2_bias)
    frame_ids = jnp.arange(frames + 2)
    inside = (frame_ids > 0) | (tm_index > 0)
    inside = inside & ((frame_ids < frames + 1) | (tm_index < tm_count - 1))
    act_two = jnp.where(inside[:, None, None, None], act_two, jnp.zeros_like(act_two))

    temporal_rows = jnp.transpose(temporal_full, (0, 2, 1))
    return temporal_call(
        act_two,
        swap_chan(act_two),
        lax.dynamic_slice_in_dim(temporal_rows, own_start, local_chan, axis=2),
        lax.dynamic_slice_in_dim(temporal_rows, other_start, local_chan, axis=2),
        hidden,
        temporal_bias[:, None],
    )


def solution(mesh):
    return jax.shard_map(
        body,
        mesh=mesh,
        in_specs=(
            P(("groups", "tm"), "height", "chan", None),
            P("chan"),
            P("chan"),
            P(None, None, "tm", "chan"),
            P("chan"),
            P("chan"),
            P("chan"),
            P(None, "tm", "chan"),
            P("chan"),
        ),
        out_specs=P(("groups", "tm"), "height", "chan", None),
        check_vma=False,
    )
```

```python
import jax
import jax.numpy as jnp
from jax import lax
from jax.experimental import pallas as pl
from jax.experimental.pallas import tpu as pltpu
from jax.sharding import PartitionSpec as P

C = 320
GROUPS = 32


EPSILON = 1e-06


def swap_chan(block):
    return lax.ppermute(block, "chan", [(0, 1), (1, 0)])


def row_halo(block):
    count = lax.axis_size("height")
    forward = [(i, i + 1) for i in range(count - 1)]
    backward = [(target, source) for source, target in forward]
    low = lax.ppermute(block[:, -1:], "height", forward)
    high = lax.ppermute(block[:, :1], "height", backward)
    return jnp.concatenate([low, block, high], axis=1)


def gather_tm(piece):
    count = lax.axis_size("tm")
    index = lax.axis_index("tm")
    pieces = [piece]
    for shift in range(1, count):
        pairs = [(i, (i - shift) % count) for i in range(count)]
        pieces.append(lax.ppermute(piece, "tm", pairs))
    stacked = jnp.roll(jnp.stack(pieces), index, axis=0)
    return stacked


def group_stats(grouped, axes, slot_axes):
    count = 1
    for axis in axes:
        count *= grouped.shape[axis]
    local_mean = jnp.sum(grouped, axis=axes) / count
    centred = grouped - jnp.expand_dims(local_mean, axes)
    local_m2 = jnp.sum(centred * centred, axis=axes)
    slots = 1
    for name in slot_axes:
        slots *= lax.axis_size(name)
    slot = 0
    for name in slot_axes:
        slot = slot * lax.axis_size(name) + lax.axis_index(name)
    mine = jnp.stack([local_mean, local_m2])
    table = jnp.zeros((slots,) + mine.shape, jnp.float32)
    table = lax.dynamic_update_index_in_dim(table, mine, slot, 0)
    for name in reversed(slot_axes):
        table = lax.psum(table, name)
    means = table[:, 0]
    average = jnp.sum(means, axis=0) / slots
    spread = means - average
    m2 = jnp.sum(table[:, 1], axis=0) + count * jnp.sum(spread * spread, axis=0)
    variance = m2 / (count * slots)
    return average, variance


def group_act(values, average, variance, gain, bias):
    frames, rows, local_chan, width = values.shape
    local_groups = average.shape[-1]
    grouped = values.reshape(frames, rows, local_groups, local_chan // local_groups, width)
    centred = grouped - average.reshape(-1, 1, local_groups, 1, 1)
    scaled = (centred * lax.rsqrt(variance.reshape(-1, 1, local_groups, 1, 1) + EPSILON)).reshape(
        frames, rows, local_chan, width
    )
    return jax.nn.silu(scaled * gain[:, None] + bias[:, None]).astype(jnp.bfloat16)


def in_order(own, other, chan_index):
    size = own.shape[2]
    joined = jnp.zeros(own.shape[:2] + (2 * size,) + own.shape[3:], own.dtype)
    joined = lax.dynamic_update_slice_in_dim(joined, own, chan_index * size, axis=2)
    return lax.dynamic_update_slice_in_dim(joined, other, (1 - chan_index) * size, axis=2)


def pair(ref, first):
    return jnp.concatenate([ref[0, first], ref[0, first + 1]], axis=1)


def spatial_kernel(xo_ref, xt_ref, wo_ref, wt_ref, res_ref, b_ref, o_ref):
    rows, local_chan, width = o_ref.shape[1], o_ref.shape[2], o_ref.shape[3]
    lane = lax.broadcasted_iota(jnp.int32, (local_chan, width), 1)
    bias = b_ref[...]

    def two_rows(i, carry):
        r = 2 * i
        y = jnp.dot(wo_ref[0], pair(xo_ref, r), preferred_element_type=jnp.float32)
        y = y + jnp.dot(wt_ref[0], pair(xt_ref, r), preferred_element_type=jnp.float32)
        for tap in (1, 2):
            y = y + jnp.dot(wo_ref[tap], pair(xo_ref, r + tap), preferred_element_type=jnp.float32)
            y = y + jnp.dot(wt_ref[tap], pair(xt_ref, r + tap), preferred_element_type=jnp.float32)
        for half in range(2):
            part = y[:, half * width : (half + 1) * width]
            left = pltpu.roll(part[:local_chan], 1, 1)
            left = jnp.where(lane == 0, 0.0, left)
            right = pltpu.roll(part[2 * local_chan :], width - 1, 1)
            right = jnp.where(lane == width - 1, 0.0, right)
            total = left + part[local_chan : 2 * local_chan] + right
            o_ref[0, r + half] = (res_ref[0, r + half].astype(jnp.float32) + total + bias).astype(
                o_ref.dtype
            )
        return carry

    lax.fori_loop(0, rows // 2, two_rows, 0)


def spatial_call(own, other, weight_own, weight_other, residual, bias):
    frames, rows, local_chan, width = residual.shape
    act_spec = pl.BlockSpec((1, rows + 2, local_chan, width), lambda f: (f, 0, 0, 0))
    weight_spec = pl.BlockSpec((3, 3 * local_chan, local_chan), lambda f: (0, 0, 0))
    return pl.pallas_call(
        spatial_kernel,
        out_shape=jax.ShapeDtypeStruct(residual.shape, jnp.bfloat16),
        grid=(frames,),
        in_specs=[
            act_spec,
            act_spec,
            weight_spec,
            weight_spec,
            pl.BlockSpec((1, rows, local_chan, width), lambda f: (f, 0, 0, 0)),
            pl.BlockSpec((local_chan, 1), lambda f: (0, 0)),
        ],
        out_specs=pl.BlockSpec((1, rows, local_chan, width), lambda f: (f, 0, 0, 0)),
        compiler_params=pltpu.CompilerParams(vmem_limit_bytes=48 * 1024 * 1024),
        cost_estimate=pl.CostEstimate(
            flops=2 * frames * rows * width * 18 * local_chan * local_chan,
            transcendentals=0,
            bytes_accessed=4 * own.size + 4 * weight_own.size + 4 * residual.size,
        ),
    )(own, other, weight_own, weight_other, residual, bias)


def temporal_kernel(*refs):
    own_refs, other_refs = refs[0:3], refs[3:6]
    wo_ref, wt_ref, res_ref, bias_ref, o_ref = refs[6:]
    rows, width = o_ref.shape[1], o_ref.shape[3]
    bias = bias_ref[...]

    def two_rows(i, carry):
        r = 2 * i
        y = jnp.dot(wo_ref[0], pair(own_refs[0], r), preferred_element_type=jnp.float32)
        y = y + jnp.dot(wt_ref[0], pair(other_refs[0], r), preferred_element_type=jnp.float32)
        for tap in (1, 2):
            y = y + jnp.dot(wo_ref[tap], pair(own_refs[tap], r), preferred_element_type=jnp.float32)
            y = y + jnp.dot(wt_ref[tap], pair(other_refs[tap], r), preferred_element_type=jnp.float32)
        for half in range(2):
            part = y[:, half * width : (half + 1) * width]
            o_ref[0, r + half] = (res_ref[0, r + half].astype(jnp.float32) + part + bias).astype(
                o_ref.dtype
            )
        return carry

    lax.fori_loop(0, rows // 2, two_rows, 0)


def frame_spec(tap, rows, chans, width):
    return pl.BlockSpec((1, rows, chans, width), lambda f: (f + tap, 0, 0, 0))


def temporal_call(own, other, weight_own, weight_other, residual, bias):
    frames, rows, local_chan, width = residual.shape
    taps = [frame_spec(tap, rows, local_chan, width) for tap in range(3)]
    weight_spec = pl.BlockSpec((3, local_chan, local_chan), lambda f: (0, 0, 0))
    return pl.pallas_call(
        temporal_kernel,
        out_shape=jax.ShapeDtypeStruct(residual.shape, jnp.bfloat16),
        grid=(frames,),
        in_specs=taps
        + taps
        + [
            weight_spec,
            weight_spec,
            pl.BlockSpec((1, rows, local_chan, width), lambda f: (f, 0, 0, 0)),
            pl.BlockSpec((local_chan, 1), lambda f: (0, 0)),
        ],
        out_specs=pl.BlockSpec((1, rows, local_chan, width), lambda f: (f, 0, 0, 0)),
        compiler_params=pltpu.CompilerParams(vmem_limit_bytes=48 * 1024 * 1024),
        cost_estimate=pl.CostEstimate(
            flops=2 * frames * rows * width * 6 * local_chan * local_chan,
            transcendentals=0,
            bytes_accessed=12 * residual.size + 4 * weight_own.size + 4 * residual.size,
        ),
    )(own, own, own, other, other, other, weight_own, weight_other, residual, bias)


def spatial_taps(running, channel_slab, weight, rows, width):
    for row_tap in range(3):
        for col_tap in range(3):
            window = channel_slab[:, row_tap : row_tap + rows, :, col_tap : col_tap + width]
            running = running + jnp.einsum(
                "frcw,co->frow", window, weight[row_tap, col_tap], preferred_element_type=jnp.float32
            )
    return running


def temporal_taps(running, channel_slab, weight, frames):
    for frame_tap in range(3):
        window = channel_slab[frame_tap : frame_tap + frames]
        running = running + jnp.einsum(
            "frcw,co->frow", window, weight[frame_tap], preferred_element_type=jnp.float32
        )
    return running


def body(
    video,
    norm1_gain,
    norm1_bias,
    spatial_weight,
    spatial_bias,
    norm2_gain,
    norm2_bias,
    temporal_weight,
    temporal_bias,
):
    frames, rows, local_chan, width = video.shape
    group_size = C // GROUPS
    local_groups = local_chan // group_size
    chan_index = lax.axis_index("chan")
    tm_index = lax.axis_index("tm")
    tm_count = lax.axis_size("tm")

    piece = spatial_weight.shape[2]
    merged = jnp.concatenate([spatial_weight.reshape(9, piece, local_chan), temporal_weight], axis=0)
    sharers = lax.axis_size("groups") * lax.axis_size("height")
    share = local_chan // sharers
    slot = lax.axis_index("groups") * lax.axis_size("height") + lax.axis_index("height")
    mine = lax.dynamic_slice_in_dim(merged, slot * share, share, axis=2)
    along_tm = gather_tm(mine)
    shared = [along_tm]
    for shift in range(1, sharers):
        pairs = [(i, (i - shift) % sharers) for i in range(sharers)]
        shared.append(lax.ppermute(along_tm, ("groups", "height"), pairs))
    shared = jnp.roll(jnp.stack(shared), slot, axis=0)

    values = video.astype(jnp.float32)
    grouped = values.reshape(frames, rows, local_groups, group_size, width)
    average, variance = group_stats(grouped, (1, 3, 4), ("height",))
    act_one = group_act(values, average, variance, norm1_gain, norm1_bias)

    with_rows = row_halo(act_one)
    with_rows, shared = lax.optimization_barrier((with_rows, shared))
    full_weight = jnp.transpose(shared, (2, 1, 3, 0, 4)).reshape(12, C, local_chan)
    spatial_full = full_weight[:9].reshape(3, 3, C, local_chan)
    temporal_full = full_weight[9:]
    own_start = chan_index * local_chan
    other_start = (1 - chan_index) * local_chan
    spatial_rows = jnp.transpose(spatial_full, (0, 1, 3, 2)).reshape(3, 3 * local_chan, C)
    hidden = spatial_call(
        with_rows,
        swap_chan(with_rows),
        lax.dynamic_slice_in_dim(spatial_rows, own_start, local_chan, axis=2),
        lax.dynamic_slice_in_dim(spatial_rows, other_start, local_chan, axis=2),
        video,
        spatial_bias[:, None],
    )

    forward = [(i, i + 1) for i in range(tm_count - 1)]
    backward = [(target, source) for source, target in forward]
    before = lax.ppermute(hidden[-1:], "tm", forward)
    after = lax.ppermute(hidden[:1], "tm", backward)

    hidden_values = hidden.astype(jnp.float32)
    grouped_two = hidden_values.reshape(frames, rows, local_groups, group_size, width)
    average_two, variance_two = group_stats(grouped_two, (0, 1, 3, 4), ("tm", "height"))

    extended = jnp.concatenate([before, hidden, after], axis=0).astype(jnp.float32)
    act_two = group_act(extended, average_two, variance_two, norm2_gain, norm2_bias)
    frame_ids = jnp.arange(frames + 2)
    inside = (frame_ids > 0) | (tm_index > 0)
    inside = inside & ((frame_ids < frames + 1) | (tm_index < tm_count - 1))
    act_two = jnp.where(inside[:, None, None, None], act_two, jnp.zeros_like(act_two))

    temporal_rows = jnp.transpose(temporal_full, (0, 2, 1))
    return temporal_call(
        act_two,
        swap_chan(act_two),
        lax.dynamic_slice_in_dim(temporal_rows, own_start, local_chan, axis=2),
        lax.dynamic_slice_in_dim(temporal_rows, other_start, local_chan, axis=2),
        hidden,
        temporal_bias[:, None],
    )


def solution(mesh):
    return jax.shard_map(
        body,
        mesh=mesh,
        in_specs=(
            P(("groups", "tm"), "height", "chan", None),
            P("chan"),
            P("chan"),
            P(None, None, "tm", "chan"),
            P("chan"),
            P("chan"),
            P("chan"),
            P(None, "tm", "chan"),
            P("chan"),
        ),
        out_specs=P(("groups", "tm"), "height", "chan", None),
        check_vma=False,
    )
```

```python
import jax
import jax.numpy as jnp
from jax import lax
from jax.experimental import pallas as pl
from jax.experimental.pallas import tpu as pltpu
from jax.sharding import PartitionSpec as P

C = 320
GROUPS = 32


EPSILON = 1e-06


def swap_chan(block):
    return lax.ppermute(block, "chan", [(0, 1), (1, 0)])


def row_halo(block):
    count = lax.axis_size("height")
    forward = [(i, i + 1) for i in range(count - 1)]
    backward = [(target, source) for source, target in forward]
    low = lax.ppermute(block[:, -1:], "height", forward)
    high = lax.ppermute(block[:, :1], "height", backward)
    return jnp.concatenate([low, block, high], axis=1)


def gather_tm(piece):
    count = lax.axis_size("tm")
    index = lax.axis_index("tm")
    pieces = [piece]
    for shift in range(1, count):
        pairs = [(i, (i - shift) % count) for i in range(count)]
        pieces.append(lax.ppermute(piece, "tm", pairs))
    stacked = jnp.roll(jnp.stack(pieces), index, axis=0)
    return stacked


def group_stats(grouped, axes, slot_axes):
    count = 1
    for axis in axes:
        count *= grouped.shape[axis]
    local_mean = jnp.sum(grouped, axis=axes) / count
    centred = grouped - jnp.expand_dims(local_mean, axes)
    local_m2 = jnp.sum(centred * centred, axis=axes)
    slots = 1
    for name in slot_axes:
        slots *= lax.axis_size(name)
    slot = 0
    for name in slot_axes:
        slot = slot * lax.axis_size(name) + lax.axis_index(name)
    mine = jnp.stack([local_mean, local_m2])
    table = jnp.zeros((slots,) + mine.shape, jnp.float32)
    table = lax.dynamic_update_index_in_dim(table, mine, slot, 0)
    for name in reversed(slot_axes):
        table = lax.psum(table, name)
    means = table[:, 0]
    average = jnp.sum(means, axis=0) / slots
    spread = means - average
    m2 = jnp.sum(table[:, 1], axis=0) + count * jnp.sum(spread * spread, axis=0)
    variance = m2 / (count * slots)
    return average, variance


def group_act(values, average, variance, gain, bias):
    frames, rows, local_chan, width = values.shape
    local_groups = average.shape[-1]
    grouped = values.reshape(frames, rows, local_groups, local_chan // local_groups, width)
    centred = grouped - average.reshape(-1, 1, local_groups, 1, 1)
    scaled = (centred * lax.rsqrt(variance.reshape(-1, 1, local_groups, 1, 1) + EPSILON)).reshape(
        frames, rows, local_chan, width
    )
    return jax.nn.silu(scaled * gain[:, None] + bias[:, None]).astype(jnp.bfloat16)


def in_order(own, other, chan_index):
    size = own.shape[2]
    joined = jnp.zeros(own.shape[:2] + (2 * size,) + own.shape[3:], own.dtype)
    joined = lax.dynamic_update_slice_in_dim(joined, own, chan_index * size, axis=2)
    return lax.dynamic_update_slice_in_dim(joined, other, (1 - chan_index) * size, axis=2)


STEP = 4


def pair(ref, first):
    return jnp.concatenate([ref[0, first + k] for k in range(STEP)], axis=1)


def spatial_kernel(xo_ref, xt_ref, wo_ref, wt_ref, res_ref, b_ref, early_ref, o_ref):
    rows, local_chan, width = o_ref.shape[1], o_ref.shape[2], o_ref.shape[3]
    lane = lax.broadcasted_iota(jnp.int32, (local_chan, width), 1)
    bias = b_ref[...]

    def two_rows(i, carry):
        r = STEP * i
        y = jnp.dot(wo_ref[0], pair(xo_ref, r), preferred_element_type=jnp.float32)
        y = y + jnp.dot(wt_ref[0], pair(xt_ref, r), preferred_element_type=jnp.float32)
        for tap in (1, 2):
            y = y + jnp.dot(wo_ref[tap], pair(xo_ref, r + tap), preferred_element_type=jnp.float32)
            y = y + jnp.dot(wt_ref[tap], pair(xt_ref, r + tap), preferred_element_type=jnp.float32)
        for half in range(STEP):
            part = y[:, half * width : (half + 1) * width]
            left = pltpu.roll(part[:local_chan], 1, 1)
            left = jnp.where(lane == 0, 0.0, left)
            right = pltpu.roll(part[2 * local_chan :], width - 1, 1)
            right = jnp.where(lane == width - 1, 0.0, right)
            total = left + part[local_chan : 2 * local_chan] + right
            o_ref[0, r + half] = (res_ref[0, r + half].astype(jnp.float32) + total + bias).astype(
                o_ref.dtype
            )
        return carry

    lax.fori_loop(0, rows // STEP, two_rows, 0)


def spatial_call(own, other, weight_own, weight_other, residual, bias, early):
    frames, rows, local_chan, width = residual.shape
    act_spec = pl.BlockSpec((1, rows + 2, local_chan, width), lambda f: (f, 0, 0, 0))
    weight_spec = pl.BlockSpec((3, 3 * local_chan, local_chan), lambda f: (0, 0, 0))
    return pl.pallas_call(
        spatial_kernel,
        out_shape=jax.ShapeDtypeStruct(residual.shape, jnp.bfloat16),
        grid=(frames,),
        in_specs=[
            act_spec,
            act_spec,
            weight_spec,
            weight_spec,
            pl.BlockSpec((1, rows, local_chan, width), lambda f: (f, 0, 0, 0)),
            pl.BlockSpec((local_chan, 1), lambda f: (0, 0)),
            pl.BlockSpec(memory_space=pl.ANY),
        ],
        out_specs=pl.BlockSpec((1, rows, local_chan, width), lambda f: (f, 0, 0, 0)),
        compiler_params=pltpu.CompilerParams(vmem_limit_bytes=48 * 1024 * 1024),
        cost_estimate=pl.CostEstimate(
            flops=2 * frames * rows * width * 18 * local_chan * local_chan,
            transcendentals=0,
            bytes_accessed=4 * own.size + 4 * weight_own.size + 4 * residual.size,
        ),
    )(own, other, weight_own, weight_other, residual, bias, early)


def temporal_kernel(*refs):
    own_refs, other_refs = refs[0:3], refs[3:6]
    wo_ref, wt_ref, res_ref, bias_ref, o_ref = refs[6:]
    rows, width = o_ref.shape[1], o_ref.shape[3]
    bias = bias_ref[...]

    def two_rows(i, carry):
        r = STEP * i
        y = jnp.dot(wo_ref[0], pair(own_refs[0], r), preferred_element_type=jnp.float32)
        y = y + jnp.dot(wt_ref[0], pair(other_refs[0], r), preferred_element_type=jnp.float32)
        for tap in (1, 2):
            y = y + jnp.dot(wo_ref[tap], pair(own_refs[tap], r), preferred_element_type=jnp.float32)
            y = y + jnp.dot(wt_ref[tap], pair(other_refs[tap], r), preferred_element_type=jnp.float32)
        for half in range(STEP):
            part = y[:, half * width : (half + 1) * width]
            o_ref[0, r + half] = (res_ref[0, r + half].astype(jnp.float32) + part + bias).astype(
                o_ref.dtype
            )
        return carry

    lax.fori_loop(0, rows // STEP, two_rows, 0)


def frame_spec(tap, rows, chans, width):
    return pl.BlockSpec((1, rows, chans, width), lambda f: (f + tap, 0, 0, 0))


def temporal_call(own, other, weight_own, weight_other, residual, bias):
    frames, rows, local_chan, width = residual.shape
    taps = [frame_spec(tap, rows, local_chan, width) for tap in range(3)]
    weight_spec = pl.BlockSpec((3, local_chan, local_chan), lambda f: (0, 0, 0))
    return pl.pallas_call(
        temporal_kernel,
        out_shape=jax.ShapeDtypeStruct(residual.shape, jnp.bfloat16),
        grid=(frames,),
        in_specs=taps
        + taps
        + [
            weight_spec,
            weight_spec,
            pl.BlockSpec((1, rows, local_chan, width), lambda f: (f, 0, 0, 0)),
            pl.BlockSpec((local_chan, 1), lambda f: (0, 0)),
        ],
        out_specs=pl.BlockSpec((1, rows, local_chan, width), lambda f: (f, 0, 0, 0)),
        compiler_params=pltpu.CompilerParams(vmem_limit_bytes=48 * 1024 * 1024),
        cost_estimate=pl.CostEstimate(
            flops=2 * frames * rows * width * 6 * local_chan * local_chan,
            transcendentals=0,
            bytes_accessed=12 * residual.size + 4 * weight_own.size + 4 * residual.size,
        ),
    )(own, own, own, other, other, other, weight_own, weight_other, residual, bias)


def spatial_taps(running, channel_slab, weight, rows, width):
    for row_tap in range(3):
        for col_tap in range(3):
            window = channel_slab[:, row_tap : row_tap + rows, :, col_tap : col_tap + width]
            running = running + jnp.einsum(
                "frcw,co->frow", window, weight[row_tap, col_tap], preferred_element_type=jnp.float32
            )
    return running


def temporal_taps(running, channel_slab, weight, frames):
    for frame_tap in range(3):
        window = channel_slab[frame_tap : frame_tap + frames]
        running = running + jnp.einsum(
            "frcw,co->frow", window, weight[frame_tap], preferred_element_type=jnp.float32
        )
    return running


def body(
    video,
    norm1_gain,
    norm1_bias,
    spatial_weight,
    spatial_bias,
    norm2_gain,
    norm2_bias,
    temporal_weight,
    temporal_bias,
):
    frames, rows, local_chan, width = video.shape
    group_size = C // GROUPS
    local_groups = local_chan // group_size
    chan_index = lax.axis_index("chan")
    tm_index = lax.axis_index("tm")
    tm_count = lax.axis_size("tm")

    spatial_full = lax.all_gather(spatial_weight, "tm", axis=2, tiled=True).reshape(9, C, local_chan)
    temporal_pieces = gather_tm(temporal_weight)
    temporal_full = jnp.moveaxis(temporal_pieces, 0, 1).reshape(3, C, local_chan)
    spatial_full = spatial_full.reshape(3, 3, C, local_chan)

    values = video.astype(jnp.float32)
    grouped = values.reshape(frames, rows, local_groups, group_size, width)
    average, variance = group_stats(grouped, (1, 3, 4), ("height",))
    act_one = group_act(values, average, variance, norm1_gain, norm1_bias)

    with_rows = row_halo(act_one)
    own_start = chan_index * local_chan
    other_start = (1 - chan_index) * local_chan
    spatial_rows = jnp.transpose(spatial_full, (0, 1, 3, 2)).reshape(3, 3 * local_chan, C)
    hidden = spatial_call(
        with_rows,
        swap_chan(with_rows),
        lax.dynamic_slice_in_dim(spatial_rows, own_start, local_chan, axis=2),
        lax.dynamic_slice_in_dim(spatial_rows, other_start, local_chan, axis=2),
        video,
        spatial_bias[:, None],
        temporal_pieces,
    )

    forward = [(i, i + 1) for i in range(tm_count - 1)]
    backward = [(target, source) for source, target in forward]
    before = lax.ppermute(hidden[-1:], "tm", forward)
    after = lax.ppermute(hidden[:1], "tm", backward)

    hidden_values = hidden.astype(jnp.float32)
    grouped_two = hidden_values.reshape(frames, rows, local_groups, group_size, width)
    average_two, variance_two = group_stats(grouped_two, (0, 1, 3, 4), ("tm", "height"))

    extended = jnp.concatenate([before, hidden, after], axis=0).astype(jnp.float32)
    act_two = group_act(extended, average_two, variance_two, norm2_gain, norm2_bias)
    frame_ids = jnp.arange(frames + 2)
    inside = (frame_ids > 0) | (tm_index > 0)
    inside = inside & ((frame_ids < frames + 1) | (tm_index < tm_count - 1))
    act_two = jnp.where(inside[:, None, None, None], act_two, jnp.zeros_like(act_two))

    temporal_rows = jnp.transpose(temporal_full, (0, 2, 1))
    return temporal_call(
        act_two,
        swap_chan(act_two),
        lax.dynamic_slice_in_dim(temporal_rows, own_start, local_chan, axis=2),
        lax.dynamic_slice_in_dim(temporal_rows, other_start, local_chan, axis=2),
        hidden,
        temporal_bias[:, None],
    )


def solution(mesh):
    return jax.shard_map(
        body,
        mesh=mesh,
        in_specs=(
            P(("groups", "tm"), "height", "chan", None),
            P("chan"),
            P("chan"),
            P(None, None, "tm", "chan"),
            P("chan"),
            P("chan"),
            P("chan"),
            P(None, "tm", "chan"),
            P("chan"),
        ),
        out_specs=P(("groups", "tm"), "height", "chan", None),
        check_vma=False,
    )
```

```python
import jax
import jax.numpy as jnp
from jax import lax
from jax.experimental import pallas as pl
from jax.experimental.pallas import tpu as pltpu
from jax.sharding import PartitionSpec as P

C = 320
GROUPS = 32


EPSILON = 1e-06


def swap_chan(block):
    return lax.ppermute(block, "chan", [(0, 1), (1, 0)])


def row_halo(block):
    count = lax.axis_size("height")
    forward = [(i, i + 1) for i in range(count - 1)]
    backward = [(target, source) for source, target in forward]
    low = lax.ppermute(block[:, -1:], "height", forward)
    high = lax.ppermute(block[:, :1], "height", backward)
    return jnp.concatenate([low, block, high], axis=1)


def gather_tm(piece):
    count = lax.axis_size("tm")
    index = lax.axis_index("tm")
    pieces = [piece]
    for shift in range(1, count):
        pairs = [(i, (i - shift) % count) for i in range(count)]
        pieces.append(lax.ppermute(piece, "tm", pairs))
    stacked = jnp.roll(jnp.stack(pieces), index, axis=0)
    return stacked


def group_stats(grouped, axes, slot_axes):
    count = 1
    for axis in axes:
        count *= grouped.shape[axis]
    local_mean = jnp.sum(grouped, axis=axes) / count
    centred = grouped - jnp.expand_dims(local_mean, axes)
    local_m2 = jnp.sum(centred * centred, axis=axes)
    slots = 1
    for name in slot_axes:
        slots *= lax.axis_size(name)
    slot = 0
    for name in slot_axes:
        slot = slot * lax.axis_size(name) + lax.axis_index(name)
    mine = jnp.stack([local_mean, local_m2])
    table = jnp.zeros((slots,) + mine.shape, jnp.float32)
    table = lax.dynamic_update_index_in_dim(table, mine, slot, 0)
    for name in reversed(slot_axes):
        table = lax.psum(table, name)
    means = table[:, 0]
    average = jnp.sum(means, axis=0) / slots
    spread = means - average
    m2 = jnp.sum(table[:, 1], axis=0) + count * jnp.sum(spread * spread, axis=0)
    variance = m2 / (count * slots)
    return average, variance


def group_act(values, average, variance, gain, bias):
    frames, rows, local_chan, width = values.shape
    local_groups = average.shape[-1]
    grouped = values.reshape(frames, rows, local_groups, local_chan // local_groups, width)
    centred = grouped - average.reshape(-1, 1, local_groups, 1, 1)
    scaled = (centred * lax.rsqrt(variance.reshape(-1, 1, local_groups, 1, 1) + EPSILON)).reshape(
        frames, rows, local_chan, width
    )
    return jax.nn.silu(scaled * gain[:, None] + bias[:, None]).astype(jnp.bfloat16)


def in_order(own, other, chan_index):
    size = own.shape[2]
    joined = jnp.zeros(own.shape[:2] + (2 * size,) + own.shape[3:], own.dtype)
    joined = lax.dynamic_update_slice_in_dim(joined, own, chan_index * size, axis=2)
    return lax.dynamic_update_slice_in_dim(joined, other, (1 - chan_index) * size, axis=2)


STEP = 6


def pair(ref, first):
    return jnp.concatenate([ref[0, first + k] for k in range(STEP)], axis=1)


def spatial_kernel(xo_ref, xt_ref, wo_ref, wt_ref, res_ref, b_ref, early_ref, o_ref):
    rows, local_chan, width = o_ref.shape[1], o_ref.shape[2], o_ref.shape[3]
    lane = lax.broadcasted_iota(jnp.int32, (local_chan, width), 1)
    bias = b_ref[...]

    def two_rows(i, carry):
        r = STEP * i
        y = jnp.dot(wo_ref[0], pair(xo_ref, r), preferred_element_type=jnp.float32)
        y = y + jnp.dot(wt_ref[0], pair(xt_ref, r), preferred_element_type=jnp.float32)
        for tap in (1, 2):
            y = y + jnp.dot(wo_ref[tap], pair(xo_ref, r + tap), preferred_element_type=jnp.float32)
            y = y + jnp.dot(wt_ref[tap], pair(xt_ref, r + tap), preferred_element_type=jnp.float32)
        for half in range(STEP):
            part = y[:, half * width : (half + 1) * width]
            left = pltpu.roll(part[:local_chan], 1, 1)
            left = jnp.where(lane == 0, 0.0, left)
            right = pltpu.roll(part[2 * local_chan :], width - 1, 1)
            right = jnp.where(lane == width - 1, 0.0, right)
            total = left + part[local_chan : 2 * local_chan] + right
            o_ref[0, r + half] = (res_ref[0, r + half].astype(jnp.float32) + total + bias).astype(
                o_ref.dtype
            )
        return carry

    lax.fori_loop(0, rows // STEP, two_rows, 0)


def spatial_call(own, other, weight_own, weight_other, residual, bias, early):
    frames, rows, local_chan, width = residual.shape
    act_spec = pl.BlockSpec((1, rows + 2, local_chan, width), lambda f: (f, 0, 0, 0))
    weight_spec = pl.BlockSpec((3, 3 * local_chan, local_chan), lambda f: (0, 0, 0))
    return pl.pallas_call(
        spatial_kernel,
        out_shape=jax.ShapeDtypeStruct(residual.shape, jnp.bfloat16),
        grid=(frames,),
        in_specs=[
            act_spec,
            act_spec,
            weight_spec,
            weight_spec,
            pl.BlockSpec((1, rows, local_chan, width), lambda f: (f, 0, 0, 0)),
            pl.BlockSpec((local_chan, 1), lambda f: (0, 0)),
            pl.BlockSpec(memory_space=pl.ANY),
        ],
        out_specs=pl.BlockSpec((1, rows, local_chan, width), lambda f: (f, 0, 0, 0)),
        compiler_params=pltpu.CompilerParams(vmem_limit_bytes=48 * 1024 * 1024),
        cost_estimate=pl.CostEstimate(
            flops=2 * frames * rows * width * 18 * local_chan * local_chan,
            transcendentals=0,
            bytes_accessed=4 * own.size + 4 * weight_own.size + 4 * residual.size,
        ),
    )(own, other, weight_own, weight_other, residual, bias, early)


def temporal_kernel(*refs):
    own_refs, other_refs = refs[0:3], refs[3:6]
    wo_ref, wt_ref, res_ref, bias_ref, o_ref = refs[6:]
    rows, width = o_ref.shape[1], o_ref.shape[3]
    bias = bias_ref[...]

    def two_rows(i, carry):
        r = STEP * i
        y = jnp.dot(wo_ref[0], pair(own_refs[0], r), preferred_element_type=jnp.float32)
        y = y + jnp.dot(wt_ref[0], pair(other_refs[0], r), preferred_element_type=jnp.float32)
        for tap in (1, 2):
            y = y + jnp.dot(wo_ref[tap], pair(own_refs[tap], r), preferred_element_type=jnp.float32)
            y = y + jnp.dot(wt_ref[tap], pair(other_refs[tap], r), preferred_element_type=jnp.float32)
        for half in range(STEP):
            part = y[:, half * width : (half + 1) * width]
            o_ref[0, r + half] = (res_ref[0, r + half].astype(jnp.float32) + part + bias).astype(
                o_ref.dtype
            )
        return carry

    lax.fori_loop(0, rows // STEP, two_rows, 0)


def frame_spec(tap, rows, chans, width):
    return pl.BlockSpec((1, rows, chans, width), lambda f: (f + tap, 0, 0, 0))


def temporal_call(own, other, weight_own, weight_other, residual, bias):
    frames, rows, local_chan, width = residual.shape
    taps = [frame_spec(tap, rows, local_chan, width) for tap in range(3)]
    weight_spec = pl.BlockSpec((3, local_chan, local_chan), lambda f: (0, 0, 0))
    return pl.pallas_call(
        temporal_kernel,
        out_shape=jax.ShapeDtypeStruct(residual.shape, jnp.bfloat16),
        grid=(frames,),
        in_specs=taps
        + taps
        + [
            weight_spec,
            weight_spec,
            pl.BlockSpec((1, rows, local_chan, width), lambda f: (f, 0, 0, 0)),
            pl.BlockSpec((local_chan, 1), lambda f: (0, 0)),
        ],
        out_specs=pl.BlockSpec((1, rows, local_chan, width), lambda f: (f, 0, 0, 0)),
        compiler_params=pltpu.CompilerParams(vmem_limit_bytes=48 * 1024 * 1024),
        cost_estimate=pl.CostEstimate(
            flops=2 * frames * rows * width * 6 * local_chan * local_chan,
            transcendentals=0,
            bytes_accessed=12 * residual.size + 4 * weight_own.size + 4 * residual.size,
        ),
    )(own, own, own, other, other, other, weight_own, weight_other, residual, bias)


def spatial_taps(running, channel_slab, weight, rows, width):
    for row_tap in range(3):
        for col_tap in range(3):
            window = channel_slab[:, row_tap : row_tap + rows, :, col_tap : col_tap + width]
            running = running + jnp.einsum(
                "frcw,co->frow", window, weight[row_tap, col_tap], preferred_element_type=jnp.float32
            )
    return running


def temporal_taps(running, channel_slab, weight, frames):
    for frame_tap in range(3):
        window = channel_slab[frame_tap : frame_tap + frames]
        running = running + jnp.einsum(
            "frcw,co->frow", window, weight[frame_tap], preferred_element_type=jnp.float32
        )
    return running


def body(
    video,
    norm1_gain,
    norm1_bias,
    spatial_weight,
    spatial_bias,
    norm2_gain,
    norm2_bias,
    temporal_weight,
    temporal_bias,
):
    frames, rows, local_chan, width = video.shape
    group_size = C // GROUPS
    local_groups = local_chan // group_size
    chan_index = lax.axis_index("chan")
    tm_index = lax.axis_index("tm")
    tm_count = lax.axis_size("tm")

    spatial_full = lax.all_gather(spatial_weight, "tm", axis=2, tiled=True).reshape(9, C, local_chan)
    temporal_pieces = gather_tm(temporal_weight)
    temporal_full = jnp.moveaxis(temporal_pieces, 0, 1).reshape(3, C, local_chan)
    spatial_full = spatial_full.reshape(3, 3, C, local_chan)

    values = video.astype(jnp.float32)
    grouped = values.reshape(frames, rows, local_groups, group_size, width)
    average, variance = group_stats(grouped, (1, 3, 4), ("height",))
    act_one = group_act(values, average, variance, norm1_gain, norm1_bias)

    with_rows = row_halo(act_one)
    own_start = chan_index * local_chan
    other_start = (1 - chan_index) * local_chan
    spatial_rows = jnp.transpose(spatial_full, (0, 1, 3, 2)).reshape(3, 3 * local_chan, C)
    hidden = spatial_call(
        with_rows,
        swap_chan(with_rows),
        lax.dynamic_slice_in_dim(spatial_rows, own_start, local_chan, axis=2),
        lax.dynamic_slice_in_dim(spatial_rows, other_start, local_chan, axis=2),
        video,
        spatial_bias[:, None],
        temporal_pieces,
    )

    forward = [(i, i + 1) for i in range(tm_count - 1)]
    backward = [(target, source) for source, target in forward]
    before = lax.ppermute(hidden[-1:], "tm", forward)
    after = lax.ppermute(hidden[:1], "tm", backward)

    hidden_values = hidden.astype(jnp.float32)
    grouped_two = hidden_values.reshape(frames, rows, local_groups, group_size, width)
    average_two, variance_two = group_stats(grouped_two, (0, 1, 3, 4), ("tm", "height"))

    extended = jnp.concatenate([before, hidden, after], axis=0).astype(jnp.float32)
    act_two = group_act(extended, average_two, variance_two, norm2_gain, norm2_bias)
    frame_ids = jnp.arange(frames + 2)
    inside = (frame_ids > 0) | (tm_index > 0)
    inside = inside & ((frame_ids < frames + 1) | (tm_index < tm_count - 1))
    act_two = jnp.where(inside[:, None, None, None], act_two, jnp.zeros_like(act_two))

    temporal_rows = jnp.transpose(temporal_full, (0, 2, 1))
    return temporal_call(
        act_two,
        swap_chan(act_two),
        lax.dynamic_slice_in_dim(temporal_rows, own_start, local_chan, axis=2),
        lax.dynamic_slice_in_dim(temporal_rows, other_start, local_chan, axis=2),
        hidden,
        temporal_bias[:, None],
    )


def solution(mesh):
    return jax.shard_map(
        body,
        mesh=mesh,
        in_specs=(
            P(("groups", "tm"), "height", "chan", None),
            P("chan"),
            P("chan"),
            P(None, None, "tm", "chan"),
            P("chan"),
            P("chan"),
            P("chan"),
            P(None, "tm", "chan"),
            P("chan"),
        ),
        out_specs=P(("groups", "tm"), "height", "chan", None),
        check_vma=False,
    )
```

```python
import jax
import jax.numpy as jnp
from jax import lax
from jax.experimental import pallas as pl
from jax.experimental.pallas import tpu as pltpu
from jax.sharding import PartitionSpec as P

C = 320
GROUPS = 32


EPSILON = 1e-06


def swap_chan(block):
    return lax.ppermute(block, "chan", [(0, 1), (1, 0)])


def row_halo(block):
    count = lax.axis_size("height")
    forward = [(i, i + 1) for i in range(count - 1)]
    backward = [(target, source) for source, target in forward]
    low = lax.ppermute(block[:, -1:], "height", forward)
    high = lax.ppermute(block[:, :1], "height", backward)
    return jnp.concatenate([low, block, high], axis=1)


def gather_tm(piece):
    count = lax.axis_size("tm")
    index = lax.axis_index("tm")
    pieces = [piece]
    for shift in range(1, count):
        pairs = [(i, (i - shift) % count) for i in range(count)]
        pieces.append(lax.ppermute(piece, "tm", pairs))
    stacked = jnp.roll(jnp.stack(pieces), index, axis=0)
    return stacked


def group_stats(grouped, axes, slot_axes):
    count = 1
    for axis in axes:
        count *= grouped.shape[axis]
    local_mean = jnp.sum(grouped, axis=axes) / count
    centred = grouped - jnp.expand_dims(local_mean, axes)
    local_m2 = jnp.sum(centred * centred, axis=axes)
    slots = 1
    for name in slot_axes:
        slots *= lax.axis_size(name)
    slot = 0
    for name in slot_axes:
        slot = slot * lax.axis_size(name) + lax.axis_index(name)
    mine = jnp.stack([local_mean, local_m2])
    table = jnp.zeros((slots,) + mine.shape, jnp.float32)
    table = lax.dynamic_update_index_in_dim(table, mine, slot, 0)
    for name in reversed(slot_axes):
        table = lax.psum(table, name)
    means = table[:, 0]
    average = jnp.sum(means, axis=0) / slots
    spread = means - average
    m2 = jnp.sum(table[:, 1], axis=0) + count * jnp.sum(spread * spread, axis=0)
    variance = m2 / (count * slots)
    return average, variance


def group_act(values, average, variance, gain, bias):
    frames, rows, local_chan, width = values.shape
    local_groups = average.shape[-1]
    grouped = values.reshape(frames, rows, local_groups, local_chan // local_groups, width)
    centred = grouped - average.reshape(-1, 1, local_groups, 1, 1)
    scaled = (centred * lax.rsqrt(variance.reshape(-1, 1, local_groups, 1, 1) + EPSILON)).reshape(
        frames, rows, local_chan, width
    )
    return jax.nn.silu(scaled * gain[:, None] + bias[:, None]).astype(jnp.bfloat16)


def in_order(own, other, chan_index):
    size = own.shape[2]
    joined = jnp.zeros(own.shape[:2] + (2 * size,) + own.shape[3:], own.dtype)
    joined = lax.dynamic_update_slice_in_dim(joined, own, chan_index * size, axis=2)
    return lax.dynamic_update_slice_in_dim(joined, other, (1 - chan_index) * size, axis=2)


STEP = 12


def pair(ref, first):
    return jnp.concatenate([ref[0, first + k] for k in range(STEP)], axis=1)


def spatial_kernel(xo_ref, xt_ref, wo_ref, wt_ref, res_ref, b_ref, early_ref, o_ref):
    rows, local_chan, width = o_ref.shape[1], o_ref.shape[2], o_ref.shape[3]
    lane = lax.broadcasted_iota(jnp.int32, (local_chan, width), 1)
    bias = b_ref[...]

    def two_rows(i, carry):
        r = STEP * i
        y = jnp.dot(wo_ref[0], pair(xo_ref, r), preferred_element_type=jnp.float32)
        y = y + jnp.dot(wt_ref[0], pair(xt_ref, r), preferred_element_type=jnp.float32)
        for tap in (1, 2):
            y = y + jnp.dot(wo_ref[tap], pair(xo_ref, r + tap), preferred_element_type=jnp.float32)
            y = y + jnp.dot(wt_ref[tap], pair(xt_ref, r + tap), preferred_element_type=jnp.float32)
        for half in range(STEP):
            part = y[:, half * width : (half + 1) * width]
            left = pltpu.roll(part[:local_chan], 1, 1)
            left = jnp.where(lane == 0, 0.0, left)
            right = pltpu.roll(part[2 * local_chan :], width - 1, 1)
            right = jnp.where(lane == width - 1, 0.0, right)
            total = left + part[local_chan : 2 * local_chan] + right
            o_ref[0, r + half] = (res_ref[0, r + half].astype(jnp.float32) + total + bias).astype(
                o_ref.dtype
            )
        return carry

    lax.fori_loop(0, rows // STEP, two_rows, 0)


def spatial_call(own, other, weight_own, weight_other, residual, bias, early):
    frames, rows, local_chan, width = residual.shape
    act_spec = pl.BlockSpec((1, rows + 2, local_chan, width), lambda f: (f, 0, 0, 0))
    weight_spec = pl.BlockSpec((3, 3 * local_chan, local_chan), lambda f: (0, 0, 0))
    return pl.pallas_call(
        spatial_kernel,
        out_shape=jax.ShapeDtypeStruct(residual.shape, jnp.bfloat16),
        grid=(frames,),
        in_specs=[
            act_spec,
            act_spec,
            weight_spec,
            weight_spec,
            pl.BlockSpec((1, rows, local_chan, width), lambda f: (f, 0, 0, 0)),
            pl.BlockSpec((local_chan, 1), lambda f: (0, 0)),
            pl.BlockSpec(memory_space=pl.ANY),
        ],
        out_specs=pl.BlockSpec((1, rows, local_chan, width), lambda f: (f, 0, 0, 0)),
        compiler_params=pltpu.CompilerParams(vmem_limit_bytes=48 * 1024 * 1024),
        cost_estimate=pl.CostEstimate(
            flops=2 * frames * rows * width * 18 * local_chan * local_chan,
            transcendentals=0,
            bytes_accessed=4 * own.size + 4 * weight_own.size + 4 * residual.size,
        ),
    )(own, other, weight_own, weight_other, residual, bias, early)


def temporal_kernel(*refs):
    own_refs, other_refs = refs[0:3], refs[3:6]
    wo_ref, wt_ref, res_ref, bias_ref, o_ref = refs[6:]
    rows, width = o_ref.shape[1], o_ref.shape[3]
    bias = bias_ref[...]

    def two_rows(i, carry):
        r = STEP * i
        y = jnp.dot(wo_ref[0], pair(own_refs[0], r), preferred_element_type=jnp.float32)
        y = y + jnp.dot(wt_ref[0], pair(other_refs[0], r), preferred_element_type=jnp.float32)
        for tap in (1, 2):
            y = y + jnp.dot(wo_ref[tap], pair(own_refs[tap], r), preferred_element_type=jnp.float32)
            y = y + jnp.dot(wt_ref[tap], pair(other_refs[tap], r), preferred_element_type=jnp.float32)
        for half in range(STEP):
            part = y[:, half * width : (half + 1) * width]
            o_ref[0, r + half] = (res_ref[0, r + half].astype(jnp.float32) + part + bias).astype(
                o_ref.dtype
            )
        return carry

    lax.fori_loop(0, rows // STEP, two_rows, 0)


def frame_spec(tap, rows, chans, width):
    return pl.BlockSpec((1, rows, chans, width), lambda f: (f + tap, 0, 0, 0))


def temporal_call(own, other, weight_own, weight_other, residual, bias):
    frames, rows, local_chan, width = residual.shape
    taps = [frame_spec(tap, rows, local_chan, width) for tap in range(3)]
    weight_spec = pl.BlockSpec((3, local_chan, local_chan), lambda f: (0, 0, 0))
    return pl.pallas_call(
        temporal_kernel,
        out_shape=jax.ShapeDtypeStruct(residual.shape, jnp.bfloat16),
        grid=(frames,),
        in_specs=taps
        + taps
        + [
            weight_spec,
            weight_spec,
            pl.BlockSpec((1, rows, local_chan, width), lambda f: (f, 0, 0, 0)),
            pl.BlockSpec((local_chan, 1), lambda f: (0, 0)),
        ],
        out_specs=pl.BlockSpec((1, rows, local_chan, width), lambda f: (f, 0, 0, 0)),
        compiler_params=pltpu.CompilerParams(vmem_limit_bytes=48 * 1024 * 1024),
        cost_estimate=pl.CostEstimate(
            flops=2 * frames * rows * width * 6 * local_chan * local_chan,
            transcendentals=0,
            bytes_accessed=12 * residual.size + 4 * weight_own.size + 4 * residual.size,
        ),
    )(own, own, own, other, other, other, weight_own, weight_other, residual, bias)


def spatial_taps(running, channel_slab, weight, rows, width):
    for row_tap in range(3):
        for col_tap in range(3):
            window = channel_slab[:, row_tap : row_tap + rows, :, col_tap : col_tap + width]
            running = running + jnp.einsum(
                "frcw,co->frow", window, weight[row_tap, col_tap], preferred_element_type=jnp.float32
            )
    return running


def temporal_taps(running, channel_slab, weight, frames):
    for frame_tap in range(3):
        window = channel_slab[frame_tap : frame_tap + frames]
        running = running + jnp.einsum(
            "frcw,co->frow", window, weight[frame_tap], preferred_element_type=jnp.float32
        )
    return running


def body(
    video,
    norm1_gain,
    norm1_bias,
    spatial_weight,
    spatial_bias,
    norm2_gain,
    norm2_bias,
    temporal_weight,
    temporal_bias,
):
    frames, rows, local_chan, width = video.shape
    group_size = C // GROUPS
    local_groups = local_chan // group_size
    chan_index = lax.axis_index("chan")
    tm_index = lax.axis_index("tm")
    tm_count = lax.axis_size("tm")

    spatial_full = lax.all_gather(spatial_weight, "tm", axis=2, tiled=True).reshape(9, C, local_chan)
    temporal_pieces = gather_tm(temporal_weight)
    temporal_full = jnp.moveaxis(temporal_pieces, 0, 1).reshape(3, C, local_chan)
    spatial_full = spatial_full.reshape(3, 3, C, local_chan)

    values = video.astype(jnp.float32)
    grouped = values.reshape(frames, rows, local_groups, group_size, width)
    average, variance = group_stats(grouped, (1, 3, 4), ("height",))
    act_one = group_act(values, average, variance, norm1_gain, norm1_bias)

    with_rows = row_halo(act_one)
    own_start = chan_index * local_chan
    other_start = (1 - chan_index) * local_chan
    spatial_rows = jnp.transpose(spatial_full, (0, 1, 3, 2)).reshape(3, 3 * local_chan, C)
    hidden = spatial_call(
        with_rows,
        swap_chan(with_rows),
        lax.dynamic_slice_in_dim(spatial_rows, own_start, local_chan, axis=2),
        lax.dynamic_slice_in_dim(spatial_rows, other_start, local_chan, axis=2),
        video,
        spatial_bias[:, None],
        temporal_pieces,
    )

    forward = [(i, i + 1) for i in range(tm_count - 1)]
    backward = [(target, source) for source, target in forward]
    before = lax.ppermute(hidden[-1:], "tm", forward)
    after = lax.ppermute(hidden[:1], "tm", backward)

    hidden_values = hidden.astype(jnp.float32)
    grouped_two = hidden_values.reshape(frames, rows, local_groups, group_size, width)
    average_two, variance_two = group_stats(grouped_two, (0, 1, 3, 4), ("tm", "height"))

    extended = jnp.concatenate([before, hidden, after], axis=0).astype(jnp.float32)
    act_two = group_act(extended, average_two, variance_two, norm2_gain, norm2_bias)
    frame_ids = jnp.arange(frames + 2)
    inside = (frame_ids > 0) | (tm_index > 0)
    inside = inside & ((frame_ids < frames + 1) | (tm_index < tm_count - 1))
    act_two = jnp.where(inside[:, None, None, None], act_two, jnp.zeros_like(act_two))

    temporal_rows = jnp.transpose(temporal_full, (0, 2, 1))
    return temporal_call(
        act_two,
        swap_chan(act_two),
        lax.dynamic_slice_in_dim(temporal_rows, own_start, local_chan, axis=2),
        lax.dynamic_slice_in_dim(temporal_rows, other_start, local_chan, axis=2),
        hidden,
        temporal_bias[:, None],
    )


def solution(mesh):
    return jax.shard_map(
        body,
        mesh=mesh,
        in_specs=(
            P(("groups", "tm"), "height", "chan", None),
            P("chan"),
            P("chan"),
            P(None, None, "tm", "chan"),
            P("chan"),
            P("chan"),
            P("chan"),
            P(None, "tm", "chan"),
            P("chan"),
        ),
        out_specs=P(("groups", "tm"), "height", "chan", None),
        check_vma=False,
    )
```

```python
import jax
import jax.numpy as jnp
from jax import lax
from jax.experimental import pallas as pl
from jax.experimental.pallas import tpu as pltpu
from jax.sharding import PartitionSpec as P

C = 320
GROUPS = 32


EPSILON = 1e-06


def swap_chan(block):
    return lax.ppermute(block, "chan", [(0, 1), (1, 0)])


def row_halo(block):
    count = lax.axis_size("height")
    forward = [(i, i + 1) for i in range(count - 1)]
    backward = [(target, source) for source, target in forward]
    low = lax.ppermute(block[:, -1:], "height", forward)
    high = lax.ppermute(block[:, :1], "height", backward)
    return jnp.concatenate([low, block, high], axis=1)


def gather_tm(piece):
    count = lax.axis_size("tm")
    index = lax.axis_index("tm")
    pieces = [piece]
    for shift in range(1, count):
        pairs = [(i, (i - shift) % count) for i in range(count)]
        pieces.append(lax.ppermute(piece, "tm", pairs))
    stacked = jnp.roll(jnp.stack(pieces), index, axis=0)
    return stacked


def group_stats(grouped, axes, slot_axes):
    count = 1
    for axis in axes:
        count *= grouped.shape[axis]
    local_mean = jnp.sum(grouped, axis=axes) / count
    centred = grouped - jnp.expand_dims(local_mean, axes)
    local_m2 = jnp.sum(centred * centred, axis=axes)
    slots = 1
    for name in slot_axes:
        slots *= lax.axis_size(name)
    slot = 0
    for name in slot_axes:
        slot = slot * lax.axis_size(name) + lax.axis_index(name)
    mine = jnp.stack([local_mean, local_m2])
    table = jnp.zeros((slots,) + mine.shape, jnp.float32)
    table = lax.dynamic_update_index_in_dim(table, mine, slot, 0)
    for name in reversed(slot_axes):
        if lax.axis_size(name) == 2:
            table = table + lax.ppermute(table, name, [(0, 1), (1, 0)])
        else:
            table = lax.psum(table, name)
    means = table[:, 0]
    average = jnp.sum(means, axis=0) / slots
    spread = means - average
    m2 = jnp.sum(table[:, 1], axis=0) + count * jnp.sum(spread * spread, axis=0)
    variance = m2 / (count * slots)
    return average, variance


def group_act(values, average, variance, gain, bias):
    frames, rows, local_chan, width = values.shape
    local_groups = average.shape[-1]
    grouped = values.reshape(frames, rows, local_groups, local_chan // local_groups, width)
    centred = grouped - average.reshape(-1, 1, local_groups, 1, 1)
    scaled = (centred * lax.rsqrt(variance.reshape(-1, 1, local_groups, 1, 1) + EPSILON)).reshape(
        frames, rows, local_chan, width
    )
    return jax.nn.silu(scaled * gain[:, None] + bias[:, None]).astype(jnp.bfloat16)


def in_order(own, other, chan_index):
    size = own.shape[2]
    joined = jnp.zeros(own.shape[:2] + (2 * size,) + own.shape[3:], own.dtype)
    joined = lax.dynamic_update_slice_in_dim(joined, own, chan_index * size, axis=2)
    return lax.dynamic_update_slice_in_dim(joined, other, (1 - chan_index) * size, axis=2)


STEP = 12


def pair(ref, first):
    return jnp.concatenate([ref[0, first + k] for k in range(STEP)], axis=1)


def spatial_kernel(xo_ref, xt_ref, wo_ref, wt_ref, res_ref, b_ref, early_ref, o_ref):
    rows, local_chan, width = o_ref.shape[1], o_ref.shape[2], o_ref.shape[3]
    lane = lax.broadcasted_iota(jnp.int32, (local_chan, width), 1)
    bias = b_ref[...]

    def two_rows(i, carry):
        r = STEP * i
        y = jnp.dot(wo_ref[0], pair(xo_ref, r), preferred_element_type=jnp.float32)
        y = y + jnp.dot(wt_ref[0], pair(xt_ref, r), preferred_element_type=jnp.float32)
        for tap in (1, 2):
            y = y + jnp.dot(wo_ref[tap], pair(xo_ref, r + tap), preferred_element_type=jnp.float32)
            y = y + jnp.dot(wt_ref[tap], pair(xt_ref, r + tap), preferred_element_type=jnp.float32)
        for half in range(STEP):
            part = y[:, half * width : (half + 1) * width]
            left = pltpu.roll(part[:local_chan], 1, 1)
            left = jnp.where(lane == 0, 0.0, left)
            right = pltpu.roll(part[2 * local_chan :], width - 1, 1)
            right = jnp.where(lane == width - 1, 0.0, right)
            total = left + part[local_chan : 2 * local_chan] + right
            o_ref[0, r + half] = (res_ref[0, r + half].astype(jnp.float32) + total + bias).astype(
                o_ref.dtype
            )
        return carry

    lax.fori_loop(0, rows // STEP, two_rows, 0)


def spatial_call(own, other, weight_own, weight_other, residual, bias, early):
    frames, rows, local_chan, width = residual.shape
    act_spec = pl.BlockSpec((1, rows + 2, local_chan, width), lambda f: (f, 0, 0, 0))
    weight_spec = pl.BlockSpec((3, 3 * local_chan, local_chan), lambda f: (0, 0, 0))
    return pl.pallas_call(
        spatial_kernel,
        out_shape=jax.ShapeDtypeStruct(residual.shape, jnp.bfloat16),
        grid=(frames,),
        in_specs=[
            act_spec,
            act_spec,
            weight_spec,
            weight_spec,
            pl.BlockSpec((1, rows, local_chan, width), lambda f: (f, 0, 0, 0)),
            pl.BlockSpec((local_chan, 1), lambda f: (0, 0)),
            pl.BlockSpec(memory_space=pl.ANY),
        ],
        out_specs=pl.BlockSpec((1, rows, local_chan, width), lambda f: (f, 0, 0, 0)),
        compiler_params=pltpu.CompilerParams(vmem_limit_bytes=48 * 1024 * 1024),
        cost_estimate=pl.CostEstimate(
            flops=2 * frames * rows * width * 18 * local_chan * local_chan,
            transcendentals=0,
            bytes_accessed=4 * own.size + 4 * weight_own.size + 4 * residual.size,
        ),
    )(own, other, weight_own, weight_other, residual, bias, early)


def temporal_kernel(*refs):
    own_refs, other_refs = refs[0:3], refs[3:6]
    wo_ref, wt_ref, res_ref, bias_ref, o_ref = refs[6:]
    rows, width = o_ref.shape[1], o_ref.shape[3]
    bias = bias_ref[...]

    def two_rows(i, carry):
        r = STEP * i
        y = jnp.dot(wo_ref[0], pair(own_refs[0], r), preferred_element_type=jnp.float32)
        y = y + jnp.dot(wt_ref[0], pair(other_refs[0], r), preferred_element_type=jnp.float32)
        for tap in (1, 2):
            y = y + jnp.dot(wo_ref[tap], pair(own_refs[tap], r), preferred_element_type=jnp.float32)
            y = y + jnp.dot(wt_ref[tap], pair(other_refs[tap], r), preferred_element_type=jnp.float32)
        for half in range(STEP):
            part = y[:, half * width : (half + 1) * width]
            o_ref[0, r + half] = (res_ref[0, r + half].astype(jnp.float32) + part + bias).astype(
                o_ref.dtype
            )
        return carry

    lax.fori_loop(0, rows // STEP, two_rows, 0)


def frame_spec(tap, rows, chans, width):
    return pl.BlockSpec((1, rows, chans, width), lambda f: (f + tap, 0, 0, 0))


def temporal_call(own, other, weight_own, weight_other, residual, bias):
    frames, rows, local_chan, width = residual.shape
    taps = [frame_spec(tap, rows, local_chan, width) for tap in range(3)]
    weight_spec = pl.BlockSpec((3, local_chan, local_chan), lambda f: (0, 0, 0))
    return pl.pallas_call(
        temporal_kernel,
        out_shape=jax.ShapeDtypeStruct(residual.shape, jnp.bfloat16),
        grid=(frames,),
        in_specs=taps
        + taps
        + [
            weight_spec,
            weight_spec,
            pl.BlockSpec((1, rows, local_chan, width), lambda f: (f, 0, 0, 0)),
            pl.BlockSpec((local_chan, 1), lambda f: (0, 0)),
        ],
        out_specs=pl.BlockSpec((1, rows, local_chan, width), lambda f: (f, 0, 0, 0)),
        compiler_params=pltpu.CompilerParams(vmem_limit_bytes=48 * 1024 * 1024),
        cost_estimate=pl.CostEstimate(
            flops=2 * frames * rows * width * 6 * local_chan * local_chan,
            transcendentals=0,
            bytes_accessed=12 * residual.size + 4 * weight_own.size + 4 * residual.size,
        ),
    )(own, own, own, other, other, other, weight_own, weight_other, residual, bias)


def spatial_taps(running, channel_slab, weight, rows, width):
    for row_tap in range(3):
        for col_tap in range(3):
            window = channel_slab[:, row_tap : row_tap + rows, :, col_tap : col_tap + width]
            running = running + jnp.einsum(
                "frcw,co->frow", window, weight[row_tap, col_tap], preferred_element_type=jnp.float32
            )
    return running


def temporal_taps(running, channel_slab, weight, frames):
    for frame_tap in range(3):
        window = channel_slab[frame_tap : frame_tap + frames]
        running = running + jnp.einsum(
            "frcw,co->frow", window, weight[frame_tap], preferred_element_type=jnp.float32
        )
    return running


def body(
    video,
    norm1_gain,
    norm1_bias,
    spatial_weight,
    spatial_bias,
    norm2_gain,
    norm2_bias,
    temporal_weight,
    temporal_bias,
):
    frames, rows, local_chan, width = video.shape
    group_size = C // GROUPS
    local_groups = local_chan // group_size
    chan_index = lax.axis_index("chan")
    tm_index = lax.axis_index("tm")
    tm_count = lax.axis_size("tm")

    spatial_full = lax.all_gather(spatial_weight, "tm", axis=2, tiled=True).reshape(9, C, local_chan)
    temporal_pieces = gather_tm(temporal_weight)
    temporal_full = jnp.moveaxis(temporal_pieces, 0, 1).reshape(3, C, local_chan)
    spatial_full = spatial_full.reshape(3, 3, C, local_chan)

    values = video.astype(jnp.float32)
    grouped = values.reshape(frames, rows, local_groups, group_size, width)
    average, variance = group_stats(grouped, (1, 3, 4), ("height",))
    act_one = group_act(values, average, variance, norm1_gain, norm1_bias)

    with_rows = row_halo(act_one)
    own_start = chan_index * local_chan
    other_start = (1 - chan_index) * local_chan
    spatial_rows = jnp.transpose(spatial_full, (0, 1, 3, 2)).reshape(3, 3 * local_chan, C)
    hidden = spatial_call(
        with_rows,
        swap_chan(with_rows),
        lax.dynamic_slice_in_dim(spatial_rows, own_start, local_chan, axis=2),
        lax.dynamic_slice_in_dim(spatial_rows, other_start, local_chan, axis=2),
        video,
        spatial_bias[:, None],
        temporal_pieces,
    )

    forward = [(i, i + 1) for i in range(tm_count - 1)]
    backward = [(target, source) for source, target in forward]
    before = lax.ppermute(hidden[-1:], "tm", forward)
    after = lax.ppermute(hidden[:1], "tm", backward)

    hidden_values = hidden.astype(jnp.float32)
    grouped_two = hidden_values.reshape(frames, rows, local_groups, group_size, width)
    average_two, variance_two = group_stats(grouped_two, (0, 1, 3, 4), ("tm", "height"))

    extended = jnp.concatenate([before, hidden, after], axis=0).astype(jnp.float32)
    act_two = group_act(extended, average_two, variance_two, norm2_gain, norm2_bias)
    frame_ids = jnp.arange(frames + 2)
    inside = (frame_ids > 0) | (tm_index > 0)
    inside = inside & ((frame_ids < frames + 1) | (tm_index < tm_count - 1))
    act_two = jnp.where(inside[:, None, None, None], act_two, jnp.zeros_like(act_two))

    temporal_rows = jnp.transpose(temporal_full, (0, 2, 1))
    return temporal_call(
        act_two,
        swap_chan(act_two),
        lax.dynamic_slice_in_dim(temporal_rows, own_start, local_chan, axis=2),
        lax.dynamic_slice_in_dim(temporal_rows, other_start, local_chan, axis=2),
        hidden,
        temporal_bias[:, None],
    )


def solution(mesh):
    return jax.shard_map(
        body,
        mesh=mesh,
        in_specs=(
            P(("groups", "tm"), "height", "chan", None),
            P("chan"),
            P("chan"),
            P(None, None, "tm", "chan"),
            P("chan"),
            P("chan"),
            P("chan"),
            P(None, "tm", "chan"),
            P("chan"),
        ),
        out_specs=P(("groups", "tm"), "height", "chan", None),
        check_vma=False,
    )
```

```python
import jax
import jax.numpy as jnp
from jax import lax
from jax.experimental import pallas as pl
from jax.experimental.pallas import tpu as pltpu
from jax.sharding import PartitionSpec as P

C = 320
GROUPS = 32


EPSILON = 1e-06


def swap_chan(block):
    return lax.ppermute(block, "chan", [(0, 1), (1, 0)])


def row_halo(block):
    count = lax.axis_size("height")
    forward = [(i, i + 1) for i in range(count - 1)]
    backward = [(target, source) for source, target in forward]
    low = lax.ppermute(block[:, -1:], "height", forward)
    high = lax.ppermute(block[:, :1], "height", backward)
    return jnp.concatenate([low, block, high], axis=1)


def gather_tm(piece):
    count = lax.axis_size("tm")
    index = lax.axis_index("tm")
    pieces = [piece]
    for shift in range(1, count):
        pairs = [(i, (i - shift) % count) for i in range(count)]
        pieces.append(lax.ppermute(piece, "tm", pairs))
    stacked = jnp.roll(jnp.stack(pieces), index, axis=0)
    return stacked


def group_stats(grouped, axes, slot_axes):
    count = 1
    for axis in axes:
        count *= grouped.shape[axis]
    local_mean = jnp.sum(grouped, axis=axes) / count
    centred = grouped - jnp.expand_dims(local_mean, axes)
    local_m2 = jnp.sum(centred * centred, axis=axes)
    slots = 1
    for name in slot_axes:
        slots *= lax.axis_size(name)
    slot = 0
    for name in slot_axes:
        slot = slot * lax.axis_size(name) + lax.axis_index(name)
    mine = jnp.stack([local_mean, local_m2])
    table = jnp.zeros((slots,) + mine.shape, jnp.float32)
    table = lax.dynamic_update_index_in_dim(table, mine, slot, 0)
    for name in reversed(slot_axes):
        if lax.axis_size(name) == 2:
            table = table + lax.ppermute(table, name, [(0, 1), (1, 0)])
        else:
            table = lax.psum(table, name)
    means = table[:, 0]
    average = jnp.sum(means, axis=0) / slots
    spread = means - average
    m2 = jnp.sum(table[:, 1], axis=0) + count * jnp.sum(spread * spread, axis=0)
    variance = m2 / (count * slots)
    return average, variance


def group_act(values, average, variance, gain, bias):
    frames, rows, local_chan, width = values.shape
    local_groups = average.shape[-1]
    grouped = values.reshape(frames, rows, local_groups, local_chan // local_groups, width)
    centred = grouped - average.reshape(-1, 1, local_groups, 1, 1)
    scaled = (centred * lax.rsqrt(variance.reshape(-1, 1, local_groups, 1, 1) + EPSILON)).reshape(
        frames, rows, local_chan, width
    )
    return jax.nn.silu(scaled * gain[:, None] + bias[:, None]).astype(jnp.bfloat16)


def in_order(own, other, chan_index):
    size = own.shape[2]
    joined = jnp.zeros(own.shape[:2] + (2 * size,) + own.shape[3:], own.dtype)
    joined = lax.dynamic_update_slice_in_dim(joined, own, chan_index * size, axis=2)
    return lax.dynamic_update_slice_in_dim(joined, other, (1 - chan_index) * size, axis=2)


STEP = 18


def pair(ref, first):
    return jnp.concatenate([ref[0, first + k] for k in range(STEP)], axis=1)


def spatial_kernel(xo_ref, xt_ref, wo_ref, wt_ref, res_ref, b_ref, early_ref, o_ref):
    rows, local_chan, width = o_ref.shape[1], o_ref.shape[2], o_ref.shape[3]
    lane = lax.broadcasted_iota(jnp.int32, (local_chan, width), 1)
    bias = b_ref[...]

    def two_rows(i, carry):
        r = STEP * i
        y = jnp.dot(wo_ref[0], pair(xo_ref, r), preferred_element_type=jnp.float32)
        y = y + jnp.dot(wt_ref[0], pair(xt_ref, r), preferred_element_type=jnp.float32)
        for tap in (1, 2):
            y = y + jnp.dot(wo_ref[tap], pair(xo_ref, r + tap), preferred_element_type=jnp.float32)
            y = y + jnp.dot(wt_ref[tap], pair(xt_ref, r + tap), preferred_element_type=jnp.float32)
        for half in range(STEP):
            part = y[:, half * width : (half + 1) * width]
            left = pltpu.roll(part[:local_chan], 1, 1)
            left = jnp.where(lane == 0, 0.0, left)
            right = pltpu.roll(part[2 * local_chan :], width - 1, 1)
            right = jnp.where(lane == width - 1, 0.0, right)
            total = left + part[local_chan : 2 * local_chan] + right
            o_ref[0, r + half] = (res_ref[0, r + half].astype(jnp.float32) + total + bias).astype(
                o_ref.dtype
            )
        return carry

    lax.fori_loop(0, rows // STEP, two_rows, 0)


def spatial_call(own, other, weight_own, weight_other, residual, bias, early):
    frames, rows, local_chan, width = residual.shape
    act_spec = pl.BlockSpec((1, rows + 2, local_chan, width), lambda f: (f, 0, 0, 0))
    weight_spec = pl.BlockSpec((3, 3 * local_chan, local_chan), lambda f: (0, 0, 0))
    return pl.pallas_call(
        spatial_kernel,
        out_shape=jax.ShapeDtypeStruct(residual.shape, jnp.bfloat16),
        grid=(frames,),
        in_specs=[
            act_spec,
            act_spec,
            weight_spec,
            weight_spec,
            pl.BlockSpec((1, rows, local_chan, width), lambda f: (f, 0, 0, 0)),
            pl.BlockSpec((local_chan, 1), lambda f: (0, 0)),
            pl.BlockSpec(memory_space=pl.ANY),
        ],
        out_specs=pl.BlockSpec((1, rows, local_chan, width), lambda f: (f, 0, 0, 0)),
        compiler_params=pltpu.CompilerParams(vmem_limit_bytes=48 * 1024 * 1024),
        cost_estimate=pl.CostEstimate(
            flops=2 * frames * rows * width * 18 * local_chan * local_chan,
            transcendentals=0,
            bytes_accessed=4 * own.size + 4 * weight_own.size + 4 * residual.size,
        ),
    )(own, other, weight_own, weight_other, residual, bias, early)


def temporal_kernel(*refs):
    own_refs, other_refs = refs[0:3], refs[3:6]
    wo_ref, wt_ref, res_ref, bias_ref, o_ref = refs[6:]
    rows, width = o_ref.shape[1], o_ref.shape[3]
    bias = bias_ref[...]

    def two_rows(i, carry):
        r = STEP * i
        y = jnp.dot(wo_ref[0], pair(own_refs[0], r), preferred_element_type=jnp.float32)
        y = y + jnp.dot(wt_ref[0], pair(other_refs[0], r), preferred_element_type=jnp.float32)
        for tap in (1, 2):
            y = y + jnp.dot(wo_ref[tap], pair(own_refs[tap], r), preferred_element_type=jnp.float32)
            y = y + jnp.dot(wt_ref[tap], pair(other_refs[tap], r), preferred_element_type=jnp.float32)
        for half in range(STEP):
            part = y[:, half * width : (half + 1) * width]
            o_ref[0, r + half] = (res_ref[0, r + half].astype(jnp.float32) + part + bias).astype(
                o_ref.dtype
            )
        return carry

    lax.fori_loop(0, rows // STEP, two_rows, 0)


def frame_spec(tap, rows, chans, width):
    return pl.BlockSpec((1, rows, chans, width), lambda f: (f + tap, 0, 0, 0))


def temporal_call(own, other, weight_own, weight_other, residual, bias):
    frames, rows, local_chan, width = residual.shape
    taps = [frame_spec(tap, rows, local_chan, width) for tap in range(3)]
    weight_spec = pl.BlockSpec((3, local_chan, local_chan), lambda f: (0, 0, 0))
    return pl.pallas_call(
        temporal_kernel,
        out_shape=jax.ShapeDtypeStruct(residual.shape, jnp.bfloat16),
        grid=(frames,),
        in_specs=taps
        + taps
        + [
            weight_spec,
            weight_spec,
            pl.BlockSpec((1, rows, local_chan, width), lambda f: (f, 0, 0, 0)),
            pl.BlockSpec((local_chan, 1), lambda f: (0, 0)),
        ],
        out_specs=pl.BlockSpec((1, rows, local_chan, width), lambda f: (f, 0, 0, 0)),
        compiler_params=pltpu.CompilerParams(vmem_limit_bytes=48 * 1024 * 1024),
        cost_estimate=pl.CostEstimate(
            flops=2 * frames * rows * width * 6 * local_chan * local_chan,
            transcendentals=0,
            bytes_accessed=12 * residual.size + 4 * weight_own.size + 4 * residual.size,
        ),
    )(own, own, own, other, other, other, weight_own, weight_other, residual, bias)


def spatial_taps(running, channel_slab, weight, rows, width):
    for row_tap in range(3):
        for col_tap in range(3):
            window = channel_slab[:, row_tap : row_tap + rows, :, col_tap : col_tap + width]
            running = running + jnp.einsum(
                "frcw,co->frow", window, weight[row_tap, col_tap], preferred_element_type=jnp.float32
            )
    return running


def temporal_taps(running, channel_slab, weight, frames):
    for frame_tap in range(3):
        window = channel_slab[frame_tap : frame_tap + frames]
        running = running + jnp.einsum(
            "frcw,co->frow", window, weight[frame_tap], preferred_element_type=jnp.float32
        )
    return running


def body(
    video,
    norm1_gain,
    norm1_bias,
    spatial_weight,
    spatial_bias,
    norm2_gain,
    norm2_bias,
    temporal_weight,
    temporal_bias,
):
    frames, rows, local_chan, width = video.shape
    group_size = C // GROUPS
    local_groups = local_chan // group_size
    chan_index = lax.axis_index("chan")
    tm_index = lax.axis_index("tm")
    tm_count = lax.axis_size("tm")

    spatial_full = lax.all_gather(spatial_weight, "tm", axis=2, tiled=True).reshape(9, C, local_chan)
    temporal_pieces = gather_tm(temporal_weight)
    temporal_full = jnp.moveaxis(temporal_pieces, 0, 1).reshape(3, C, local_chan)
    spatial_full = spatial_full.reshape(3, 3, C, local_chan)

    values = video.astype(jnp.float32)
    grouped = values.reshape(frames, rows, local_groups, group_size, width)
    average, variance = group_stats(grouped, (1, 3, 4), ("height",))
    act_one = group_act(values, average, variance, norm1_gain, norm1_bias)

    with_rows = row_halo(act_one)
    own_start = chan_index * local_chan
    other_start = (1 - chan_index) * local_chan
    spatial_rows = jnp.transpose(spatial_full, (0, 1, 3, 2)).reshape(3, 3 * local_chan, C)
    hidden = spatial_call(
        with_rows,
        swap_chan(with_rows),
        lax.dynamic_slice_in_dim(spatial_rows, own_start, local_chan, axis=2),
        lax.dynamic_slice_in_dim(spatial_rows, other_start, local_chan, axis=2),
        video,
        spatial_bias[:, None],
        temporal_pieces,
    )

    forward = [(i, i + 1) for i in range(tm_count - 1)]
    backward = [(target, source) for source, target in forward]
    before = lax.ppermute(hidden[-1:], "tm", forward)
    after = lax.ppermute(hidden[:1], "tm", backward)

    hidden_values = hidden.astype(jnp.float32)
    grouped_two = hidden_values.reshape(frames, rows, local_groups, group_size, width)
    average_two, variance_two = group_stats(grouped_two, (0, 1, 3, 4), ("tm", "height"))

    extended = jnp.concatenate([before, hidden, after], axis=0).astype(jnp.float32)
    act_two = group_act(extended, average_two, variance_two, norm2_gain, norm2_bias)
    frame_ids = jnp.arange(frames + 2)
    inside = (frame_ids > 0) | (tm_index > 0)
    inside = inside & ((frame_ids < frames + 1) | (tm_index < tm_count - 1))
    act_two = jnp.where(inside[:, None, None, None], act_two, jnp.zeros_like(act_two))

    temporal_rows = jnp.transpose(temporal_full, (0, 2, 1))
    return temporal_call(
        act_two,
        swap_chan(act_two),
        lax.dynamic_slice_in_dim(temporal_rows, own_start, local_chan, axis=2),
        lax.dynamic_slice_in_dim(temporal_rows, other_start, local_chan, axis=2),
        hidden,
        temporal_bias[:, None],
    )


def solution(mesh):
    return jax.shard_map(
        body,
        mesh=mesh,
        in_specs=(
            P(("groups", "tm"), "height", "chan", None),
            P("chan"),
            P("chan"),
            P(None, None, "tm", "chan"),
            P("chan"),
            P("chan"),
            P("chan"),
            P(None, "tm", "chan"),
            P("chan"),
        ),
        out_specs=P(("groups", "tm"), "height", "chan", None),
        check_vma=False,
    )
```

```python
import jax
import jax.numpy as jnp
from jax import lax
from jax.experimental import pallas as pl
from jax.experimental.pallas import tpu as pltpu
from jax.sharding import PartitionSpec as P

C = 320
GROUPS = 32


EPSILON = 1e-06


def swap_chan(block):
    return lax.ppermute(block, "chan", [(0, 1), (1, 0)])


def row_halo(block):
    count = lax.axis_size("height")
    if count == 2:
        index = lax.axis_index("height")
        edge = jnp.where(index == 0, block[:, -1:], block[:, :1])
        received = lax.ppermute(edge, "height", [(0, 1), (1, 0)])
        empty = jnp.zeros_like(received)
        low = jnp.where(index == 1, received, empty)
        high = jnp.where(index == 0, received, empty)
        return jnp.concatenate([low, block, high], axis=1)
    forward = [(i, i + 1) for i in range(count - 1)]
    backward = [(target, source) for source, target in forward]
    low = lax.ppermute(block[:, -1:], "height", forward)
    high = lax.ppermute(block[:, :1], "height", backward)
    return jnp.concatenate([low, block, high], axis=1)


def gather_tm(piece):
    count = lax.axis_size("tm")
    index = lax.axis_index("tm")
    pieces = [piece]
    for shift in range(1, count):
        pairs = [(i, (i - shift) % count) for i in range(count)]
        pieces.append(lax.ppermute(piece, "tm", pairs))
    stacked = jnp.roll(jnp.stack(pieces), index, axis=0)
    return stacked


def group_stats(grouped, axes, slot_axes):
    count = 1
    for axis in axes:
        count *= grouped.shape[axis]
    local_mean = jnp.sum(grouped, axis=axes) / count
    centred = grouped - jnp.expand_dims(local_mean, axes)
    local_m2 = jnp.sum(centred * centred, axis=axes)
    slots = 1
    for name in slot_axes:
        slots *= lax.axis_size(name)
    slot = 0
    for name in slot_axes:
        slot = slot * lax.axis_size(name) + lax.axis_index(name)
    mine = jnp.stack([local_mean, local_m2])
    table = jnp.zeros((slots,) + mine.shape, jnp.float32)
    table = lax.dynamic_update_index_in_dim(table, mine, slot, 0)
    for name in reversed(slot_axes):
        if lax.axis_size(name) == 2:
            table = table + lax.ppermute(table, name, [(0, 1), (1, 0)])
        else:
            table = lax.psum(table, name)
    means = table[:, 0]
    average = jnp.sum(means, axis=0) / slots
    spread = means - average
    m2 = jnp.sum(table[:, 1], axis=0) + count * jnp.sum(spread * spread, axis=0)
    variance = m2 / (count * slots)
    return average, variance


def group_act(values, average, variance, gain, bias):
    frames, rows, local_chan, width = values.shape
    local_groups = average.shape[-1]
    grouped = values.reshape(frames, rows, local_groups, local_chan // local_groups, width)
    centred = grouped - average.reshape(-1, 1, local_groups, 1, 1)
    scaled = (centred * lax.rsqrt(variance.reshape(-1, 1, local_groups, 1, 1) + EPSILON)).reshape(
        frames, rows, local_chan, width
    )
    return jax.nn.silu(scaled * gain[:, None] + bias[:, None]).astype(jnp.bfloat16)


def in_order(own, other, chan_index):
    size = own.shape[2]
    joined = jnp.zeros(own.shape[:2] + (2 * size,) + own.shape[3:], own.dtype)
    joined = lax.dynamic_update_slice_in_dim(joined, own, chan_index * size, axis=2)
    return lax.dynamic_update_slice_in_dim(joined, other, (1 - chan_index) * size, axis=2)


STEP = 18


def pair(ref, first):
    return jnp.concatenate([ref[0, first + k] for k in range(STEP)], axis=1)


def spatial_kernel(xo_ref, xt_ref, wo_ref, wt_ref, res_ref, b_ref, early_ref, o_ref):
    rows, local_chan, width = o_ref.shape[1], o_ref.shape[2], o_ref.shape[3]
    lane = lax.broadcasted_iota(jnp.int32, (local_chan, width), 1)
    bias = b_ref[...]

    def two_rows(i, carry):
        r = STEP * i
        y = jnp.dot(wo_ref[0], pair(xo_ref, r), preferred_element_type=jnp.float32)
        y = y + jnp.dot(wt_ref[0], pair(xt_ref, r), preferred_element_type=jnp.float32)
        for tap in (1, 2):
            y = y + jnp.dot(wo_ref[tap], pair(xo_ref, r + tap), preferred_element_type=jnp.float32)
            y = y + jnp.dot(wt_ref[tap], pair(xt_ref, r + tap), preferred_element_type=jnp.float32)
        for half in range(STEP):
            part = y[:, half * width : (half + 1) * width]
            left = pltpu.roll(part[:local_chan], 1, 1)
            left = jnp.where(lane == 0, 0.0, left)
            right = pltpu.roll(part[2 * local_chan :], width - 1, 1)
            right = jnp.where(lane == width - 1, 0.0, right)
            total = left + part[local_chan : 2 * local_chan] + right
            o_ref[0, r + half] = (res_ref[0, r + half].astype(jnp.float32) + total + bias).astype(
                o_ref.dtype
            )
        return carry

    lax.fori_loop(0, rows // STEP, two_rows, 0)


def spatial_call(own, other, weight_own, weight_other, residual, bias, early):
    frames, rows, local_chan, width = residual.shape
    act_spec = pl.BlockSpec((1, rows + 2, local_chan, width), lambda f: (f, 0, 0, 0))
    weight_spec = pl.BlockSpec((3, 3 * local_chan, local_chan), lambda f: (0, 0, 0))
    return pl.pallas_call(
        spatial_kernel,
        out_shape=jax.ShapeDtypeStruct(residual.shape, jnp.bfloat16),
        grid=(frames,),
        in_specs=[
            act_spec,
            act_spec,
            weight_spec,
            weight_spec,
            pl.BlockSpec((1, rows, local_chan, width), lambda f: (f, 0, 0, 0)),
            pl.BlockSpec((local_chan, 1), lambda f: (0, 0)),
            pl.BlockSpec(memory_space=pl.ANY),
        ],
        out_specs=pl.BlockSpec((1, rows, local_chan, width), lambda f: (f, 0, 0, 0)),
        compiler_params=pltpu.CompilerParams(vmem_limit_bytes=48 * 1024 * 1024),
        cost_estimate=pl.CostEstimate(
            flops=2 * frames * rows * width * 18 * local_chan * local_chan,
            transcendentals=0,
            bytes_accessed=4 * own.size + 4 * weight_own.size + 4 * residual.size,
        ),
    )(own, other, weight_own, weight_other, residual, bias, early)


def temporal_kernel(*refs):
    own_refs, other_refs = refs[0:3], refs[3:6]
    wo_ref, wt_ref, res_ref, bias_ref, o_ref = refs[6:]
    rows, width = o_ref.shape[1], o_ref.shape[3]
    bias = bias_ref[...]

    def two_rows(i, carry):
        r = STEP * i
        y = jnp.dot(wo_ref[0], pair(own_refs[0], r), preferred_element_type=jnp.float32)
        y = y + jnp.dot(wt_ref[0], pair(other_refs[0], r), preferred_element_type=jnp.float32)
        for tap in (1, 2):
            y = y + jnp.dot(wo_ref[tap], pair(own_refs[tap], r), preferred_element_type=jnp.float32)
            y = y + jnp.dot(wt_ref[tap], pair(other_refs[tap], r), preferred_element_type=jnp.float32)
        for half in range(STEP):
            part = y[:, half * width : (half + 1) * width]
            o_ref[0, r + half] = (res_ref[0, r + half].astype(jnp.float32) + part + bias).astype(
                o_ref.dtype
            )
        return carry

    lax.fori_loop(0, rows // STEP, two_rows, 0)


def frame_spec(tap, rows, chans, width):
    return pl.BlockSpec((1, rows, chans, width), lambda f: (f + tap, 0, 0, 0))


def temporal_call(own, other, weight_own, weight_other, residual, bias):
    frames, rows, local_chan, width = residual.shape
    taps = [frame_spec(tap, rows, local_chan, width) for tap in range(3)]
    weight_spec = pl.BlockSpec((3, local_chan, local_chan), lambda f: (0, 0, 0))
    return pl.pallas_call(
        temporal_kernel,
        out_shape=jax.ShapeDtypeStruct(residual.shape, jnp.bfloat16),
        grid=(frames,),
        in_specs=taps
        + taps
        + [
            weight_spec,
            weight_spec,
            pl.BlockSpec((1, rows, local_chan, width), lambda f: (f, 0, 0, 0)),
            pl.BlockSpec((local_chan, 1), lambda f: (0, 0)),
        ],
        out_specs=pl.BlockSpec((1, rows, local_chan, width), lambda f: (f, 0, 0, 0)),
        compiler_params=pltpu.CompilerParams(vmem_limit_bytes=48 * 1024 * 1024),
        cost_estimate=pl.CostEstimate(
            flops=2 * frames * rows * width * 6 * local_chan * local_chan,
            transcendentals=0,
            bytes_accessed=12 * residual.size + 4 * weight_own.size + 4 * residual.size,
        ),
    )(own, own, own, other, other, other, weight_own, weight_other, residual, bias)


def spatial_taps(running, channel_slab, weight, rows, width):
    for row_tap in range(3):
        for col_tap in range(3):
            window = channel_slab[:, row_tap : row_tap + rows, :, col_tap : col_tap + width]
            running = running + jnp.einsum(
                "frcw,co->frow", window, weight[row_tap, col_tap], preferred_element_type=jnp.float32
            )
    return running


def temporal_taps(running, channel_slab, weight, frames):
    for frame_tap in range(3):
        window = channel_slab[frame_tap : frame_tap + frames]
        running = running + jnp.einsum(
            "frcw,co->frow", window, weight[frame_tap], preferred_element_type=jnp.float32
        )
    return running


def body(
    video,
    norm1_gain,
    norm1_bias,
    spatial_weight,
    spatial_bias,
    norm2_gain,
    norm2_bias,
    temporal_weight,
    temporal_bias,
):
    frames, rows, local_chan, width = video.shape
    group_size = C // GROUPS
    local_groups = local_chan // group_size
    chan_index = lax.axis_index("chan")
    tm_index = lax.axis_index("tm")
    tm_count = lax.axis_size("tm")

    spatial_full = lax.all_gather(spatial_weight, "tm", axis=2, tiled=True).reshape(9, C, local_chan)
    temporal_pieces = gather_tm(temporal_weight)
    temporal_full = jnp.moveaxis(temporal_pieces, 0, 1).reshape(3, C, local_chan)
    spatial_full = spatial_full.reshape(3, 3, C, local_chan)

    values = video.astype(jnp.float32)
    grouped = values.reshape(frames, rows, local_groups, group_size, width)
    average, variance = group_stats(grouped, (1, 3, 4), ("height",))
    act_one = group_act(values, average, variance, norm1_gain, norm1_bias)

    with_rows = row_halo(act_one)
    own_start = chan_index * local_chan
    other_start = (1 - chan_index) * local_chan
    spatial_rows = jnp.transpose(spatial_full, (0, 1, 3, 2)).reshape(3, 3 * local_chan, C)
    hidden = spatial_call(
        with_rows,
        swap_chan(with_rows),
        lax.dynamic_slice_in_dim(spatial_rows, own_start, local_chan, axis=2),
        lax.dynamic_slice_in_dim(spatial_rows, other_start, local_chan, axis=2),
        video,
        spatial_bias[:, None],
        temporal_pieces,
    )

    forward = [(i, i + 1) for i in range(tm_count - 1)]
    backward = [(target, source) for source, target in forward]
    before = lax.ppermute(hidden[-1:], "tm", forward)
    after = lax.ppermute(hidden[:1], "tm", backward)

    hidden_values = hidden.astype(jnp.float32)
    grouped_two = hidden_values.reshape(frames, rows, local_groups, group_size, width)
    average_two, variance_two = group_stats(grouped_two, (0, 1, 3, 4), ("tm", "height"))

    extended = jnp.concatenate([before, hidden, after], axis=0).astype(jnp.float32)
    act_two = group_act(extended, average_two, variance_two, norm2_gain, norm2_bias)
    frame_ids = jnp.arange(frames + 2)
    inside = (frame_ids > 0) | (tm_index > 0)
    inside = inside & ((frame_ids < frames + 1) | (tm_index < tm_count - 1))
    act_two = jnp.where(inside[:, None, None, None], act_two, jnp.zeros_like(act_two))

    temporal_rows = jnp.transpose(temporal_full, (0, 2, 1))
    return temporal_call(
        act_two,
        swap_chan(act_two),
        lax.dynamic_slice_in_dim(temporal_rows, own_start, local_chan, axis=2),
        lax.dynamic_slice_in_dim(temporal_rows, other_start, local_chan, axis=2),
        hidden,
        temporal_bias[:, None],
    )


def solution(mesh):
    return jax.shard_map(
        body,
        mesh=mesh,
        in_specs=(
            P(("groups", "tm"), "height", "chan", None),
            P("chan"),
            P("chan"),
            P(None, None, "tm", "chan"),
            P("chan"),
            P("chan"),
            P("chan"),
            P(None, "tm", "chan"),
            P("chan"),
        ),
        out_specs=P(("groups", "tm"), "height", "chan", None),
        check_vma=False,
    )
```

```python
import jax
import jax.numpy as jnp
from jax import lax
from jax.experimental import pallas as pl
from jax.experimental.pallas import tpu as pltpu
from jax.sharding import PartitionSpec as P

C = 320
GROUPS = 32


EPSILON = 1e-06


def swap_chan(block):
    return lax.ppermute(block, "chan", [(0, 1), (1, 0)])


def row_halo(block):
    count = lax.axis_size("height")
    if count == 2:
        index = lax.axis_index("height")
        edge = jnp.where(index == 0, block[:, -1:], block[:, :1])
        received = lax.ppermute(edge, "height", [(0, 1), (1, 0)])
        empty = jnp.zeros_like(received)
        low = jnp.where(index == 1, received, empty)
        high = jnp.where(index == 0, received, empty)
        return jnp.concatenate([low, block, high], axis=1)
    forward = [(i, i + 1) for i in range(count - 1)]
    backward = [(target, source) for source, target in forward]
    low = lax.ppermute(block[:, -1:], "height", forward)
    high = lax.ppermute(block[:, :1], "height", backward)
    return jnp.concatenate([low, block, high], axis=1)


def gather_tm(piece):
    count = lax.axis_size("tm")
    index = lax.axis_index("tm")
    pieces = [piece]
    for shift in range(1, count):
        pairs = [(i, (i - shift) % count) for i in range(count)]
        pieces.append(lax.ppermute(piece, "tm", pairs))
    stacked = jnp.roll(jnp.stack(pieces), index, axis=0)
    return stacked


def group_stats(grouped, axes, slot_axes):
    count = 1
    for axis in axes:
        count *= grouped.shape[axis]
    local_mean = jnp.sum(grouped, axis=axes) / count
    centred = grouped - jnp.expand_dims(local_mean, axes)
    local_m2 = jnp.sum(centred * centred, axis=axes)
    slots = 1
    for name in slot_axes:
        slots *= lax.axis_size(name)
    slot = 0
    for name in slot_axes:
        slot = slot * lax.axis_size(name) + lax.axis_index(name)
    mine = jnp.stack([local_mean, local_m2])
    table = jnp.zeros((slots,) + mine.shape, jnp.float32)
    table = lax.dynamic_update_index_in_dim(table, mine, slot, 0)
    for name in reversed(slot_axes):
        if lax.axis_size(name) == 2:
            table = table + lax.ppermute(table, name, [(0, 1), (1, 0)])
        else:
            table = lax.psum(table, name)
    means = table[:, 0]
    average = jnp.sum(means, axis=0) / slots
    spread = means - average
    m2 = jnp.sum(table[:, 1], axis=0) + count * jnp.sum(spread * spread, axis=0)
    variance = m2 / (count * slots)
    return average, variance


def group_act(values, average, variance, gain, bias):
    frames, rows, local_chan, width = values.shape
    local_groups = average.shape[-1]
    grouped = values.reshape(frames, rows, local_groups, local_chan // local_groups, width)
    centred = grouped - average.reshape(-1, 1, local_groups, 1, 1)
    scaled = (centred * lax.rsqrt(variance.reshape(-1, 1, local_groups, 1, 1) + EPSILON)).reshape(
        frames, rows, local_chan, width
    )
    return jax.nn.silu(scaled * gain[:, None] + bias[:, None]).astype(jnp.bfloat16)


def in_order(own, other, chan_index):
    size = own.shape[2]
    joined = jnp.zeros(own.shape[:2] + (2 * size,) + own.shape[3:], own.dtype)
    joined = lax.dynamic_update_slice_in_dim(joined, own, chan_index * size, axis=2)
    return lax.dynamic_update_slice_in_dim(joined, other, (1 - chan_index) * size, axis=2)


STEP = 18


def pair(ref, first):
    return jnp.concatenate([ref[0, first + k] for k in range(STEP)], axis=1)


def spatial_kernel(xo_ref, xt_ref, wo_ref, wt_ref, res_ref, b_ref, early_ref, o_ref):
    rows, local_chan, width = o_ref.shape[1], o_ref.shape[2], o_ref.shape[3]
    lane = lax.broadcasted_iota(jnp.int32, (local_chan, width), 1)
    bias = b_ref[...]

    def two_rows(i, carry):
        r = STEP * i
        y = jnp.dot(wo_ref[0], pair(xo_ref, r), preferred_element_type=jnp.float32)
        y = y + jnp.dot(wt_ref[0], pair(xt_ref, r), preferred_element_type=jnp.float32)
        for tap in (1, 2):
            y = y + jnp.dot(wo_ref[tap], pair(xo_ref, r + tap), preferred_element_type=jnp.float32)
            y = y + jnp.dot(wt_ref[tap], pair(xt_ref, r + tap), preferred_element_type=jnp.float32)
        for half in range(STEP):
            part = y[:, half * width : (half + 1) * width]
            left = pltpu.roll(part[:local_chan], 1, 1)
            left = jnp.where(lane == 0, 0.0, left)
            right = pltpu.roll(part[2 * local_chan :], width - 1, 1)
            right = jnp.where(lane == width - 1, 0.0, right)
            total = left + part[local_chan : 2 * local_chan] + right
            o_ref[0, r + half] = (res_ref[0, r + half].astype(jnp.float32) + total + bias).astype(
                o_ref.dtype
            )
        return carry

    lax.fori_loop(0, rows // STEP, two_rows, 0, unroll=True)


def spatial_call(own, other, weight_own, weight_other, residual, bias, early):
    frames, rows, local_chan, width = residual.shape
    act_spec = pl.BlockSpec((1, rows + 2, local_chan, width), lambda f: (f, 0, 0, 0))
    weight_spec = pl.BlockSpec((3, 3 * local_chan, local_chan), lambda f: (0, 0, 0))
    return pl.pallas_call(
        spatial_kernel,
        out_shape=jax.ShapeDtypeStruct(residual.shape, jnp.bfloat16),
        grid=(frames,),
        in_specs=[
            act_spec,
            act_spec,
            weight_spec,
            weight_spec,
            pl.BlockSpec((1, rows, local_chan, width), lambda f: (f, 0, 0, 0)),
            pl.BlockSpec((local_chan, 1), lambda f: (0, 0)),
            pl.BlockSpec(memory_space=pl.ANY),
        ],
        out_specs=pl.BlockSpec((1, rows, local_chan, width), lambda f: (f, 0, 0, 0)),
        compiler_params=pltpu.CompilerParams(vmem_limit_bytes=48 * 1024 * 1024),
        cost_estimate=pl.CostEstimate(
            flops=2 * frames * rows * width * 18 * local_chan * local_chan,
            transcendentals=0,
            bytes_accessed=4 * own.size + 4 * weight_own.size + 4 * residual.size,
        ),
    )(own, other, weight_own, weight_other, residual, bias, early)


def temporal_kernel(*refs):
    own_refs, other_refs = refs[0:3], refs[3:6]
    wo_ref, wt_ref, res_ref, bias_ref, o_ref = refs[6:]
    rows, width = o_ref.shape[1], o_ref.shape[3]
    bias = bias_ref[...]

    def two_rows(i, carry):
        r = STEP * i
        y = jnp.dot(wo_ref[0], pair(own_refs[0], r), preferred_element_type=jnp.float32)
        y = y + jnp.dot(wt_ref[0], pair(other_refs[0], r), preferred_element_type=jnp.float32)
        for tap in (1, 2):
            y = y + jnp.dot(wo_ref[tap], pair(own_refs[tap], r), preferred_element_type=jnp.float32)
            y = y + jnp.dot(wt_ref[tap], pair(other_refs[tap], r), preferred_element_type=jnp.float32)
        for half in range(STEP):
            part = y[:, half * width : (half + 1) * width]
            o_ref[0, r + half] = (res_ref[0, r + half].astype(jnp.float32) + part + bias).astype(
                o_ref.dtype
            )
        return carry

    lax.fori_loop(0, rows // STEP, two_rows, 0, unroll=True)


def frame_spec(tap, rows, chans, width):
    return pl.BlockSpec((1, rows, chans, width), lambda f: (f + tap, 0, 0, 0))


def temporal_call(own, other, weight_own, weight_other, residual, bias):
    frames, rows, local_chan, width = residual.shape
    taps = [frame_spec(tap, rows, local_chan, width) for tap in range(3)]
    weight_spec = pl.BlockSpec((3, local_chan, local_chan), lambda f: (0, 0, 0))
    return pl.pallas_call(
        temporal_kernel,
        out_shape=jax.ShapeDtypeStruct(residual.shape, jnp.bfloat16),
        grid=(frames,),
        in_specs=taps
        + taps
        + [
            weight_spec,
            weight_spec,
            pl.BlockSpec((1, rows, local_chan, width), lambda f: (f, 0, 0, 0)),
            pl.BlockSpec((local_chan, 1), lambda f: (0, 0)),
        ],
        out_specs=pl.BlockSpec((1, rows, local_chan, width), lambda f: (f, 0, 0, 0)),
        compiler_params=pltpu.CompilerParams(vmem_limit_bytes=48 * 1024 * 1024),
        cost_estimate=pl.CostEstimate(
            flops=2 * frames * rows * width * 6 * local_chan * local_chan,
            transcendentals=0,
            bytes_accessed=12 * residual.size + 4 * weight_own.size + 4 * residual.size,
        ),
    )(own, own, own, other, other, other, weight_own, weight_other, residual, bias)


def spatial_taps(running, channel_slab, weight, rows, width):
    for row_tap in range(3):
        for col_tap in range(3):
            window = channel_slab[:, row_tap : row_tap + rows, :, col_tap : col_tap + width]
            running = running + jnp.einsum(
                "frcw,co->frow", window, weight[row_tap, col_tap], preferred_element_type=jnp.float32
            )
    return running


def temporal_taps(running, channel_slab, weight, frames):
    for frame_tap in range(3):
        window = channel_slab[frame_tap : frame_tap + frames]
        running = running + jnp.einsum(
            "frcw,co->frow", window, weight[frame_tap], preferred_element_type=jnp.float32
        )
    return running


def body(
    video,
    norm1_gain,
    norm1_bias,
    spatial_weight,
    spatial_bias,
    norm2_gain,
    norm2_bias,
    temporal_weight,
    temporal_bias,
):
    frames, rows, local_chan, width = video.shape
    group_size = C // GROUPS
    local_groups = local_chan // group_size
    chan_index = lax.axis_index("chan")
    tm_index = lax.axis_index("tm")
    tm_count = lax.axis_size("tm")

    spatial_full = lax.all_gather(spatial_weight, "tm", axis=2, tiled=True).reshape(9, C, local_chan)
    temporal_pieces = gather_tm(temporal_weight)
    temporal_full = jnp.moveaxis(temporal_pieces, 0, 1).reshape(3, C, local_chan)
    spatial_full = spatial_full.reshape(3, 3, C, local_chan)

    values = video.astype(jnp.float32)
    grouped = values.reshape(frames, rows, local_groups, group_size, width)
    average, variance = group_stats(grouped, (1, 3, 4), ("height",))
    act_one = group_act(values, average, variance, norm1_gain, norm1_bias)

    with_rows = row_halo(act_one)
    own_start = chan_index * local_chan
    other_start = (1 - chan_index) * local_chan
    spatial_rows = jnp.transpose(spatial_full, (0, 1, 3, 2)).reshape(3, 3 * local_chan, C)
    hidden = spatial_call(
        with_rows,
        swap_chan(with_rows),
        lax.dynamic_slice_in_dim(spatial_rows, own_start, local_chan, axis=2),
        lax.dynamic_slice_in_dim(spatial_rows, other_start, local_chan, axis=2),
        video,
        spatial_bias[:, None],
        temporal_pieces,
    )

    forward = [(i, i + 1) for i in range(tm_count - 1)]
    backward = [(target, source) for source, target in forward]
    before = lax.ppermute(hidden[-1:], "tm", forward)
    after = lax.ppermute(hidden[:1], "tm", backward)

    hidden_values = hidden.astype(jnp.float32)
    grouped_two = hidden_values.reshape(frames, rows, local_groups, group_size, width)
    average_two, variance_two = group_stats(grouped_two, (0, 1, 3, 4), ("tm", "height"))

    extended = jnp.concatenate([before, hidden, after], axis=0).astype(jnp.float32)
    act_two = group_act(extended, average_two, variance_two, norm2_gain, norm2_bias)
    frame_ids = jnp.arange(frames + 2)
    inside = (frame_ids > 0) | (tm_index > 0)
    inside = inside & ((frame_ids < frames + 1) | (tm_index < tm_count - 1))
    act_two = jnp.where(inside[:, None, None, None], act_two, jnp.zeros_like(act_two))

    temporal_rows = jnp.transpose(temporal_full, (0, 2, 1))
    return temporal_call(
        act_two,
        swap_chan(act_two),
        lax.dynamic_slice_in_dim(temporal_rows, own_start, local_chan, axis=2),
        lax.dynamic_slice_in_dim(temporal_rows, other_start, local_chan, axis=2),
        hidden,
        temporal_bias[:, None],
    )


def solution(mesh):
    return jax.shard_map(
        body,
        mesh=mesh,
        in_specs=(
            P(("groups", "tm"), "height", "chan", None),
            P("chan"),
            P("chan"),
            P(None, None, "tm", "chan"),
            P("chan"),
            P("chan"),
            P("chan"),
            P(None, "tm", "chan"),
            P("chan"),
        ),
        out_specs=P(("groups", "tm"), "height", "chan", None),
        check_vma=False,
    )
```

```python
import jax
import jax.numpy as jnp
from jax import lax
from jax.experimental import pallas as pl
from jax.experimental.pallas import tpu as pltpu
from jax.sharding import PartitionSpec as P

C = 320
GROUPS = 32


EPSILON = 1e-06


def swap_chan(block):
    return lax.ppermute(block, "chan", [(0, 1), (1, 0)])


def row_halo(block):
    count = lax.axis_size("height")
    if count == 2:
        index = lax.axis_index("height")
        edge = jnp.where(index == 0, block[:, -1:], block[:, :1])
        received = lax.ppermute(edge, "height", [(0, 1), (1, 0)])
        empty = jnp.zeros_like(received)
        low = jnp.where(index == 1, received, empty)
        high = jnp.where(index == 0, received, empty)
        return jnp.concatenate([low, block, high], axis=1)
    forward = [(i, i + 1) for i in range(count - 1)]
    backward = [(target, source) for source, target in forward]
    low = lax.ppermute(block[:, -1:], "height", forward)
    high = lax.ppermute(block[:, :1], "height", backward)
    return jnp.concatenate([low, block, high], axis=1)


def gather_tm(piece):
    count = lax.axis_size("tm")
    index = lax.axis_index("tm")
    pieces = [piece]
    for shift in range(1, count):
        pairs = [(i, (i - shift) % count) for i in range(count)]
        pieces.append(lax.ppermute(piece, "tm", pairs))
    stacked = jnp.roll(jnp.stack(pieces), index, axis=0)
    return stacked


def group_stats(grouped, axes, slot_axes):
    count = 1
    for axis in axes:
        count *= grouped.shape[axis]
    local_mean = jnp.sum(grouped, axis=axes) / count
    centred = grouped - jnp.expand_dims(local_mean, axes)
    local_m2 = jnp.sum(centred * centred, axis=axes)
    slots = 1
    for name in slot_axes:
        slots *= lax.axis_size(name)
    slot = 0
    for name in slot_axes:
        slot = slot * lax.axis_size(name) + lax.axis_index(name)
    mine = jnp.stack([local_mean, local_m2])
    table = jnp.zeros((slots,) + mine.shape, jnp.float32)
    table = lax.dynamic_update_index_in_dim(table, mine, slot, 0)
    for name in reversed(slot_axes):
        if lax.axis_size(name) == 2:
            table = table + lax.ppermute(table, name, [(0, 1), (1, 0)])
        else:
            table = lax.psum(table, name)
    means = table[:, 0]
    average = jnp.sum(means, axis=0) / slots
    spread = means - average
    m2 = jnp.sum(table[:, 1], axis=0) + count * jnp.sum(spread * spread, axis=0)
    variance = m2 / (count * slots)
    return average, variance


def group_act(values, average, variance, gain, bias):
    frames, rows, local_chan, width = values.shape
    local_groups = average.shape[-1]
    grouped = values.reshape(frames, rows, local_groups, local_chan // local_groups, width)
    centred = grouped - average.reshape(-1, 1, local_groups, 1, 1)
    scaled = (centred * lax.rsqrt(variance.reshape(-1, 1, local_groups, 1, 1) + EPSILON)).reshape(
        frames, rows, local_chan, width
    )
    return jax.nn.silu(scaled * gain[:, None] + bias[:, None]).astype(jnp.bfloat16)


def in_order(own, other, chan_index):
    size = own.shape[2]
    joined = jnp.zeros(own.shape[:2] + (2 * size,) + own.shape[3:], own.dtype)
    joined = lax.dynamic_update_slice_in_dim(joined, own, chan_index * size, axis=2)
    return lax.dynamic_update_slice_in_dim(joined, other, (1 - chan_index) * size, axis=2)


STEP = 12


def pair(ref, first):
    return jnp.concatenate([ref[0, first + k] for k in range(STEP)], axis=1)


def spatial_kernel(xo_ref, xt_ref, wo_ref, wt_ref, res_ref, b_ref, early_ref, o_ref):
    rows, local_chan, width = o_ref.shape[1], o_ref.shape[2], o_ref.shape[3]
    lane = lax.broadcasted_iota(jnp.int32, (local_chan, width), 1)
    bias = b_ref[...]

    def two_rows(i, carry):
        r = STEP * i
        y = jnp.dot(wo_ref[0], pair(xo_ref, r), preferred_element_type=jnp.float32)
        y = y + jnp.dot(wt_ref[0], pair(xt_ref, r), preferred_element_type=jnp.float32)
        for tap in (1, 2):
            y = y + jnp.dot(wo_ref[tap], pair(xo_ref, r + tap), preferred_element_type=jnp.float32)
            y = y + jnp.dot(wt_ref[tap], pair(xt_ref, r + tap), preferred_element_type=jnp.float32)
        for half in range(STEP):
            part = y[:, half * width : (half + 1) * width]
            left = pltpu.roll(part[:local_chan], 1, 1)
            left = jnp.where(lane == 0, 0.0, left)
            right = pltpu.roll(part[2 * local_chan :], width - 1, 1)
            right = jnp.where(lane == width - 1, 0.0, right)
            total = left + part[local_chan : 2 * local_chan] + right
            o_ref[0, r + half] = (res_ref[0, r + half].astype(jnp.float32) + total + bias).astype(
                o_ref.dtype
            )
        return carry

    lax.fori_loop(0, rows // STEP, two_rows, 0, unroll=True)


def spatial_call(own, other, weight_own, weight_other, residual, bias, early):
    frames, rows, local_chan, width = residual.shape
    act_spec = pl.BlockSpec((1, rows + 2, local_chan, width), lambda f: (f, 0, 0, 0))
    weight_spec = pl.BlockSpec((3, 3 * local_chan, local_chan), lambda f: (0, 0, 0))
    return pl.pallas_call(
        spatial_kernel,
        out_shape=jax.ShapeDtypeStruct(residual.shape, jnp.bfloat16),
        grid=(frames,),
        in_specs=[
            act_spec,
            act_spec,
            weight_spec,
            weight_spec,
            pl.BlockSpec((1, rows, local_chan, width), lambda f: (f, 0, 0, 0)),
            pl.BlockSpec((local_chan, 1), lambda f: (0, 0)),
            pl.BlockSpec(memory_space=pl.ANY),
        ],
        out_specs=pl.BlockSpec((1, rows, local_chan, width), lambda f: (f, 0, 0, 0)),
        compiler_params=pltpu.CompilerParams(vmem_limit_bytes=48 * 1024 * 1024),
        cost_estimate=pl.CostEstimate(
            flops=2 * frames * rows * width * 18 * local_chan * local_chan,
            transcendentals=0,
            bytes_accessed=4 * own.size + 4 * weight_own.size + 4 * residual.size,
        ),
    )(own, other, weight_own, weight_other, residual, bias, early)


def temporal_kernel(*refs):
    own_refs, other_refs = refs[0:3], refs[3:6]
    wo_ref, wt_ref, res_ref, bias_ref, o_ref = refs[6:]
    rows, width = o_ref.shape[1], o_ref.shape[3]
    bias = bias_ref[...]

    def two_rows(i, carry):
        r = STEP * i
        y = jnp.dot(wo_ref[0], pair(own_refs[0], r), preferred_element_type=jnp.float32)
        y = y + jnp.dot(wt_ref[0], pair(other_refs[0], r), preferred_element_type=jnp.float32)
        for tap in (1, 2):
            y = y + jnp.dot(wo_ref[tap], pair(own_refs[tap], r), preferred_element_type=jnp.float32)
            y = y + jnp.dot(wt_ref[tap], pair(other_refs[tap], r), preferred_element_type=jnp.float32)
        for half in range(STEP):
            part = y[:, half * width : (half + 1) * width]
            o_ref[0, r + half] = (res_ref[0, r + half].astype(jnp.float32) + part + bias).astype(
                o_ref.dtype
            )
        return carry

    lax.fori_loop(0, rows // STEP, two_rows, 0, unroll=True)


def frame_spec(tap, rows, chans, width):
    return pl.BlockSpec((1, rows, chans, width), lambda f: (f + tap, 0, 0, 0))


def temporal_call(own, other, weight_own, weight_other, residual, bias):
    frames, rows, local_chan, width = residual.shape
    taps = [frame_spec(tap, rows, local_chan, width) for tap in range(3)]
    weight_spec = pl.BlockSpec((3, local_chan, local_chan), lambda f: (0, 0, 0))
    return pl.pallas_call(
        temporal_kernel,
        out_shape=jax.ShapeDtypeStruct(residual.shape, jnp.bfloat16),
        grid=(frames,),
        in_specs=taps
        + taps
        + [
            weight_spec,
            weight_spec,
            pl.BlockSpec((1, rows, local_chan, width), lambda f: (f, 0, 0, 0)),
            pl.BlockSpec((local_chan, 1), lambda f: (0, 0)),
        ],
        out_specs=pl.BlockSpec((1, rows, local_chan, width), lambda f: (f, 0, 0, 0)),
        compiler_params=pltpu.CompilerParams(vmem_limit_bytes=48 * 1024 * 1024),
        cost_estimate=pl.CostEstimate(
            flops=2 * frames * rows * width * 6 * local_chan * local_chan,
            transcendentals=0,
            bytes_accessed=12 * residual.size + 4 * weight_own.size + 4 * residual.size,
        ),
    )(own, own, own, other, other, other, weight_own, weight_other, residual, bias)


def spatial_taps(running, channel_slab, weight, rows, width):
    for row_tap in range(3):
        for col_tap in range(3):
            window = channel_slab[:, row_tap : row_tap + rows, :, col_tap : col_tap + width]
            running = running + jnp.einsum(
                "frcw,co->frow", window, weight[row_tap, col_tap], preferred_element_type=jnp.float32
            )
    return running


def temporal_taps(running, channel_slab, weight, frames):
    for frame_tap in range(3):
        window = channel_slab[frame_tap : frame_tap + frames]
        running = running + jnp.einsum(
            "frcw,co->frow", window, weight[frame_tap], preferred_element_type=jnp.float32
        )
    return running


def body(
    video,
    norm1_gain,
    norm1_bias,
    spatial_weight,
    spatial_bias,
    norm2_gain,
    norm2_bias,
    temporal_weight,
    temporal_bias,
):
    frames, rows, local_chan, width = video.shape
    group_size = C // GROUPS
    local_groups = local_chan // group_size
    chan_index = lax.axis_index("chan")
    tm_index = lax.axis_index("tm")
    tm_count = lax.axis_size("tm")

    spatial_full = lax.all_gather(spatial_weight, "tm", axis=2, tiled=True).reshape(9, C, local_chan)
    temporal_pieces = gather_tm(temporal_weight)
    temporal_full = jnp.moveaxis(temporal_pieces, 0, 1).reshape(3, C, local_chan)
    spatial_full = spatial_full.reshape(3, 3, C, local_chan)

    values = video.astype(jnp.float32)
    grouped = values.reshape(frames, rows, local_groups, group_size, width)
    average, variance = group_stats(grouped, (1, 3, 4), ("height",))
    act_one = group_act(values, average, variance, norm1_gain, norm1_bias)

    with_rows = row_halo(act_one)
    own_start = chan_index * local_chan
    other_start = (1 - chan_index) * local_chan
    spatial_rows = jnp.transpose(spatial_full, (0, 1, 3, 2)).reshape(3, 3 * local_chan, C)
    hidden = spatial_call(
        with_rows,
        swap_chan(with_rows),
        lax.dynamic_slice_in_dim(spatial_rows, own_start, local_chan, axis=2),
        lax.dynamic_slice_in_dim(spatial_rows, other_start, local_chan, axis=2),
        video,
        spatial_bias[:, None],
        temporal_pieces,
    )

    forward = [(i, i + 1) for i in range(tm_count - 1)]
    backward = [(target, source) for source, target in forward]
    before = lax.ppermute(hidden[-1:], "tm", forward)
    after = lax.ppermute(hidden[:1], "tm", backward)

    hidden_values = hidden.astype(jnp.float32)
    grouped_two = hidden_values.reshape(frames, rows, local_groups, group_size, width)
    average_two, variance_two = group_stats(grouped_two, (0, 1, 3, 4), ("tm", "height"))

    extended = jnp.concatenate([before, hidden, after], axis=0).astype(jnp.float32)
    act_two = group_act(extended, average_two, variance_two, norm2_gain, norm2_bias)
    frame_ids = jnp.arange(frames + 2)
    inside = (frame_ids > 0) | (tm_index > 0)
    inside = inside & ((frame_ids < frames + 1) | (tm_index < tm_count - 1))
    act_two = jnp.where(inside[:, None, None, None], act_two, jnp.zeros_like(act_two))

    temporal_rows = jnp.transpose(temporal_full, (0, 2, 1))
    return temporal_call(
        act_two,
        swap_chan(act_two),
        lax.dynamic_slice_in_dim(temporal_rows, own_start, local_chan, axis=2),
        lax.dynamic_slice_in_dim(temporal_rows, other_start, local_chan, axis=2),
        hidden,
        temporal_bias[:, None],
    )


def solution(mesh):
    return jax.shard_map(
        body,
        mesh=mesh,
        in_specs=(
            P(("groups", "tm"), "height", "chan", None),
            P("chan"),
            P("chan"),
            P(None, None, "tm", "chan"),
            P("chan"),
            P("chan"),
            P("chan"),
            P(None, "tm", "chan"),
            P("chan"),
        ),
        out_specs=P(("groups", "tm"), "height", "chan", None),
        check_vma=False,
    )
```

```python
import jax
import jax.numpy as jnp
from jax import lax
from jax.experimental import pallas as pl
from jax.experimental.pallas import tpu as pltpu
from jax.sharding import PartitionSpec as P

C = 320
GROUPS = 32


EPSILON = 1e-06


def swap_chan(block):
    return lax.ppermute(block, "chan", [(0, 1), (1, 0)])


def row_halo(block):
    count = lax.axis_size("height")
    if count == 2:
        index = lax.axis_index("height")
        edge = jnp.where(index == 0, block[:, -1:], block[:, :1])
        received = lax.ppermute(edge, "height", [(0, 1), (1, 0)])
        empty = jnp.zeros_like(received)
        low = jnp.where(index == 1, received, empty)
        high = jnp.where(index == 0, received, empty)
        return jnp.concatenate([low, block, high], axis=1)
    forward = [(i, i + 1) for i in range(count - 1)]
    backward = [(target, source) for source, target in forward]
    low = lax.ppermute(block[:, -1:], "height", forward)
    high = lax.ppermute(block[:, :1], "height", backward)
    return jnp.concatenate([low, block, high], axis=1)


def gather_tm(piece):
    count = lax.axis_size("tm")
    index = lax.axis_index("tm")
    pieces = [piece]
    for shift in range(1, count):
        pairs = [(i, (i - shift) % count) for i in range(count)]
        pieces.append(lax.ppermute(piece, "tm", pairs))
    stacked = jnp.roll(jnp.stack(pieces), index, axis=0)
    return stacked


def group_stats(grouped, axes, slot_axes):
    count = 1
    for axis in axes:
        count *= grouped.shape[axis]
    local_mean = jnp.sum(grouped, axis=axes) / count
    centred = grouped - jnp.expand_dims(local_mean, axes)
    local_m2 = jnp.sum(centred * centred, axis=axes)
    slots = 1
    for name in slot_axes:
        slots *= lax.axis_size(name)
    slot = 0
    for name in slot_axes:
        slot = slot * lax.axis_size(name) + lax.axis_index(name)
    mine = jnp.stack([local_mean, local_m2])
    table = jnp.zeros((slots,) + mine.shape, jnp.float32)
    table = lax.dynamic_update_index_in_dim(table, mine, slot, 0)
    for name in reversed(slot_axes):
        if lax.axis_size(name) == 2:
            table = table + lax.ppermute(table, name, [(0, 1), (1, 0)])
        else:
            table = lax.psum(table, name)
    means = table[:, 0]
    average = jnp.sum(means, axis=0) / slots
    spread = means - average
    m2 = jnp.sum(table[:, 1], axis=0) + count * jnp.sum(spread * spread, axis=0)
    variance = m2 / (count * slots)
    return average, variance


def group_act(values, average, variance, gain, bias):
    frames, rows, local_chan, width = values.shape
    local_groups = average.shape[-1]
    grouped = values.reshape(frames, rows, local_groups, local_chan // local_groups, width)
    centred = grouped - average.reshape(-1, 1, local_groups, 1, 1)
    scaled = (centred * lax.rsqrt(variance.reshape(-1, 1, local_groups, 1, 1) + EPSILON)).reshape(
        frames, rows, local_chan, width
    )
    return jax.nn.silu(scaled * gain[:, None] + bias[:, None]).astype(jnp.bfloat16)


def in_order(own, other, chan_index):
    size = own.shape[2]
    joined = jnp.zeros(own.shape[:2] + (2 * size,) + own.shape[3:], own.dtype)
    joined = lax.dynamic_update_slice_in_dim(joined, own, chan_index * size, axis=2)
    return lax.dynamic_update_slice_in_dim(joined, other, (1 - chan_index) * size, axis=2)


STEP = 6


def pair(ref, first):
    return jnp.concatenate([ref[0, first + k] for k in range(STEP)], axis=1)


def spatial_kernel(xo_ref, xt_ref, wo_ref, wt_ref, res_ref, b_ref, early_ref, o_ref):
    rows, local_chan, width = o_ref.shape[1], o_ref.shape[2], o_ref.shape[3]
    lane = lax.broadcasted_iota(jnp.int32, (local_chan, width), 1)
    bias = b_ref[...]

    def two_rows(i, carry):
        r = STEP * i
        y = jnp.dot(wo_ref[0], pair(xo_ref, r), preferred_element_type=jnp.float32)
        y = y + jnp.dot(wt_ref[0], pair(xt_ref, r), preferred_element_type=jnp.float32)
        for tap in (1, 2):
            y = y + jnp.dot(wo_ref[tap], pair(xo_ref, r + tap), preferred_element_type=jnp.float32)
            y = y + jnp.dot(wt_ref[tap], pair(xt_ref, r + tap), preferred_element_type=jnp.float32)
        for half in range(STEP):
            part = y[:, half * width : (half + 1) * width]
            left = pltpu.roll(part[:local_chan], 1, 1)
            left = jnp.where(lane == 0, 0.0, left)
            right = pltpu.roll(part[2 * local_chan :], width - 1, 1)
            right = jnp.where(lane == width - 1, 0.0, right)
            total = left + part[local_chan : 2 * local_chan] + right
            o_ref[0, r + half] = (res_ref[0, r + half].astype(jnp.float32) + total + bias).astype(
                o_ref.dtype
            )
        return carry

    lax.fori_loop(0, rows // STEP, two_rows, 0, unroll=True)


def spatial_call(own, other, weight_own, weight_other, residual, bias, early):
    frames, rows, local_chan, width = residual.shape
    act_spec = pl.BlockSpec((1, rows + 2, local_chan, width), lambda f: (f, 0, 0, 0))
    weight_spec = pl.BlockSpec((3, 3 * local_chan, local_chan), lambda f: (0, 0, 0))
    return pl.pallas_call(
        spatial_kernel,
        out_shape=jax.ShapeDtypeStruct(residual.shape, jnp.bfloat16),
        grid=(frames,),
        in_specs=[
            act_spec,
            act_spec,
            weight_spec,
            weight_spec,
            pl.BlockSpec((1, rows, local_chan, width), lambda f: (f, 0, 0, 0)),
            pl.BlockSpec((local_chan, 1), lambda f: (0, 0)),
            pl.BlockSpec(memory_space=pl.ANY),
        ],
        out_specs=pl.BlockSpec((1, rows, local_chan, width), lambda f: (f, 0, 0, 0)),
        compiler_params=pltpu.CompilerParams(vmem_limit_bytes=48 * 1024 * 1024),
        cost_estimate=pl.CostEstimate(
            flops=2 * frames * rows * width * 18 * local_chan * local_chan,
            transcendentals=0,
            bytes_accessed=4 * own.size + 4 * weight_own.size + 4 * residual.size,
        ),
    )(own, other, weight_own, weight_other, residual, bias, early)


def temporal_kernel(*refs):
    own_refs, other_refs = refs[0:3], refs[3:6]
    wo_ref, wt_ref, res_ref, bias_ref, o_ref = refs[6:]
    rows, width = o_ref.shape[1], o_ref.shape[3]
    bias = bias_ref[...]

    def two_rows(i, carry):
        r = STEP * i
        y = jnp.dot(wo_ref[0], pair(own_refs[0], r), preferred_element_type=jnp.float32)
        y = y + jnp.dot(wt_ref[0], pair(other_refs[0], r), preferred_element_type=jnp.float32)
        for tap in (1, 2):
            y = y + jnp.dot(wo_ref[tap], pair(own_refs[tap], r), preferred_element_type=jnp.float32)
            y = y + jnp.dot(wt_ref[tap], pair(other_refs[tap], r), preferred_element_type=jnp.float32)
        for half in range(STEP):
            part = y[:, half * width : (half + 1) * width]
            o_ref[0, r + half] = (res_ref[0, r + half].astype(jnp.float32) + part + bias).astype(
                o_ref.dtype
            )
        return carry

    lax.fori_loop(0, rows // STEP, two_rows, 0, unroll=True)


def frame_spec(tap, rows, chans, width):
    return pl.BlockSpec((1, rows, chans, width), lambda f: (f + tap, 0, 0, 0))


def temporal_call(own, other, weight_own, weight_other, residual, bias):
    frames, rows, local_chan, width = residual.shape
    taps = [frame_spec(tap, rows, local_chan, width) for tap in range(3)]
    weight_spec = pl.BlockSpec((3, local_chan, local_chan), lambda f: (0, 0, 0))
    return pl.pallas_call(
        temporal_kernel,
        out_shape=jax.ShapeDtypeStruct(residual.shape, jnp.bfloat16),
        grid=(frames,),
        in_specs=taps
        + taps
        + [
            weight_spec,
            weight_spec,
            pl.BlockSpec((1, rows, local_chan, width), lambda f: (f, 0, 0, 0)),
            pl.BlockSpec((local_chan, 1), lambda f: (0, 0)),
        ],
        out_specs=pl.BlockSpec((1, rows, local_chan, width), lambda f: (f, 0, 0, 0)),
        compiler_params=pltpu.CompilerParams(vmem_limit_bytes=48 * 1024 * 1024),
        cost_estimate=pl.CostEstimate(
            flops=2 * frames * rows * width * 6 * local_chan * local_chan,
            transcendentals=0,
            bytes_accessed=12 * residual.size + 4 * weight_own.size + 4 * residual.size,
        ),
    )(own, own, own, other, other, other, weight_own, weight_other, residual, bias)


def spatial_taps(running, channel_slab, weight, rows, width):
    for row_tap in range(3):
        for col_tap in range(3):
            window = channel_slab[:, row_tap : row_tap + rows, :, col_tap : col_tap + width]
            running = running + jnp.einsum(
                "frcw,co->frow", window, weight[row_tap, col_tap], preferred_element_type=jnp.float32
            )
    return running


def temporal_taps(running, channel_slab, weight, frames):
    for frame_tap in range(3):
        window = channel_slab[frame_tap : frame_tap + frames]
        running = running + jnp.einsum(
            "frcw,co->frow", window, weight[frame_tap], preferred_element_type=jnp.float32
        )
    return running


def body(
    video,
    norm1_gain,
    norm1_bias,
    spatial_weight,
    spatial_bias,
    norm2_gain,
    norm2_bias,
    temporal_weight,
    temporal_bias,
):
    frames, rows, local_chan, width = video.shape
    group_size = C // GROUPS
    local_groups = local_chan // group_size
    chan_index = lax.axis_index("chan")
    tm_index = lax.axis_index("tm")
    tm_count = lax.axis_size("tm")

    spatial_full = lax.all_gather(spatial_weight, "tm", axis=2, tiled=True).reshape(9, C, local_chan)
    temporal_pieces = gather_tm(temporal_weight)
    temporal_full = jnp.moveaxis(temporal_pieces, 0, 1).reshape(3, C, local_chan)
    spatial_full = spatial_full.reshape(3, 3, C, local_chan)

    values = video.astype(jnp.float32)
    grouped = values.reshape(frames, rows, local_groups, group_size, width)
    average, variance = group_stats(grouped, (1, 3, 4), ("height",))
    act_one = group_act(values, average, variance, norm1_gain, norm1_bias)

    with_rows = row_halo(act_one)
    own_start = chan_index * local_chan
    other_start = (1 - chan_index) * local_chan
    spatial_rows = jnp.transpose(spatial_full, (0, 1, 3, 2)).reshape(3, 3 * local_chan, C)
    hidden = spatial_call(
        with_rows,
        swap_chan(with_rows),
        lax.dynamic_slice_in_dim(spatial_rows, own_start, local_chan, axis=2),
        lax.dynamic_slice_in_dim(spatial_rows, other_start, local_chan, axis=2),
        video,
        spatial_bias[:, None],
        temporal_pieces,
    )

    forward = [(i, i + 1) for i in range(tm_count - 1)]
    backward = [(target, source) for source, target in forward]
    before = lax.ppermute(hidden[-1:], "tm", forward)
    after = lax.ppermute(hidden[:1], "tm", backward)

    hidden_values = hidden.astype(jnp.float32)
    grouped_two = hidden_values.reshape(frames, rows, local_groups, group_size, width)
    average_two, variance_two = group_stats(grouped_two, (0, 1, 3, 4), ("tm", "height"))

    extended = jnp.concatenate([before, hidden, after], axis=0).astype(jnp.float32)
    act_two = group_act(extended, average_two, variance_two, norm2_gain, norm2_bias)
    frame_ids = jnp.arange(frames + 2)
    inside = (frame_ids > 0) | (tm_index > 0)
    inside = inside & ((frame_ids < frames + 1) | (tm_index < tm_count - 1))
    act_two = jnp.where(inside[:, None, None, None], act_two, jnp.zeros_like(act_two))

    temporal_rows = jnp.transpose(temporal_full, (0, 2, 1))
    return temporal_call(
        act_two,
        swap_chan(act_two),
        lax.dynamic_slice_in_dim(temporal_rows, own_start, local_chan, axis=2),
        lax.dynamic_slice_in_dim(temporal_rows, other_start, local_chan, axis=2),
        hidden,
        temporal_bias[:, None],
    )


def solution(mesh):
    return jax.shard_map(
        body,
        mesh=mesh,
        in_specs=(
            P(("groups", "tm"), "height", "chan", None),
            P("chan"),
            P("chan"),
            P(None, None, "tm", "chan"),
            P("chan"),
            P("chan"),
            P("chan"),
            P(None, "tm", "chan"),
            P("chan"),
        ),
        out_specs=P(("groups", "tm"), "height", "chan", None),
        check_vma=False,
    )
```

```python
import jax
import jax.numpy as jnp
from jax import lax
from jax.experimental import pallas as pl
from jax.experimental.pallas import tpu as pltpu
from jax.sharding import PartitionSpec as P

C = 320
GROUPS = 32


EPSILON = 1e-06


def swap_chan(block):
    return lax.ppermute(block, "chan", [(0, 1), (1, 0)])


def row_halo(block):
    count = lax.axis_size("height")
    if count == 2:
        index = lax.axis_index("height")
        edge = jnp.where(index == 0, block[:, -1:], block[:, :1])
        received = lax.ppermute(edge, "height", [(0, 1), (1, 0)])
        empty = jnp.zeros_like(received)
        low = jnp.where(index == 1, received, empty)
        high = jnp.where(index == 0, received, empty)
        return jnp.concatenate([low, block, high], axis=1)
    forward = [(i, i + 1) for i in range(count - 1)]
    backward = [(target, source) for source, target in forward]
    low = lax.ppermute(block[:, -1:], "height", forward)
    high = lax.ppermute(block[:, :1], "height", backward)
    return jnp.concatenate([low, block, high], axis=1)


def gather_tm(piece):
    count = lax.axis_size("tm")
    index = lax.axis_index("tm")
    pieces = [piece]
    for shift in range(1, count):
        pairs = [(i, (i - shift) % count) for i in range(count)]
        pieces.append(lax.ppermute(piece, "tm", pairs))
    stacked = jnp.roll(jnp.stack(pieces), index, axis=0)
    return stacked


def group_stats(grouped, axes, slot_axes):
    count = 1
    for axis in axes:
        count *= grouped.shape[axis]
    local_mean = jnp.sum(grouped, axis=axes) / count
    centred = grouped - jnp.expand_dims(local_mean, axes)
    local_m2 = jnp.sum(centred * centred, axis=axes)
    slots = 1
    for name in slot_axes:
        slots *= lax.axis_size(name)
    slot = 0
    for name in slot_axes:
        slot = slot * lax.axis_size(name) + lax.axis_index(name)
    mine = jnp.stack([local_mean, local_m2])
    table = jnp.zeros((slots,) + mine.shape, jnp.float32)
    table = lax.dynamic_update_index_in_dim(table, mine, slot, 0)
    for name in reversed(slot_axes):
        if lax.axis_size(name) == 2:
            table = table + lax.ppermute(table, name, [(0, 1), (1, 0)])
        else:
            table = lax.psum(table, name)
    means = table[:, 0]
    average = jnp.sum(means, axis=0) / slots
    spread = means - average
    m2 = jnp.sum(table[:, 1], axis=0) + count * jnp.sum(spread * spread, axis=0)
    variance = m2 / (count * slots)
    return average, variance


def group_act(values, average, variance, gain, bias):
    frames, rows, local_chan, width = values.shape
    local_groups = average.shape[-1]
    grouped = values.reshape(frames, rows, local_groups, local_chan // local_groups, width)
    centred = grouped - average.reshape(-1, 1, local_groups, 1, 1)
    scaled = (centred * lax.rsqrt(variance.reshape(-1, 1, local_groups, 1, 1) + EPSILON)).reshape(
        frames, rows, local_chan, width
    )
    return jax.nn.silu(scaled * gain[:, None] + bias[:, None]).astype(jnp.bfloat16)


def in_order(own, other, chan_index):
    size = own.shape[2]
    joined = jnp.zeros(own.shape[:2] + (2 * size,) + own.shape[3:], own.dtype)
    joined = lax.dynamic_update_slice_in_dim(joined, own, chan_index * size, axis=2)
    return lax.dynamic_update_slice_in_dim(joined, other, (1 - chan_index) * size, axis=2)


STEP = 12


def pair(ref, first):
    return jnp.concatenate([ref[0, first + k] for k in range(STEP)], axis=1)


def spatial_kernel(xo_ref, xt_ref, wo_ref, wt_ref, res_ref, b_ref, early_ref, o_ref):
    rows, local_chan, width = o_ref.shape[1], o_ref.shape[2], o_ref.shape[3]
    lane = lax.broadcasted_iota(jnp.int32, (local_chan, width), 1)
    bias = b_ref[...]

    def two_rows(i, carry):
        r = STEP * i
        y = jnp.dot(wo_ref[0], pair(xo_ref, r), preferred_element_type=jnp.float32)
        y = y + jnp.dot(wt_ref[0], pair(xt_ref, r), preferred_element_type=jnp.float32)
        for tap in (1, 2):
            y = y + jnp.dot(wo_ref[tap], pair(xo_ref, r + tap), preferred_element_type=jnp.float32)
            y = y + jnp.dot(wt_ref[tap], pair(xt_ref, r + tap), preferred_element_type=jnp.float32)
        for half in range(STEP):
            part = y[:, half * width : (half + 1) * width]
            left = pltpu.roll(part[:local_chan], 1, 1)
            left = jnp.where(lane == 0, 0.0, left)
            right = pltpu.roll(part[2 * local_chan :], width - 1, 1)
            right = jnp.where(lane == width - 1, 0.0, right)
            total = left + part[local_chan : 2 * local_chan] + right
            o_ref[0, r + half] = (res_ref[0, r + half].astype(jnp.float32) + total + bias).astype(
                o_ref.dtype
            )
        return carry

    lax.fori_loop(0, rows // STEP, two_rows, 0, unroll=True)


def spatial_call(own, other, weight_own, weight_other, residual, bias, early):
    frames, rows, local_chan, width = residual.shape
    act_spec = pl.BlockSpec((1, rows + 2, local_chan, width), lambda f: (f, 0, 0, 0))
    weight_spec = pl.BlockSpec((3, 3 * local_chan, local_chan), lambda f: (0, 0, 0))
    return pl.pallas_call(
        spatial_kernel,
        out_shape=jax.ShapeDtypeStruct(residual.shape, jnp.bfloat16),
        grid=(frames,),
        in_specs=[
            act_spec,
            act_spec,
            weight_spec,
            weight_spec,
            pl.BlockSpec((1, rows, local_chan, width), lambda f: (f, 0, 0, 0)),
            pl.BlockSpec((local_chan, 1), lambda f: (0, 0)),
            pl.BlockSpec(memory_space=pl.ANY),
        ],
        out_specs=pl.BlockSpec((1, rows, local_chan, width), lambda f: (f, 0, 0, 0)),
        compiler_params=pltpu.CompilerParams(vmem_limit_bytes=48 * 1024 * 1024),
        cost_estimate=pl.CostEstimate(
            flops=2 * frames * rows * width * 18 * local_chan * local_chan,
            transcendentals=0,
            bytes_accessed=4 * own.size + 4 * weight_own.size + 4 * residual.size,
        ),
    )(own, other, weight_own, weight_other, residual, bias, early)


def temporal_kernel(*refs):
    own_refs, other_refs = refs[0:3], refs[3:6]
    wo_ref, wt_ref, res_ref, bias_ref, o_ref = refs[6:]
    rows, width = o_ref.shape[1], o_ref.shape[3]
    bias = bias_ref[...]

    def two_rows(i, carry):
        r = STEP * i
        y = jnp.dot(wo_ref[0], pair(own_refs[0], r), preferred_element_type=jnp.float32)
        y = y + jnp.dot(wt_ref[0], pair(other_refs[0], r), preferred_element_type=jnp.float32)
        for tap in (1, 2):
            y = y + jnp.dot(wo_ref[tap], pair(own_refs[tap], r), preferred_element_type=jnp.float32)
            y = y + jnp.dot(wt_ref[tap], pair(other_refs[tap], r), preferred_element_type=jnp.float32)
        for half in range(STEP):
            part = y[:, half * width : (half + 1) * width]
            o_ref[0, r + half] = (res_ref[0, r + half].astype(jnp.float32) + part + bias).astype(
                o_ref.dtype
            )
        return carry

    lax.fori_loop(0, rows // STEP, two_rows, 0, unroll=True)


def frame_spec(tap, rows, chans, width):
    return pl.BlockSpec((1, rows, chans, width), lambda f: (f + tap, 0, 0, 0))


def temporal_call(own, other, weight_own, weight_other, residual, bias):
    frames, rows, local_chan, width = residual.shape
    taps = [frame_spec(tap, rows, local_chan, width) for tap in range(3)]
    weight_spec = pl.BlockSpec((3, local_chan, local_chan), lambda f: (0, 0, 0))
    return pl.pallas_call(
        temporal_kernel,
        out_shape=jax.ShapeDtypeStruct(residual.shape, jnp.bfloat16),
        grid=(frames,),
        in_specs=taps
        + taps
        + [
            weight_spec,
            weight_spec,
            pl.BlockSpec((1, rows, local_chan, width), lambda f: (f, 0, 0, 0)),
            pl.BlockSpec((local_chan, 1), lambda f: (0, 0)),
        ],
        out_specs=pl.BlockSpec((1, rows, local_chan, width), lambda f: (f, 0, 0, 0)),
        compiler_params=pltpu.CompilerParams(vmem_limit_bytes=48 * 1024 * 1024),
        cost_estimate=pl.CostEstimate(
            flops=2 * frames * rows * width * 6 * local_chan * local_chan,
            transcendentals=0,
            bytes_accessed=12 * residual.size + 4 * weight_own.size + 4 * residual.size,
        ),
    )(own, own, own, other, other, other, weight_own, weight_other, residual, bias)


def spatial_taps(running, channel_slab, weight, rows, width):
    for row_tap in range(3):
        for col_tap in range(3):
            window = channel_slab[:, row_tap : row_tap + rows, :, col_tap : col_tap + width]
            running = running + jnp.einsum(
                "frcw,co->frow", window, weight[row_tap, col_tap], preferred_element_type=jnp.float32
            )
    return running


def temporal_taps(running, channel_slab, weight, frames):
    for frame_tap in range(3):
        window = channel_slab[frame_tap : frame_tap + frames]
        running = running + jnp.einsum(
            "frcw,co->frow", window, weight[frame_tap], preferred_element_type=jnp.float32
        )
    return running


def body(
    video,
    norm1_gain,
    norm1_bias,
    spatial_weight,
    spatial_bias,
    norm2_gain,
    norm2_bias,
    temporal_weight,
    temporal_bias,
):
    frames, rows, local_chan, width = video.shape
    group_size = C // GROUPS
    local_groups = local_chan // group_size
    chan_index = lax.axis_index("chan")
    tm_index = lax.axis_index("tm")
    tm_count = lax.axis_size("tm")

    spatial_stack = lax.all_gather(spatial_weight, "tm", axis=0)
    spatial_full = jnp.moveaxis(spatial_stack, 0, 2).reshape(9, C, local_chan)
    temporal_pieces = gather_tm(temporal_weight)
    temporal_full = jnp.moveaxis(temporal_pieces, 0, 1).reshape(3, C, local_chan)
    spatial_full = spatial_full.reshape(3, 3, C, local_chan)

    values = video.astype(jnp.float32)
    grouped = values.reshape(frames, rows, local_groups, group_size, width)
    average, variance = group_stats(grouped, (1, 3, 4), ("height",))
    act_one = group_act(values, average, variance, norm1_gain, norm1_bias)

    with_rows = row_halo(act_one)
    own_start = chan_index * local_chan
    other_start = (1 - chan_index) * local_chan
    spatial_rows = jnp.transpose(spatial_full, (0, 1, 3, 2)).reshape(3, 3 * local_chan, C)
    hidden = spatial_call(
        with_rows,
        swap_chan(with_rows),
        lax.dynamic_slice_in_dim(spatial_rows, own_start, local_chan, axis=2),
        lax.dynamic_slice_in_dim(spatial_rows, other_start, local_chan, axis=2),
        video,
        spatial_bias[:, None],
        temporal_pieces,
    )

    forward = [(i, i + 1) for i in range(tm_count - 1)]
    backward = [(target, source) for source, target in forward]
    before = lax.ppermute(hidden[-1:], "tm", forward)
    after = lax.ppermute(hidden[:1], "tm", backward)

    hidden_values = hidden.astype(jnp.float32)
    grouped_two = hidden_values.reshape(frames, rows, local_groups, group_size, width)
    average_two, variance_two = group_stats(grouped_two, (0, 1, 3, 4), ("tm", "height"))

    extended = jnp.concatenate([before, hidden, after], axis=0).astype(jnp.float32)
    act_two = group_act(extended, average_two, variance_two, norm2_gain, norm2_bias)
    frame_ids = jnp.arange(frames + 2)
    inside = (frame_ids > 0) | (tm_index > 0)
    inside = inside & ((frame_ids < frames + 1) | (tm_index < tm_count - 1))
    act_two = jnp.where(inside[:, None, None, None], act_two, jnp.zeros_like(act_two))

    temporal_rows = jnp.transpose(temporal_full, (0, 2, 1))
    return temporal_call(
        act_two,
        swap_chan(act_two),
        lax.dynamic_slice_in_dim(temporal_rows, own_start, local_chan, axis=2),
        lax.dynamic_slice_in_dim(temporal_rows, other_start, local_chan, axis=2),
        hidden,
        temporal_bias[:, None],
    )


def solution(mesh):
    return jax.shard_map(
        body,
        mesh=mesh,
        in_specs=(
            P(("groups", "tm"), "height", "chan", None),
            P("chan"),
            P("chan"),
            P(None, None, "tm", "chan"),
            P("chan"),
            P("chan"),
            P("chan"),
            P(None, "tm", "chan"),
            P("chan"),
        ),
        out_specs=P(("groups", "tm"), "height", "chan", None),
        check_vma=False,
    )
```

```python
import jax
import jax.numpy as jnp
from jax import lax
from jax.experimental import pallas as pl
from jax.experimental.pallas import tpu as pltpu
from jax.sharding import PartitionSpec as P

C = 320
GROUPS = 32


EPSILON = 1e-06


def swap_chan(block):
    return lax.ppermute(block, "chan", [(0, 1), (1, 0)])


def row_halo(block):
    count = lax.axis_size("height")
    if count == 2:
        index = lax.axis_index("height")
        edge = jnp.where(index == 0, block[:, -1:], block[:, :1])
        received = lax.ppermute(edge, "height", [(0, 1), (1, 0)])
        empty = jnp.zeros_like(received)
        low = jnp.where(index == 1, received, empty)
        high = jnp.where(index == 0, received, empty)
        return jnp.concatenate([low, high], axis=1)
    forward = [(i, i + 1) for i in range(count - 1)]
    backward = [(target, source) for source, target in forward]
    low = lax.ppermute(block[:, -1:], "height", forward)
    high = lax.ppermute(block[:, :1], "height", backward)
    return jnp.concatenate([low, high], axis=1)


def gather_tm(piece):
    count = lax.axis_size("tm")
    index = lax.axis_index("tm")
    pieces = [piece]
    for shift in range(1, count):
        pairs = [(i, (i - shift) % count) for i in range(count)]
        pieces.append(lax.ppermute(piece, "tm", pairs))
    stacked = jnp.roll(jnp.stack(pieces), index, axis=0)
    return stacked


def group_stats(grouped, axes, slot_axes):
    count = 1
    for axis in axes:
        count *= grouped.shape[axis]
    local_mean = jnp.sum(grouped, axis=axes) / count
    centred = grouped - jnp.expand_dims(local_mean, axes)
    local_m2 = jnp.sum(centred * centred, axis=axes)
    slots = 1
    for name in slot_axes:
        slots *= lax.axis_size(name)
    slot = 0
    for name in slot_axes:
        slot = slot * lax.axis_size(name) + lax.axis_index(name)
    mine = jnp.stack([local_mean, local_m2])
    table = jnp.zeros((slots,) + mine.shape, jnp.float32)
    table = lax.dynamic_update_index_in_dim(table, mine, slot, 0)
    for name in reversed(slot_axes):
        if lax.axis_size(name) == 2:
            table = table + lax.ppermute(table, name, [(0, 1), (1, 0)])
        else:
            table = lax.psum(table, name)
    means = table[:, 0]
    average = jnp.sum(means, axis=0) / slots
    spread = means - average
    m2 = jnp.sum(table[:, 1], axis=0) + count * jnp.sum(spread * spread, axis=0)
    variance = m2 / (count * slots)
    return average, variance


def group_act(values, average, variance, gain, bias):
    frames, rows, local_chan, width = values.shape
    local_groups = average.shape[-1]
    grouped = values.reshape(frames, rows, local_groups, local_chan // local_groups, width)
    centred = grouped - average.reshape(-1, 1, local_groups, 1, 1)
    scaled = (centred * lax.rsqrt(variance.reshape(-1, 1, local_groups, 1, 1) + EPSILON)).reshape(
        frames, rows, local_chan, width
    )
    return jax.nn.silu(scaled * gain[:, None] + bias[:, None]).astype(jnp.bfloat16)


def in_order(own, other, chan_index):
    size = own.shape[2]
    joined = jnp.zeros(own.shape[:2] + (2 * size,) + own.shape[3:], own.dtype)
    joined = lax.dynamic_update_slice_in_dim(joined, own, chan_index * size, axis=2)
    return lax.dynamic_update_slice_in_dim(joined, other, (1 - chan_index) * size, axis=2)


STEP = 12


def pair(ref, first):
    return jnp.concatenate([ref[0, first + k] for k in range(STEP)], axis=1)


def halo_rows(ref, edge_ref, first):
    rows = ref.shape[1]
    picked = []
    for q in range(first, first + STEP):
        if q == 0:
            picked.append(edge_ref[0, 0])
        elif q == rows + 1:
            picked.append(edge_ref[0, 1])
        else:
            picked.append(ref[0, q - 1])
    return jnp.concatenate(picked, axis=1)


def spatial_kernel(xo_ref, eo_ref, xt_ref, et_ref, wo_ref, wt_ref, res_ref, b_ref, early_ref, o_ref):
    rows, local_chan, width = o_ref.shape[1], o_ref.shape[2], o_ref.shape[3]
    lane = lax.broadcasted_iota(jnp.int32, (local_chan, width), 1)
    bias = b_ref[...]

    for i in range(rows // STEP):
        r = STEP * i
        y = jnp.dot(wo_ref[0], halo_rows(xo_ref, eo_ref, r), preferred_element_type=jnp.float32)
        y = y + jnp.dot(wt_ref[0], halo_rows(xt_ref, et_ref, r), preferred_element_type=jnp.float32)
        for tap in (1, 2):
            y = y + jnp.dot(
                wo_ref[tap], halo_rows(xo_ref, eo_ref, r + tap), preferred_element_type=jnp.float32
            )
            y = y + jnp.dot(
                wt_ref[tap], halo_rows(xt_ref, et_ref, r + tap), preferred_element_type=jnp.float32
            )
        for half in range(STEP):
            part = y[:, half * width : (half + 1) * width]
            left = pltpu.roll(part[:local_chan], 1, 1)
            left = jnp.where(lane == 0, 0.0, left)
            right = pltpu.roll(part[2 * local_chan :], width - 1, 1)
            right = jnp.where(lane == width - 1, 0.0, right)
            total = left + part[local_chan : 2 * local_chan] + right
            o_ref[0, r + half] = (res_ref[0, r + half].astype(jnp.float32) + total + bias).astype(
                o_ref.dtype
            )


def spatial_call(own, own_edges, other, other_edges, weight_own, weight_other, residual, bias, early):
    frames, rows, local_chan, width = residual.shape
    act_spec = pl.BlockSpec((1, rows, local_chan, width), lambda f: (f, 0, 0, 0))
    edge_spec = pl.BlockSpec((1, 2, local_chan, width), lambda f: (f, 0, 0, 0))
    weight_spec = pl.BlockSpec((3, 3 * local_chan, local_chan), lambda f: (0, 0, 0))
    return pl.pallas_call(
        spatial_kernel,
        out_shape=jax.ShapeDtypeStruct(residual.shape, jnp.bfloat16),
        grid=(frames,),
        in_specs=[
            act_spec,
            edge_spec,
            act_spec,
            edge_spec,
            weight_spec,
            weight_spec,
            pl.BlockSpec((1, rows, local_chan, width), lambda f: (f, 0, 0, 0)),
            pl.BlockSpec((local_chan, 1), lambda f: (0, 0)),
            pl.BlockSpec(memory_space=pl.ANY),
        ],
        out_specs=pl.BlockSpec((1, rows, local_chan, width), lambda f: (f, 0, 0, 0)),
        compiler_params=pltpu.CompilerParams(vmem_limit_bytes=48 * 1024 * 1024),
        cost_estimate=pl.CostEstimate(
            flops=2 * frames * rows * width * 18 * local_chan * local_chan,
            transcendentals=0,
            bytes_accessed=4 * own.size + 4 * weight_own.size + 4 * residual.size,
        ),
    )(own, own_edges, other, other_edges, weight_own, weight_other, residual, bias, early)


def temporal_kernel(*refs):
    own_refs, other_refs = refs[0:3], refs[3:6]
    wo_ref, wt_ref, res_ref, bias_ref, o_ref = refs[6:]
    rows, width = o_ref.shape[1], o_ref.shape[3]
    bias = bias_ref[...]

    def two_rows(i, carry):
        r = STEP * i
        y = jnp.dot(wo_ref[0], pair(own_refs[0], r), preferred_element_type=jnp.float32)
        y = y + jnp.dot(wt_ref[0], pair(other_refs[0], r), preferred_element_type=jnp.float32)
        for tap in (1, 2):
            y = y + jnp.dot(wo_ref[tap], pair(own_refs[tap], r), preferred_element_type=jnp.float32)
            y = y + jnp.dot(wt_ref[tap], pair(other_refs[tap], r), preferred_element_type=jnp.float32)
        for half in range(STEP):
            part = y[:, half * width : (half + 1) * width]
            o_ref[0, r + half] = (res_ref[0, r + half].astype(jnp.float32) + part + bias).astype(
                o_ref.dtype
            )
        return carry

    lax.fori_loop(0, rows // STEP, two_rows, 0, unroll=True)


def frame_spec(tap, rows, chans, width):
    return pl.BlockSpec((1, rows, chans, width), lambda f: (f + tap, 0, 0, 0))


def temporal_call(own, other, weight_own, weight_other, residual, bias):
    frames, rows, local_chan, width = residual.shape
    taps = [frame_spec(tap, rows, local_chan, width) for tap in range(3)]
    weight_spec = pl.BlockSpec((3, local_chan, local_chan), lambda f: (0, 0, 0))
    return pl.pallas_call(
        temporal_kernel,
        out_shape=jax.ShapeDtypeStruct(residual.shape, jnp.bfloat16),
        grid=(frames,),
        in_specs=taps
        + taps
        + [
            weight_spec,
            weight_spec,
            pl.BlockSpec((1, rows, local_chan, width), lambda f: (f, 0, 0, 0)),
            pl.BlockSpec((local_chan, 1), lambda f: (0, 0)),
        ],
        out_specs=pl.BlockSpec((1, rows, local_chan, width), lambda f: (f, 0, 0, 0)),
        compiler_params=pltpu.CompilerParams(vmem_limit_bytes=48 * 1024 * 1024),
        cost_estimate=pl.CostEstimate(
            flops=2 * frames * rows * width * 6 * local_chan * local_chan,
            transcendentals=0,
            bytes_accessed=12 * residual.size + 4 * weight_own.size + 4 * residual.size,
        ),
    )(own, own, own, other, other, other, weight_own, weight_other, residual, bias)


def spatial_taps(running, channel_slab, weight, rows, width):
    for row_tap in range(3):
        for col_tap in range(3):
            window = channel_slab[:, row_tap : row_tap + rows, :, col_tap : col_tap + width]
            running = running + jnp.einsum(
                "frcw,co->frow", window, weight[row_tap, col_tap], preferred_element_type=jnp.float32
            )
    return running


def temporal_taps(running, channel_slab, weight, frames):
    for frame_tap in range(3):
        window = channel_slab[frame_tap : frame_tap + frames]
        running = running + jnp.einsum(
            "frcw,co->frow", window, weight[frame_tap], preferred_element_type=jnp.float32
        )
    return running


def body(
    video,
    norm1_gain,
    norm1_bias,
    spatial_weight,
    spatial_bias,
    norm2_gain,
    norm2_bias,
    temporal_weight,
    temporal_bias,
):
    frames, rows, local_chan, width = video.shape
    group_size = C // GROUPS
    local_groups = local_chan // group_size
    chan_index = lax.axis_index("chan")
    tm_index = lax.axis_index("tm")
    tm_count = lax.axis_size("tm")

    spatial_full = lax.all_gather(spatial_weight, "tm", axis=2, tiled=True).reshape(9, C, local_chan)
    temporal_pieces = gather_tm(temporal_weight)
    temporal_full = jnp.moveaxis(temporal_pieces, 0, 1).reshape(3, C, local_chan)
    spatial_full = spatial_full.reshape(3, 3, C, local_chan)

    values = video.astype(jnp.float32)
    grouped = values.reshape(frames, rows, local_groups, group_size, width)
    average, variance = group_stats(grouped, (1, 3, 4), ("height",))
    act_one = group_act(values, average, variance, norm1_gain, norm1_bias)

    edges = row_halo(act_one)
    own_start = chan_index * local_chan
    other_start = (1 - chan_index) * local_chan
    spatial_rows = jnp.transpose(spatial_full, (0, 1, 3, 2)).reshape(3, 3 * local_chan, C)
    hidden = spatial_call(
        act_one,
        edges,
        swap_chan(act_one),
        swap_chan(edges),
        lax.dynamic_slice_in_dim(spatial_rows, own_start, local_chan, axis=2),
        lax.dynamic_slice_in_dim(spatial_rows, other_start, local_chan, axis=2),
        video,
        spatial_bias[:, None],
        temporal_pieces,
    )

    forward = [(i, i + 1) for i in range(tm_count - 1)]
    backward = [(target, source) for source, target in forward]
    before = lax.ppermute(hidden[-1:], "tm", forward)
    after = lax.ppermute(hidden[:1], "tm", backward)

    hidden_values = hidden.astype(jnp.float32)
    grouped_two = hidden_values.reshape(frames, rows, local_groups, group_size, width)
    average_two, variance_two = group_stats(grouped_two, (0, 1, 3, 4), ("tm", "height"))

    extended = jnp.concatenate([before, hidden, after], axis=0).astype(jnp.float32)
    act_two = group_act(extended, average_two, variance_two, norm2_gain, norm2_bias)
    frame_ids = jnp.arange(frames + 2)
    inside = (frame_ids > 0) | (tm_index > 0)
    inside = inside & ((frame_ids < frames + 1) | (tm_index < tm_count - 1))
    act_two = jnp.where(inside[:, None, None, None], act_two, jnp.zeros_like(act_two))

    temporal_rows = jnp.transpose(temporal_full, (0, 2, 1))
    return temporal_call(
        act_two,
        swap_chan(act_two),
        lax.dynamic_slice_in_dim(temporal_rows, own_start, local_chan, axis=2),
        lax.dynamic_slice_in_dim(temporal_rows, other_start, local_chan, axis=2),
        hidden,
        temporal_bias[:, None],
    )


def solution(mesh):
    return jax.shard_map(
        body,
        mesh=mesh,
        in_specs=(
            P(("groups", "tm"), "height", "chan", None),
            P("chan"),
            P("chan"),
            P(None, None, "tm", "chan"),
            P("chan"),
            P("chan"),
            P("chan"),
            P(None, "tm", "chan"),
            P("chan"),
        ),
        out_specs=P(("groups", "tm"), "height", "chan", None),
        check_vma=False,
    )
```

```python
import jax
import jax.numpy as jnp
from jax import lax
from jax.experimental import pallas as pl
from jax.experimental.pallas import tpu as pltpu
from jax.sharding import PartitionSpec as P

C = 320
GROUPS = 32


EPSILON = 1e-06


def swap_chan(block):
    return lax.ppermute(block, "chan", [(0, 1), (1, 0)])


def row_halo(block):
    count = lax.axis_size("height")
    if count == 2:
        index = lax.axis_index("height")
        edge = jnp.where(index == 0, block[:, -1:], block[:, :1])
        received = lax.ppermute(edge, "height", [(0, 1), (1, 0)])
        empty = jnp.zeros_like(received)
        low = jnp.where(index == 1, received, empty)
        high = jnp.where(index == 0, received, empty)
        return jnp.concatenate([low, high], axis=1)
    forward = [(i, i + 1) for i in range(count - 1)]
    backward = [(target, source) for source, target in forward]
    low = lax.ppermute(block[:, -1:], "height", forward)
    high = lax.ppermute(block[:, :1], "height", backward)
    return jnp.concatenate([low, high], axis=1)


def gather_tm(piece):
    count = lax.axis_size("tm")
    index = lax.axis_index("tm")
    pieces = [piece]
    for shift in range(1, count):
        pairs = [(i, (i - shift) % count) for i in range(count)]
        pieces.append(lax.ppermute(piece, "tm", pairs))
    stacked = jnp.roll(jnp.stack(pieces), index, axis=0)
    return stacked


def group_stats(grouped, axes, slot_axes):
    count = 1
    for axis in axes:
        count *= grouped.shape[axis]
    local_mean = jnp.sum(grouped, axis=axes) / count
    centred = grouped - jnp.expand_dims(local_mean, axes)
    local_m2 = jnp.sum(centred * centred, axis=axes)
    slots = 1
    for name in slot_axes:
        slots *= lax.axis_size(name)
    slot = 0
    for name in slot_axes:
        slot = slot * lax.axis_size(name) + lax.axis_index(name)
    mine = jnp.stack([local_mean, local_m2])
    table = jnp.zeros((slots,) + mine.shape, jnp.float32)
    table = lax.dynamic_update_index_in_dim(table, mine, slot, 0)
    for name in reversed(slot_axes):
        if lax.axis_size(name) == 2:
            table = table + lax.ppermute(table, name, [(0, 1), (1, 0)])
        else:
            table = lax.psum(table, name)
    means = table[:, 0]
    average = jnp.sum(means, axis=0) / slots
    spread = means - average
    m2 = jnp.sum(table[:, 1], axis=0) + count * jnp.sum(spread * spread, axis=0)
    variance = m2 / (count * slots)
    return average, variance


def group_act(values, average, variance, gain, bias):
    frames, rows, local_chan, width = values.shape
    local_groups = average.shape[-1]
    grouped = values.reshape(frames, rows, local_groups, local_chan // local_groups, width)
    centred = grouped - average.reshape(-1, 1, local_groups, 1, 1)
    scaled = (centred * lax.rsqrt(variance.reshape(-1, 1, local_groups, 1, 1) + EPSILON)).reshape(
        frames, rows, local_chan, width
    )
    return jax.nn.silu(scaled * gain[:, None] + bias[:, None]).astype(jnp.bfloat16)


def in_order(own, other, chan_index):
    size = own.shape[2]
    joined = jnp.zeros(own.shape[:2] + (2 * size,) + own.shape[3:], own.dtype)
    joined = lax.dynamic_update_slice_in_dim(joined, own, chan_index * size, axis=2)
    return lax.dynamic_update_slice_in_dim(joined, other, (1 - chan_index) * size, axis=2)


STEP = 12


def pair(ref, first):
    return jnp.concatenate([ref[0, first + k] for k in range(STEP)], axis=1)


def halo_rows(ref, edge_ref, first):
    rows = ref.shape[1]
    picked = []
    for q in range(first, first + STEP):
        if q == 0:
            picked.append(edge_ref[0, 0])
        elif q == rows + 1:
            picked.append(edge_ref[0, 1])
        else:
            picked.append(ref[0, q - 1])
    return jnp.concatenate(picked, axis=1)


def spatial_kernel(xo_ref, eo_ref, xt_ref, et_ref, wo_ref, wt_ref, res_ref, b_ref, early_ref, o_ref):
    rows, local_chan, width = o_ref.shape[1], o_ref.shape[2], o_ref.shape[3]
    lane = lax.broadcasted_iota(jnp.int32, (local_chan, width), 1)
    bias = b_ref[...]

    for i in range(rows // STEP):
        r = STEP * i
        y = jnp.dot(wo_ref[0], halo_rows(xo_ref, eo_ref, r), preferred_element_type=jnp.float32)
        y = y + jnp.dot(wt_ref[0], halo_rows(xt_ref, et_ref, r), preferred_element_type=jnp.float32)
        for tap in (1, 2):
            y = y + jnp.dot(
                wo_ref[tap], halo_rows(xo_ref, eo_ref, r + tap), preferred_element_type=jnp.float32
            )
            y = y + jnp.dot(
                wt_ref[tap], halo_rows(xt_ref, et_ref, r + tap), preferred_element_type=jnp.float32
            )
        for half in range(STEP):
            part = y[:, half * width : (half + 1) * width]
            left = pltpu.roll(part[:local_chan], 1, 1)
            left = jnp.where(lane == 0, 0.0, left)
            right = pltpu.roll(part[2 * local_chan :], width - 1, 1)
            right = jnp.where(lane == width - 1, 0.0, right)
            total = left + part[local_chan : 2 * local_chan] + right
            o_ref[0, r + half] = (res_ref[0, r + half].astype(jnp.float32) + total + bias).astype(
                o_ref.dtype
            )


def spatial_call(own, own_edges, other, other_edges, weight_own, weight_other, residual, bias, early):
    frames, rows, local_chan, width = residual.shape
    act_spec = pl.BlockSpec((1, rows, local_chan, width), lambda f: (f, 0, 0, 0))
    edge_spec = pl.BlockSpec((1, 2, local_chan, width), lambda f: (f, 0, 0, 0))
    weight_spec = pl.BlockSpec((3, 3 * local_chan, local_chan), lambda f: (0, 0, 0))
    return pl.pallas_call(
        spatial_kernel,
        out_shape=jax.ShapeDtypeStruct(residual.shape, jnp.bfloat16),
        grid=(frames,),
        in_specs=[
            act_spec,
            edge_spec,
            act_spec,
            edge_spec,
            weight_spec,
            weight_spec,
            pl.BlockSpec((1, rows, local_chan, width), lambda f: (f, 0, 0, 0)),
            pl.BlockSpec((local_chan, 1), lambda f: (0, 0)),
            pl.BlockSpec(memory_space=pl.ANY),
        ],
        out_specs=pl.BlockSpec((1, rows, local_chan, width), lambda f: (f, 0, 0, 0)),
        compiler_params=pltpu.CompilerParams(vmem_limit_bytes=48 * 1024 * 1024),
        cost_estimate=pl.CostEstimate(
            flops=2 * frames * rows * width * 18 * local_chan * local_chan,
            transcendentals=0,
            bytes_accessed=4 * own.size + 4 * weight_own.size + 4 * residual.size,
        ),
    )(own, own_edges, other, other_edges, weight_own, weight_other, residual, bias, early)


def temporal_kernel(*refs):
    own_refs, other_refs = refs[0:3], refs[3:6]
    wo_ref, wt_ref, res_ref, bias_ref, o_ref = refs[6:]
    rows, width = o_ref.shape[1], o_ref.shape[3]
    bias = bias_ref[...]

    def two_rows(i, carry):
        r = STEP * i
        y = jnp.dot(wo_ref[0], pair(own_refs[0], r), preferred_element_type=jnp.float32)
        y = y + jnp.dot(wt_ref[0], pair(other_refs[0], r), preferred_element_type=jnp.float32)
        for tap in (1, 2):
            y = y + jnp.dot(wo_ref[tap], pair(own_refs[tap], r), preferred_element_type=jnp.float32)
            y = y + jnp.dot(wt_ref[tap], pair(other_refs[tap], r), preferred_element_type=jnp.float32)
        for half in range(STEP):
            part = y[:, half * width : (half + 1) * width]
            o_ref[0, r + half] = (res_ref[0, r + half].astype(jnp.float32) + part + bias).astype(
                o_ref.dtype
            )
        return carry

    lax.fori_loop(0, rows // STEP, two_rows, 0, unroll=True)


def frame_spec(tap, rows, chans, width):
    return pl.BlockSpec((1, rows, chans, width), lambda f: (f + tap, 0, 0, 0))


def temporal_call(own, other, weight_own, weight_other, residual, bias):
    frames, rows, local_chan, width = residual.shape
    taps = [frame_spec(tap, rows, local_chan, width) for tap in range(3)]
    weight_spec = pl.BlockSpec((3, local_chan, local_chan), lambda f: (0, 0, 0))
    return pl.pallas_call(
        temporal_kernel,
        out_shape=jax.ShapeDtypeStruct(residual.shape, jnp.bfloat16),
        grid=(frames,),
        in_specs=taps
        + taps
        + [
            weight_spec,
            weight_spec,
            pl.BlockSpec((1, rows, local_chan, width), lambda f: (f, 0, 0, 0)),
            pl.BlockSpec((local_chan, 1), lambda f: (0, 0)),
        ],
        out_specs=pl.BlockSpec((1, rows, local_chan, width), lambda f: (f, 0, 0, 0)),
        compiler_params=pltpu.CompilerParams(vmem_limit_bytes=48 * 1024 * 1024),
        cost_estimate=pl.CostEstimate(
            flops=2 * frames * rows * width * 6 * local_chan * local_chan,
            transcendentals=0,
            bytes_accessed=12 * residual.size + 4 * weight_own.size + 4 * residual.size,
        ),
    )(own, own, own, other, other, other, weight_own, weight_other, residual, bias)


def spatial_taps(running, channel_slab, weight, rows, width):
    for row_tap in range(3):
        for col_tap in range(3):
            window = channel_slab[:, row_tap : row_tap + rows, :, col_tap : col_tap + width]
            running = running + jnp.einsum(
                "frcw,co->frow", window, weight[row_tap, col_tap], preferred_element_type=jnp.float32
            )
    return running


def temporal_taps(running, channel_slab, weight, frames):
    for frame_tap in range(3):
        window = channel_slab[frame_tap : frame_tap + frames]
        running = running + jnp.einsum(
            "frcw,co->frow", window, weight[frame_tap], preferred_element_type=jnp.float32
        )
    return running


def body(
    video,
    norm1_gain,
    norm1_bias,
    spatial_weight,
    spatial_bias,
    norm2_gain,
    norm2_bias,
    temporal_weight,
    temporal_bias,
):
    frames, rows, local_chan, width = video.shape
    group_size = C // GROUPS
    local_groups = local_chan // group_size
    chan_index = lax.axis_index("chan")
    tm_index = lax.axis_index("tm")
    tm_count = lax.axis_size("tm")

    temporal_pieces = gather_tm(temporal_weight)
    temporal_full = jnp.moveaxis(temporal_pieces, 0, 1).reshape(3, C, local_chan)

    values = video.astype(jnp.float32)
    grouped = values.reshape(frames, rows, local_groups, group_size, width)
    average, variance = group_stats(grouped, (1, 3, 4), ("height",))
    act_one = group_act(values, average, variance, norm1_gain, norm1_bias)
    act_one, spatial_weight = lax.optimization_barrier((act_one, spatial_weight))
    spatial_full = lax.all_gather(spatial_weight, "tm", axis=2, tiled=True)

    edges = row_halo(act_one)
    own_start = chan_index * local_chan
    other_start = (1 - chan_index) * local_chan
    spatial_rows = jnp.transpose(spatial_full, (0, 1, 3, 2)).reshape(3, 3 * local_chan, C)
    hidden = spatial_call(
        act_one,
        edges,
        swap_chan(act_one),
        swap_chan(edges),
        lax.dynamic_slice_in_dim(spatial_rows, own_start, local_chan, axis=2),
        lax.dynamic_slice_in_dim(spatial_rows, other_start, local_chan, axis=2),
        video,
        spatial_bias[:, None],
        temporal_pieces,
    )

    forward = [(i, i + 1) for i in range(tm_count - 1)]
    backward = [(target, source) for source, target in forward]
    before = lax.ppermute(hidden[-1:], "tm", forward)
    after = lax.ppermute(hidden[:1], "tm", backward)

    hidden_values = hidden.astype(jnp.float32)
    grouped_two = hidden_values.reshape(frames, rows, local_groups, group_size, width)
    average_two, variance_two = group_stats(grouped_two, (0, 1, 3, 4), ("tm", "height"))

    extended = jnp.concatenate([before, hidden, after], axis=0).astype(jnp.float32)
    act_two = group_act(extended, average_two, variance_two, norm2_gain, norm2_bias)
    frame_ids = jnp.arange(frames + 2)
    inside = (frame_ids > 0) | (tm_index > 0)
    inside = inside & ((frame_ids < frames + 1) | (tm_index < tm_count - 1))
    act_two = jnp.where(inside[:, None, None, None], act_two, jnp.zeros_like(act_two))

    temporal_rows = jnp.transpose(temporal_full, (0, 2, 1))
    return temporal_call(
        act_two,
        swap_chan(act_two),
        lax.dynamic_slice_in_dim(temporal_rows, own_start, local_chan, axis=2),
        lax.dynamic_slice_in_dim(temporal_rows, other_start, local_chan, axis=2),
        hidden,
        temporal_bias[:, None],
    )


def solution(mesh):
    return jax.shard_map(
        body,
        mesh=mesh,
        in_specs=(
            P(("groups", "tm"), "height", "chan", None),
            P("chan"),
            P("chan"),
            P(None, None, "tm", "chan"),
            P("chan"),
            P("chan"),
            P("chan"),
            P(None, "tm", "chan"),
            P("chan"),
        ),
        out_specs=P(("groups", "tm"), "height", "chan", None),
        check_vma=False,
    )
```

```python
import jax
import jax.numpy as jnp
from jax import lax
from jax.experimental import pallas as pl
from jax.experimental.pallas import tpu as pltpu
from jax.sharding import PartitionSpec as P

C = 320
GROUPS = 32


EPSILON = 1e-06


def swap_chan(block):
    return lax.ppermute(block, "chan", [(0, 1), (1, 0)])


def row_halo(block):
    count = lax.axis_size("height")
    if count == 2:
        index = lax.axis_index("height")
        edge = jnp.where(index == 0, block[:, -1:], block[:, :1])
        received = lax.ppermute(edge, "height", [(0, 1), (1, 0)])
        empty = jnp.zeros_like(received)
        low = jnp.where(index == 1, received, empty)
        high = jnp.where(index == 0, received, empty)
        return jnp.concatenate([low, high], axis=1)
    forward = [(i, i + 1) for i in range(count - 1)]
    backward = [(target, source) for source, target in forward]
    low = lax.ppermute(block[:, -1:], "height", forward)
    high = lax.ppermute(block[:, :1], "height", backward)
    return jnp.concatenate([low, high], axis=1)


def gather_tm(piece):
    count = lax.axis_size("tm")
    index = lax.axis_index("tm")
    pieces = [piece]
    for shift in range(1, count):
        pairs = [(i, (i - shift) % count) for i in range(count)]
        pieces.append(lax.ppermute(piece, "tm", pairs))
    stacked = jnp.roll(jnp.stack(pieces), index, axis=0)
    return stacked


def group_stats(grouped, axes, slot_axes):
    count = 1
    for axis in axes:
        count *= grouped.shape[axis]
    local_mean = jnp.sum(grouped, axis=axes) / count
    centred = grouped - jnp.expand_dims(local_mean, axes)
    local_m2 = jnp.sum(centred * centred, axis=axes)
    slots = 1
    for name in slot_axes:
        slots *= lax.axis_size(name)
    slot = 0
    for name in slot_axes:
        slot = slot * lax.axis_size(name) + lax.axis_index(name)
    mine = jnp.stack([local_mean, local_m2])
    table = jnp.zeros((slots,) + mine.shape, jnp.float32)
    table = lax.dynamic_update_index_in_dim(table, mine, slot, 0)
    for name in reversed(slot_axes):
        if lax.axis_size(name) == 2:
            table = table + lax.ppermute(table, name, [(0, 1), (1, 0)])
        else:
            table = lax.psum(table, name)
    means = table[:, 0]
    average = jnp.sum(means, axis=0) / slots
    spread = means - average
    m2 = jnp.sum(table[:, 1], axis=0) + count * jnp.sum(spread * spread, axis=0)
    variance = m2 / (count * slots)
    return average, variance


def group_act(values, average, variance, gain, bias):
    frames, rows, local_chan, width = values.shape
    local_groups = average.shape[-1]
    grouped = values.reshape(frames, rows, local_groups, local_chan // local_groups, width)
    centred = grouped - average.reshape(-1, 1, local_groups, 1, 1)
    scaled = (centred * lax.rsqrt(variance.reshape(-1, 1, local_groups, 1, 1) + EPSILON)).reshape(
        frames, rows, local_chan, width
    )
    return jax.nn.silu(scaled * gain[:, None] + bias[:, None]).astype(jnp.bfloat16)


def in_order(own, other, chan_index):
    size = own.shape[2]
    joined = jnp.zeros(own.shape[:2] + (2 * size,) + own.shape[3:], own.dtype)
    joined = lax.dynamic_update_slice_in_dim(joined, own, chan_index * size, axis=2)
    return lax.dynamic_update_slice_in_dim(joined, other, (1 - chan_index) * size, axis=2)


STEP = 12


def pair(ref, first):
    return jnp.concatenate([ref[0, first + k] for k in range(STEP)], axis=1)


def halo_rows(ref, edge_ref, first):
    rows = ref.shape[1]
    picked = []
    for q in range(first, first + STEP):
        if q == 0:
            picked.append(edge_ref[0, 0])
        elif q == rows + 1:
            picked.append(edge_ref[0, 1])
        else:
            picked.append(ref[0, q - 1])
    return jnp.concatenate(picked, axis=1)


def spatial_kernel(xo_ref, eo_ref, xt_ref, et_ref, wo_ref, wt_ref, res_ref, b_ref, early_ref, o_ref):
    rows, local_chan, width = o_ref.shape[1], o_ref.shape[2], o_ref.shape[3]
    lane = lax.broadcasted_iota(jnp.int32, (local_chan, width), 1)
    bias = b_ref[...]

    for i in range(rows // STEP):
        r = STEP * i
        y = jnp.dot(wo_ref[0], halo_rows(xo_ref, eo_ref, r), preferred_element_type=jnp.float32)
        y = y + jnp.dot(wt_ref[0], halo_rows(xt_ref, et_ref, r), preferred_element_type=jnp.float32)
        for tap in (1, 2):
            y = y + jnp.dot(
                wo_ref[tap], halo_rows(xo_ref, eo_ref, r + tap), preferred_element_type=jnp.float32
            )
            y = y + jnp.dot(
                wt_ref[tap], halo_rows(xt_ref, et_ref, r + tap), preferred_element_type=jnp.float32
            )
        for half in range(STEP):
            part = y[:, half * width : (half + 1) * width]
            left = pltpu.roll(part[:local_chan], 1, 1)
            left = jnp.where(lane == 0, 0.0, left)
            right = pltpu.roll(part[2 * local_chan :], width - 1, 1)
            right = jnp.where(lane == width - 1, 0.0, right)
            total = left + part[local_chan : 2 * local_chan] + right
            o_ref[0, r + half] = (res_ref[0, r + half].astype(jnp.float32) + total + bias).astype(
                o_ref.dtype
            )


def spatial_call(own, own_edges, other, other_edges, weight_own, weight_other, residual, bias, early):
    frames, rows, local_chan, width = residual.shape
    act_spec = pl.BlockSpec((1, rows, local_chan, width), lambda f: (f, 0, 0, 0))
    edge_spec = pl.BlockSpec((1, 2, local_chan, width), lambda f: (f, 0, 0, 0))
    weight_spec = pl.BlockSpec((3, 3 * local_chan, local_chan), lambda f: (0, 0, 0))
    return pl.pallas_call(
        spatial_kernel,
        out_shape=jax.ShapeDtypeStruct(residual.shape, jnp.bfloat16),
        grid=(frames,),
        in_specs=[
            act_spec,
            edge_spec,
            act_spec,
            edge_spec,
            weight_spec,
            weight_spec,
            pl.BlockSpec((1, rows, local_chan, width), lambda f: (f, 0, 0, 0)),
            pl.BlockSpec((local_chan, 1), lambda f: (0, 0)),
            pl.BlockSpec(memory_space=pl.ANY),
        ],
        out_specs=pl.BlockSpec((1, rows, local_chan, width), lambda f: (f, 0, 0, 0)),
        compiler_params=pltpu.CompilerParams(vmem_limit_bytes=48 * 1024 * 1024),
        cost_estimate=pl.CostEstimate(
            flops=2 * frames * rows * width * 18 * local_chan * local_chan,
            transcendentals=0,
            bytes_accessed=4 * own.size + 4 * weight_own.size + 4 * residual.size,
        ),
    )(own, own_edges, other, other_edges, weight_own, weight_other, residual, bias, early)


def temporal_kernel(*refs):
    own_refs, other_refs = refs[0:3], refs[3:6]
    wo_ref, wt_ref, res_ref, bias_ref, o_ref = refs[6:]
    rows, width = o_ref.shape[1], o_ref.shape[3]
    bias = bias_ref[...]

    def two_rows(i, carry):
        r = STEP * i
        y = jnp.dot(wo_ref[0], pair(own_refs[0], r), preferred_element_type=jnp.float32)
        y = y + jnp.dot(wt_ref[0], pair(other_refs[0], r), preferred_element_type=jnp.float32)
        for tap in (1, 2):
            y = y + jnp.dot(wo_ref[tap], pair(own_refs[tap], r), preferred_element_type=jnp.float32)
            y = y + jnp.dot(wt_ref[tap], pair(other_refs[tap], r), preferred_element_type=jnp.float32)
        for half in range(STEP):
            part = y[:, half * width : (half + 1) * width]
            o_ref[0, r + half] = (res_ref[0, r + half].astype(jnp.float32) + part + bias).astype(
                o_ref.dtype
            )
        return carry

    lax.fori_loop(0, rows // STEP, two_rows, 0, unroll=True)


def frame_spec(tap, rows, chans, width):
    return pl.BlockSpec((1, rows, chans, width), lambda f, j: (f + tap, j, 0, 0))


def temporal_call(own, other, weight_own, weight_other, residual, bias):
    frames, rows, local_chan, width = residual.shape
    taps = [frame_spec(tap, STEP, local_chan, width) for tap in range(3)]
    weight_spec = pl.BlockSpec((3, local_chan, local_chan), lambda f, j: (0, 0, 0))
    row_spec = pl.BlockSpec((1, STEP, local_chan, width), lambda f, j: (f, j, 0, 0))
    return pl.pallas_call(
        temporal_kernel,
        out_shape=jax.ShapeDtypeStruct(residual.shape, jnp.bfloat16),
        grid=(frames, rows // STEP),
        in_specs=taps
        + taps
        + [
            weight_spec,
            weight_spec,
            row_spec,
            pl.BlockSpec((local_chan, 1), lambda f, j: (0, 0)),
        ],
        out_specs=row_spec,
        compiler_params=pltpu.CompilerParams(vmem_limit_bytes=48 * 1024 * 1024),
        cost_estimate=pl.CostEstimate(
            flops=2 * frames * rows * width * 6 * local_chan * local_chan,
            transcendentals=0,
            bytes_accessed=12 * residual.size + 4 * weight_own.size + 4 * residual.size,
        ),
    )(own, own, own, other, other, other, weight_own, weight_other, residual, bias)


def spatial_taps(running, channel_slab, weight, rows, width):
    for row_tap in range(3):
        for col_tap in range(3):
            window = channel_slab[:, row_tap : row_tap + rows, :, col_tap : col_tap + width]
            running = running + jnp.einsum(
                "frcw,co->frow", window, weight[row_tap, col_tap], preferred_element_type=jnp.float32
            )
    return running


def temporal_taps(running, channel_slab, weight, frames):
    for frame_tap in range(3):
        window = channel_slab[frame_tap : frame_tap + frames]
        running = running + jnp.einsum(
            "frcw,co->frow", window, weight[frame_tap], preferred_element_type=jnp.float32
        )
    return running


def body(
    video,
    norm1_gain,
    norm1_bias,
    spatial_weight,
    spatial_bias,
    norm2_gain,
    norm2_bias,
    temporal_weight,
    temporal_bias,
):
    frames, rows, local_chan, width = video.shape
    group_size = C // GROUPS
    local_groups = local_chan // group_size
    chan_index = lax.axis_index("chan")
    tm_index = lax.axis_index("tm")
    tm_count = lax.axis_size("tm")

    spatial_full = lax.all_gather(spatial_weight, "tm", axis=2, tiled=True).reshape(9, C, local_chan)
    temporal_pieces = gather_tm(temporal_weight)
    temporal_full = jnp.moveaxis(temporal_pieces, 0, 1).reshape(3, C, local_chan)
    spatial_full = spatial_full.reshape(3, 3, C, local_chan)

    values = video.astype(jnp.float32)
    grouped = values.reshape(frames, rows, local_groups, group_size, width)
    average, variance = group_stats(grouped, (1, 3, 4), ("height",))
    act_one = group_act(values, average, variance, norm1_gain, norm1_bias)

    edges = row_halo(act_one)
    own_start = chan_index * local_chan
    other_start = (1 - chan_index) * local_chan
    spatial_rows = jnp.transpose(spatial_full, (0, 1, 3, 2)).reshape(3, 3 * local_chan, C)
    hidden = spatial_call(
        act_one,
        edges,
        swap_chan(act_one),
        swap_chan(edges),
        lax.dynamic_slice_in_dim(spatial_rows, own_start, local_chan, axis=2),
        lax.dynamic_slice_in_dim(spatial_rows, other_start, local_chan, axis=2),
        video,
        spatial_bias[:, None],
        temporal_pieces,
    )

    forward = [(i, i + 1) for i in range(tm_count - 1)]
    backward = [(target, source) for source, target in forward]
    before = lax.ppermute(hidden[-1:], "tm", forward)
    after = lax.ppermute(hidden[:1], "tm", backward)

    hidden_values = hidden.astype(jnp.float32)
    grouped_two = hidden_values.reshape(frames, rows, local_groups, group_size, width)
    average_two, variance_two = group_stats(grouped_two, (0, 1, 3, 4), ("tm", "height"))

    extended = jnp.concatenate([before, hidden, after], axis=0).astype(jnp.float32)
    act_two = group_act(extended, average_two, variance_two, norm2_gain, norm2_bias)
    frame_ids = jnp.arange(frames + 2)
    inside = (frame_ids > 0) | (tm_index > 0)
    inside = inside & ((frame_ids < frames + 1) | (tm_index < tm_count - 1))
    act_two = jnp.where(inside[:, None, None, None], act_two, jnp.zeros_like(act_two))

    temporal_rows = jnp.transpose(temporal_full, (0, 2, 1))
    return temporal_call(
        act_two,
        swap_chan(act_two),
        lax.dynamic_slice_in_dim(temporal_rows, own_start, local_chan, axis=2),
        lax.dynamic_slice_in_dim(temporal_rows, other_start, local_chan, axis=2),
        hidden,
        temporal_bias[:, None],
    )


def solution(mesh):
    return jax.shard_map(
        body,
        mesh=mesh,
        in_specs=(
            P(("groups", "tm"), "height", "chan", None),
            P("chan"),
            P("chan"),
            P(None, None, "tm", "chan"),
            P("chan"),
            P("chan"),
            P("chan"),
            P(None, "tm", "chan"),
            P("chan"),
        ),
        out_specs=P(("groups", "tm"), "height", "chan", None),
        check_vma=False,
    )
```

```python
import jax
import jax.numpy as jnp
from jax import lax
from jax.experimental import pallas as pl
from jax.experimental.pallas import tpu as pltpu
from jax.sharding import PartitionSpec as P

C = 320
GROUPS = 32


EPSILON = 1e-06


def swap_chan(block):
    return lax.ppermute(block, "chan", [(0, 1), (1, 0)])


def row_halo(block):
    count = lax.axis_size("height")
    if count == 2:
        index = lax.axis_index("height")
        edge = jnp.where(index == 0, block[:, -1:], block[:, :1])
        received = lax.ppermute(edge, "height", [(0, 1), (1, 0)])
        empty = jnp.zeros_like(received)
        low = jnp.where(index == 1, received, empty)
        high = jnp.where(index == 0, received, empty)
        return jnp.concatenate([low, high], axis=1)
    forward = [(i, i + 1) for i in range(count - 1)]
    backward = [(target, source) for source, target in forward]
    low = lax.ppermute(block[:, -1:], "height", forward)
    high = lax.ppermute(block[:, :1], "height", backward)
    return jnp.concatenate([low, high], axis=1)


def gather_tm(piece):
    count = lax.axis_size("tm")
    index = lax.axis_index("tm")
    pieces = [piece]
    for shift in range(1, count):
        pairs = [(i, (i - shift) % count) for i in range(count)]
        pieces.append(lax.ppermute(piece, "tm", pairs))
    stacked = jnp.roll(jnp.stack(pieces), index, axis=0)
    return stacked


def group_stats(grouped, axes, slot_axes):
    count = 1
    for axis in axes:
        count *= grouped.shape[axis]
    local_mean = jnp.sum(grouped, axis=axes) / count
    centred = grouped - jnp.expand_dims(local_mean, axes)
    local_m2 = jnp.sum(centred * centred, axis=axes)
    slots = 1
    for name in slot_axes:
        slots *= lax.axis_size(name)
    slot = 0
    for name in slot_axes:
        slot = slot * lax.axis_size(name) + lax.axis_index(name)
    mine = jnp.stack([local_mean, local_m2])
    table = jnp.zeros((slots,) + mine.shape, jnp.float32)
    table = lax.dynamic_update_index_in_dim(table, mine, slot, 0)
    for name in reversed(slot_axes):
        if lax.axis_size(name) == 2:
            table = table + lax.ppermute(table, name, [(0, 1), (1, 0)])
        else:
            table = lax.psum(table, name)
    means = table[:, 0]
    average = jnp.sum(means, axis=0) / slots
    spread = means - average
    m2 = jnp.sum(table[:, 1], axis=0) + count * jnp.sum(spread * spread, axis=0)
    variance = m2 / (count * slots)
    return average, variance


def group_act(values, average, variance, gain, bias):
    frames, rows, local_chan, width = values.shape
    local_groups = average.shape[-1]
    grouped = values.reshape(frames, rows, local_groups, local_chan // local_groups, width)
    centred = grouped - average.reshape(-1, 1, local_groups, 1, 1)
    scaled = (centred * lax.rsqrt(variance.reshape(-1, 1, local_groups, 1, 1) + EPSILON)).reshape(
        frames, rows, local_chan, width
    )
    return jax.nn.silu(scaled * gain[:, None] + bias[:, None]).astype(jnp.bfloat16)


def in_order(own, other, chan_index):
    size = own.shape[2]
    joined = jnp.zeros(own.shape[:2] + (2 * size,) + own.shape[3:], own.dtype)
    joined = lax.dynamic_update_slice_in_dim(joined, own, chan_index * size, axis=2)
    return lax.dynamic_update_slice_in_dim(joined, other, (1 - chan_index) * size, axis=2)


STEP = 18


def pair(ref, first):
    return jnp.concatenate([ref[0, first + k] for k in range(STEP)], axis=1)


def halo_rows(ref, edge_ref, first):
    rows = ref.shape[1]
    picked = []
    for q in range(first, first + STEP):
        if q == 0:
            picked.append(edge_ref[0, 0])
        elif q == rows + 1:
            picked.append(edge_ref[0, 1])
        else:
            picked.append(ref[0, q - 1])
    return jnp.concatenate(picked, axis=1)


def spatial_kernel(xo_ref, eo_ref, xt_ref, et_ref, wo_ref, wt_ref, res_ref, b_ref, early_ref, o_ref):
    rows, local_chan, width = o_ref.shape[1], o_ref.shape[2], o_ref.shape[3]
    lane = lax.broadcasted_iota(jnp.int32, (local_chan, width), 1)
    bias = b_ref[...]

    for i in range(rows // STEP):
        r = STEP * i
        y = jnp.dot(wo_ref[0], halo_rows(xo_ref, eo_ref, r), preferred_element_type=jnp.float32)
        y = y + jnp.dot(wt_ref[0], halo_rows(xt_ref, et_ref, r), preferred_element_type=jnp.float32)
        for tap in (1, 2):
            y = y + jnp.dot(
                wo_ref[tap], halo_rows(xo_ref, eo_ref, r + tap), preferred_element_type=jnp.float32
            )
            y = y + jnp.dot(
                wt_ref[tap], halo_rows(xt_ref, et_ref, r + tap), preferred_element_type=jnp.float32
            )
        for half in range(STEP):
            part = y[:, half * width : (half + 1) * width]
            left = pltpu.roll(part[:local_chan], 1, 1)
            left = jnp.where(lane == 0, 0.0, left)
            right = pltpu.roll(part[2 * local_chan :], width - 1, 1)
            right = jnp.where(lane == width - 1, 0.0, right)
            total = left + part[local_chan : 2 * local_chan] + right
            o_ref[0, r + half] = (res_ref[0, r + half].astype(jnp.float32) + total + bias).astype(
                o_ref.dtype
            )


def spatial_call(own, own_edges, other, other_edges, weight_own, weight_other, residual, bias, early):
    frames, rows, local_chan, width = residual.shape
    act_spec = pl.BlockSpec((1, rows, local_chan, width), lambda f: (f, 0, 0, 0))
    edge_spec = pl.BlockSpec((1, 2, local_chan, width), lambda f: (f, 0, 0, 0))
    weight_spec = pl.BlockSpec((3, 3 * local_chan, local_chan), lambda f: (0, 0, 0))
    return pl.pallas_call(
        spatial_kernel,
        out_shape=jax.ShapeDtypeStruct(residual.shape, jnp.bfloat16),
        grid=(frames,),
        in_specs=[
            act_spec,
            edge_spec,
            act_spec,
            edge_spec,
            weight_spec,
            weight_spec,
            pl.BlockSpec((1, rows, local_chan, width), lambda f: (f, 0, 0, 0)),
            pl.BlockSpec((local_chan, 1), lambda f: (0, 0)),
            pl.BlockSpec(memory_space=pl.ANY),
        ],
        out_specs=pl.BlockSpec((1, rows, local_chan, width), lambda f: (f, 0, 0, 0)),
        compiler_params=pltpu.CompilerParams(vmem_limit_bytes=48 * 1024 * 1024),
        cost_estimate=pl.CostEstimate(
            flops=2 * frames * rows * width * 18 * local_chan * local_chan,
            transcendentals=0,
            bytes_accessed=4 * own.size + 4 * weight_own.size + 4 * residual.size,
        ),
    )(own, own_edges, other, other_edges, weight_own, weight_other, residual, bias, early)


def temporal_kernel(*refs):
    own_refs, other_refs = refs[0:3], refs[3:6]
    wo_ref, wt_ref, res_ref, bias_ref, o_ref = refs[6:]
    rows, width = o_ref.shape[1], o_ref.shape[3]
    bias = bias_ref[...]

    def two_rows(i, carry):
        r = STEP * i
        y = jnp.dot(wo_ref[0], pair(own_refs[0], r), preferred_element_type=jnp.float32)
        y = y + jnp.dot(wt_ref[0], pair(other_refs[0], r), preferred_element_type=jnp.float32)
        for tap in (1, 2):
            y = y + jnp.dot(wo_ref[tap], pair(own_refs[tap], r), preferred_element_type=jnp.float32)
            y = y + jnp.dot(wt_ref[tap], pair(other_refs[tap], r), preferred_element_type=jnp.float32)
        for half in range(STEP):
            part = y[:, half * width : (half + 1) * width]
            o_ref[0, r + half] = (res_ref[0, r + half].astype(jnp.float32) + part + bias).astype(
                o_ref.dtype
            )
        return carry

    lax.fori_loop(0, rows // STEP, two_rows, 0, unroll=True)


def frame_spec(tap, rows, chans, width):
    return pl.BlockSpec((1, rows, chans, width), lambda f: (f + tap, 0, 0, 0))


def temporal_call(own, other, weight_own, weight_other, residual, bias):
    frames, rows, local_chan, width = residual.shape
    taps = [frame_spec(tap, rows, local_chan, width) for tap in range(3)]
    weight_spec = pl.BlockSpec((3, local_chan, local_chan), lambda f: (0, 0, 0))
    return pl.pallas_call(
        temporal_kernel,
        out_shape=jax.ShapeDtypeStruct(residual.shape, jnp.bfloat16),
        grid=(frames,),
        in_specs=taps
        + taps
        + [
            weight_spec,
            weight_spec,
            pl.BlockSpec((1, rows, local_chan, width), lambda f: (f, 0, 0, 0)),
            pl.BlockSpec((local_chan, 1), lambda f: (0, 0)),
        ],
        out_specs=pl.BlockSpec((1, rows, local_chan, width), lambda f: (f, 0, 0, 0)),
        compiler_params=pltpu.CompilerParams(vmem_limit_bytes=48 * 1024 * 1024),
        cost_estimate=pl.CostEstimate(
            flops=2 * frames * rows * width * 6 * local_chan * local_chan,
            transcendentals=0,
            bytes_accessed=12 * residual.size + 4 * weight_own.size + 4 * residual.size,
        ),
    )(own, own, own, other, other, other, weight_own, weight_other, residual, bias)


def spatial_taps(running, channel_slab, weight, rows, width):
    for row_tap in range(3):
        for col_tap in range(3):
            window = channel_slab[:, row_tap : row_tap + rows, :, col_tap : col_tap + width]
            running = running + jnp.einsum(
                "frcw,co->frow", window, weight[row_tap, col_tap], preferred_element_type=jnp.float32
            )
    return running


def temporal_taps(running, channel_slab, weight, frames):
    for frame_tap in range(3):
        window = channel_slab[frame_tap : frame_tap + frames]
        running = running + jnp.einsum(
            "frcw,co->frow", window, weight[frame_tap], preferred_element_type=jnp.float32
        )
    return running


def body(
    video,
    norm1_gain,
    norm1_bias,
    spatial_weight,
    spatial_bias,
    norm2_gain,
    norm2_bias,
    temporal_weight,
    temporal_bias,
):
    frames, rows, local_chan, width = video.shape
    group_size = C // GROUPS
    local_groups = local_chan // group_size
    chan_index = lax.axis_index("chan")
    tm_index = lax.axis_index("tm")
    tm_count = lax.axis_size("tm")

    spatial_full = lax.all_gather(spatial_weight, "tm", axis=2, tiled=True).reshape(9, C, local_chan)
    temporal_pieces = gather_tm(temporal_weight)
    temporal_full = jnp.moveaxis(temporal_pieces, 0, 1).reshape(3, C, local_chan)
    spatial_full = spatial_full.reshape(3, 3, C, local_chan)

    values = video.astype(jnp.float32)
    grouped = values.reshape(frames, rows, local_groups, group_size, width)
    average, variance = group_stats(grouped, (1, 3, 4), ("height",))
    act_one = group_act(values, average, variance, norm1_gain, norm1_bias)

    edges = row_halo(act_one)
    own_start = chan_index * local_chan
    other_start = (1 - chan_index) * local_chan
    spatial_rows = jnp.transpose(spatial_full, (0, 1, 3, 2)).reshape(3, 3 * local_chan, C)
    hidden = spatial_call(
        act_one,
        edges,
        swap_chan(act_one),
        swap_chan(edges),
        lax.dynamic_slice_in_dim(spatial_rows, own_start, local_chan, axis=2),
        lax.dynamic_slice_in_dim(spatial_rows, other_start, local_chan, axis=2),
        video,
        spatial_bias[:, None],
        temporal_pieces,
    )

    forward = [(i, i + 1) for i in range(tm_count - 1)]
    backward = [(target, source) for source, target in forward]
    before = lax.ppermute(hidden[-1:], "tm", forward)
    after = lax.ppermute(hidden[:1], "tm", backward)

    hidden_values = hidden.astype(jnp.float32)
    grouped_two = hidden_values.reshape(frames, rows, local_groups, group_size, width)
    average_two, variance_two = group_stats(grouped_two, (0, 1, 3, 4), ("tm", "height"))

    extended = jnp.concatenate([before, hidden, after], axis=0).astype(jnp.float32)
    act_two = group_act(extended, average_two, variance_two, norm2_gain, norm2_bias)
    frame_ids = jnp.arange(frames + 2)
    inside = (frame_ids > 0) | (tm_index > 0)
    inside = inside & ((frame_ids < frames + 1) | (tm_index < tm_count - 1))
    act_two = jnp.where(inside[:, None, None, None], act_two, jnp.zeros_like(act_two))

    temporal_rows = jnp.transpose(temporal_full, (0, 2, 1))
    return temporal_call(
        act_two,
        swap_chan(act_two),
        lax.dynamic_slice_in_dim(temporal_rows, own_start, local_chan, axis=2),
        lax.dynamic_slice_in_dim(temporal_rows, other_start, local_chan, axis=2),
        hidden,
        temporal_bias[:, None],
    )


def solution(mesh):
    return jax.shard_map(
        body,
        mesh=mesh,
        in_specs=(
            P(("groups", "tm"), "height", "chan", None),
            P("chan"),
            P("chan"),
            P(None, None, "tm", "chan"),
            P("chan"),
            P("chan"),
            P("chan"),
            P(None, "tm", "chan"),
            P("chan"),
        ),
        out_specs=P(("groups", "tm"), "height", "chan", None),
        check_vma=False,
    )
```
